32 devices in a mesh: req: 8 (over z, y), tp: 4 (over x, core).
Axes of the slice: x: 2, y: 2, z: 4, core: 2. Of those that a mesh axis runs over, the one named last changes fastest.
Arguments:
- tokens_in: bfloat16 [24, 4, 2048], P('req'), may hold values from -6 to 6
- attn_norm: bfloat16 [2048], replicated, may hold values from 0.099609375 to 1.8984375
- qkv_weight: bfloat16 [2048, 3, 2048], P(None, None, 'tp'), may hold values from -0.125 to 0.125
- qkv_bias: bfloat16 [3, 2048], P(None, 'tp'), may hold values from -12 to 12
- out_weight: bfloat16 [2048, 2048], P('tp'), may hold values from -0.125 to 0.125
- cache_keys: bfloat16 [320, 128, 2048], P('req', None, 'tp'), may hold values from -12 to 12
- cache_values: bfloat16 [320, 128, 2048], P('req', None, 'tp'), may hold values from -6 to 6
- page_table: int32 [24, 37], replicated, may hold values from -1 to 319, as said below
- cache_lengths: int32 [24], replicated, may hold values from 1 to 4736, as said below
- mlp_norm: bfloat16 [2048], replicated, may hold values from 0.099609375 to 1.8984375
- routes: int32 [24, 4, 4], P('req'), may hold values from 0 to 7, all different within a row; in each aligned block of 12 rows (0 to 11, 12 to 23, ..., all dimensions but the last counted through in order) at most 6 rows name the same one
- route_gates: float32 [24, 4, 4], P('req'), may hold values from 0.05 to 0.5
- expert_w_gate: bfloat16 [8, 2048, 1408], P('req', None, 'tp'), may hold values from -0.125 to 0.125
- expert_w_up: bfloat16 [8, 2048, 1408], P('req', None, 'tp'), may hold values from -0.125 to 0.125
- expert_w_down: bfloat16 [8, 1408, 2048], P('req', 'tp'), may hold values from -0.15625 to 0.15625
- shared_w_gate: bfloat16 [2048, 5632], P('tp', 'req'), may hold values from -0.125 to 0.125
- shared_w_up: bfloat16 [2048, 5632], P('tp', 'req'), may hold values from -0.125 to 0.125
- shared_w_down: bfloat16 [5632, 2048], P('req', 'tp'), may hold values from -0.078125 to 0.078125
- shared_switch: bfloat16 [2048], replicated, may hold values from -0.125 to 0.125
Outputs:
- layer_out: bfloat16 [24, 4, 2048], P('req', None, 'tp')
The draws below stay inside these ranges and needn't reach their ends.
Inputs may be any that keep to these rules, and one draw needn't show every extreme that they name: `page_table`: entry [r, j] is the pool page holding positions j*128 to (j+1)*128 - 1 of request r's cache, or -1. No pool page is named twice. 6 requests, drawn from the seed, have all 37 entries set, all outside the first 12 pages of every block of 40 pool pages; every other request r has exactly its first 4 entries set, all among pool pages (r // 3)*40 to (r // 3)*40 + 3*4 - 1. `cache_lengths`: A long request has 2368 to 4736 cached tokens, any other 1 to 512; both largest values occur in every draw. `routes`: the 4 experts of a token differ. Among the 12 tokens of each aligned block of rows (those of one index of req) no expert is named more than 6 times, and in some of those blocks one expert is named exactly 6 times.
All inputs are finite; a program needn't handle non-finite values.
Results may differ from the reference program's by a relative error of at most 0.006.
Values may be sent and summed in bfloat16 or wider, within the bound.
No kernel may reach another device: no remote copies, remote signals or barrier semaphores. Data moves between devices by JAX's collectives and lax.ppermute only.
A program may use at most 128 MiB of HBM per device.

```python
import math
from functools import partial
import jax
import jax.numpy as jnp
import numpy as np
from jax import lax

D = 2048
HEADS = 16
HD = 128
FE = 1408
FS = 5632
TOPK = 4
STEPS = 4
PAGE = 128
SHORT_PAGES = 4
LONG = 6
PAGES_DEV = 40
R_DEV = 3
REQS = 24
EXPERTS = 8
CAP = 6
POOL = 320
LONG_PAGES = 37


def draw_qkv_bias(key, part):
    bias_rows = jnp.clip(jax.random.normal(jax.random.fold_in(key, 9), (3, HEADS * HD), jnp.float32), -6.0, 6.0)
    return bias_rows.astype(jnp.bfloat16)


def draw_cache_keys(key, part):
    key_shape = (POOL, PAGE, HEADS, HD)
    entries = jnp.clip(jax.random.normal(jax.random.fold_in(key, 5), key_shape, jnp.float32) * 2.0, -12.0, 12.0)
    return entries.reshape(POOL, PAGE, HEADS * HD).astype(jnp.bfloat16)


def page_layout(key):
    base_key = jax.random.fold_in(key, 17)
    long_pick = jax.random.permutation(jax.random.fold_in(base_key, 1), REQS)[:LONG]
    is_long = jnp.zeros((REQS,), jnp.int32).at[long_pick].set(1)
    request_ids = jnp.arange(REQS, dtype=jnp.int32)
    home_device = request_ids // R_DEV
    within = request_ids % R_DEV
    reserved = R_DEV * SHORT_PAGES
    devices = POOL // PAGES_DEV
    draw_scores = jax.random.randint(jax.random.fold_in(base_key, 2), (devices, reserved), 0, 1 << 20) * reserved + jnp.arange(reserved, dtype=jnp.int32)[None, :]
    local_order = jnp.argsort(draw_scores, axis=1).astype(jnp.int32)
    page_ids = jnp.arange(LONG_PAGES, dtype=jnp.int32)
    column = jnp.minimum(within[:, None] * SHORT_PAGES + page_ids[None, :], reserved - 1)
    short_table = home_device[:, None] * PAGES_DEV + jnp.take_along_axis(local_order[home_device], column, axis=1)
    short_table = jnp.where(page_ids[None, :] < SHORT_PAGES, short_table, -1)
    spare_count = PAGES_DEV - reserved
    spare_ids = jnp.arange(devices * spare_count, dtype=jnp.int32)
    spare_pages = spare_ids // spare_count * PAGES_DEV + reserved + spare_ids % spare_count
    shuffled = jax.random.permutation(jax.random.fold_in(base_key, 3), spare_pages)
    long_table = shuffled[:LONG * LONG_PAGES].reshape(LONG, LONG_PAGES)
    long_rank = jnp.clip(jnp.cumsum(is_long) - 1, 0, LONG - 1)
    full_table = jnp.where(is_long[:, None] == 1, long_table[long_rank], short_table)
    short_len = jax.random.randint(jax.random.fold_in(base_key, 4), (REQS,), 1, SHORT_PAGES * PAGE + 1)
    long_len = jax.random.randint(jax.random.fold_in(base_key, 5), (REQS,), LONG_PAGES * PAGE // 2, LONG_PAGES * PAGE + 1)
    short_len = short_len.at[jnp.argmin(is_long)].set(SHORT_PAGES * PAGE)
    long_len = long_len.at[jnp.argmax(is_long)].set(LONG_PAGES * PAGE)
    lengths = jnp.where(is_long == 1, long_len, short_len)
    return (full_table.astype(jnp.int32), lengths.astype(jnp.int32))


def draw_page_table(key, part):
    full_table, lengths = page_layout(key)
    return full_table


def draw_cache_lengths(key, part):
    full_table, lengths = page_layout(key)
    return lengths


def level_of(key, extent, cuts, least, largest):
    loudness = 1.0
    for axis_at, shards_of in cuts:
        heights = jax.random.uniform(jax.random.fold_in(jax.random.fold_in(key, 6), axis_at), (shards_of,), jnp.float32, least / len(cuts), largest / len(cuts))
        loudness = loudness * jnp.repeat(jnp.exp(heights), extent[axis_at] // shards_of).reshape((-1,) + (1,) * (len(extent) - 1 - axis_at))
    return loudness


def assign_block(stream_key, own, number, rows, number_of, top, most, skew):
    order = jax.random.permutation(stream_key, number_of)
    heavy_load, common = load_shares(number_of, rows * top, most, skew, True), load_shares(number_of, rows * top, most, skew, False)
    places = jnp.arange(number_of)

    def named(tallies, turn):
        used = int((tallies > 0).sum())
        fixed = max(1, used // 4)
        moved = fixed + (places - fixed + turn * (used - fixed)) % max(1, number_of - fixed)
        return jnp.zeros((number_of,), jnp.int32).at[order[jnp.where(places < fixed, places, moved)]].set(jnp.asarray(tallies, jnp.int32))

    tallies = jnp.where(number % 4 == 0, named(heavy_load, number // 4), named(common, number - number // 4 - 1))
    mixed = jax.random.permutation(jax.random.fold_in(own, 3), number_of)
    source_of, receiver = mixed[0:number_of // 2 * 2:2], mixed[1:number_of // 2 * 2:2]
    margin = jnp.minimum(tallies[source_of] - 1, most - tallies[receiver]) // 2
    margin = jnp.where((source_of == order[0]) | (receiver == order[0]) | (tallies[receiver] == 0), 0, jnp.maximum(margin, 0))
    moved = jax.random.randint(jax.random.fold_in(own, 4), (number_of // 2,), 0, 1 << 20) % (margin + 1)
    tallies = tallies.at[source_of].add(-moved).at[receiver].add(moved)
    items = jnp.searchsorted(jnp.cumsum(tallies), jnp.arange(rows * top), side="right").astype(jnp.int32)
    grid = items.reshape(top, rows).T
    grid = grid[jax.random.permutation(jax.random.fold_in(own, 1), rows)]
    turn = jax.random.randint(jax.random.fold_in(own, 2), (rows, 1), 0, top)
    return jnp.take_along_axis(grid, (jnp.arange(top)[None, :] + turn) % top, axis=1)


def load_shares(number_of, total, most, slope, full):
    weights = [(1 << 20) // math.isqrt(grade ** slope) + 1 for grade in range(1, number_of + 1)]
    largest = most if full else min(most, max(-(-total // number_of), total * weights[0] // sum(weights)))
    least = 1 if total - largest >= number_of - 1 else 0
    holding, spare = [largest] + [least] * (number_of - 1), total - largest - least * (number_of - 1)
    while spare > 0:
        movable = [i for i in range(1, number_of) if holding[i] < largest] or [i for i in range(1, number_of) if holding[i] < most]
        mass, budget = sum([weights[i] for i in movable]), spare
        for i in movable:
            addition = min(most - holding[i], max(1, budget * weights[i] // mass), spare)
            holding[i] = holding[i] + addition
            spare = spare - addition
    return np.array(holding)


def scatter_about(own_key, extent, scale, limit, split=(), kind=jnp.bfloat16):
    values = scale * jax.random.normal(own_key, extent, jnp.float32)
    if split:
        values = values * level_of(own_key, extent, split, -0.22, 0.18)
    return jnp.clip(values, -limit, limit).astype(kind)


def setup_inputs(seed: int = 0) -> dict:
    splits = jax.random.split(jax.random.key(seed), 20)
    tokens_in = scatter_about(splits[0], (REQS, STEPS, D), 1.0, 6.0, ((0, 8),))
    attn_norm = jnp.clip(1.0 + 0.18 * jax.random.normal(splits[1], (D,), jnp.float32), 0.099609375, 1.8984375).astype(jnp.bfloat16)
    qkv_weight = scatter_about(splits[2], (D, 3, HEADS * HD), D ** -0.5, 0.125, ((2, 4),))
    qkv_bias = draw_qkv_bias(jax.random.fold_in(splits[19], 71), 0)
    out_weight = scatter_about(splits[4], (HEADS * HD, D), (HEADS * HD) ** -0.5, 0.125, ((0, 4),))
    cache_keys = draw_cache_keys(jax.random.fold_in(splits[19], 71), 0)
    cache_values = scatter_about(splits[6], (POOL, PAGE, HEADS * HD), 1.0, 6.0, ((0, 8), (2, 4)))
    page_table = draw_page_table(jax.random.fold_in(splits[19], 71), 0)
    cache_lengths = draw_cache_lengths(jax.random.fold_in(splits[19], 71), 0)
    mlp_norm = jnp.clip(1.0 + 0.18 * jax.random.normal(splits[9], (D,), jnp.float32), 0.099609375, 1.8984375).astype(jnp.bfloat16)
    routes_keys = jax.random.split(jax.random.fold_in(splits[10], 1), REQS * STEPS // (R_DEV * STEPS))
    routes_turns = jax.random.permutation(jax.random.fold_in(splits[10], 3), REQS * STEPS // (R_DEV * STEPS))
    routes = jax.vmap(lambda own, number: assign_block(jax.random.fold_in(splits[10], 2), own, number, R_DEV * STEPS, EXPERTS, TOPK, CAP, 2))(routes_keys, routes_turns).reshape((REQS, STEPS, TOPK))
    route_gates = jnp.clip(0.05 + 0.45 * jax.random.uniform(splits[11], (REQS, STEPS, TOPK), jnp.float32) ** level_of(splits[11], (REQS, STEPS, TOPK), ((0, 8),), -0.2, 0.2), 0.05, 0.5)
    expert_w_gate = scatter_about(splits[12], (EXPERTS, D, FE), D ** -0.5, 0.125, ((0, 8), (2, 4)))
    expert_w_up = scatter_about(splits[13], (EXPERTS, D, FE), D ** -0.5, 0.125, ((0, 8), (2, 4)))
    expert_w_down = scatter_about(splits[14], (EXPERTS, FE, D), FE ** -0.5, 0.15625, ((0, 8), (1, 4)))
    shared_w_gate = scatter_about(splits[15], (D, FS), D ** -0.5, 0.125, ((0, 4), (1, 8)))
    shared_w_up = scatter_about(splits[16], (D, FS), D ** -0.5, 0.125, ((0, 4), (1, 8)))
    shared_w_down = scatter_about(splits[17], (FS, D), FS ** -0.5, 0.078125, ((0, 8), (1, 4)))
    shared_switch = scatter_about(splits[18], (D,), D ** -0.5, 0.125)
    return {"tokens_in": tokens_in, "attn_norm": attn_norm, "qkv_weight": qkv_weight, "qkv_bias": qkv_bias, "out_weight": out_weight, "cache_keys": cache_keys, "cache_values": cache_values, "page_table": page_table, "cache_lengths": cache_lengths, "mlp_norm": mlp_norm, "routes": routes, "route_gates": route_gates, "expert_w_gate": expert_w_gate, "expert_w_up": expert_w_up, "expert_w_down": expert_w_down, "shared_w_gate": shared_w_gate, "shared_w_up": shared_w_up, "shared_w_down": shared_w_down, "shared_switch": shared_switch}


NEG = -1e+30
EPS = 1e-06
THETA = 1000000.0
HIGHEST = lax.Precision.HIGHEST

def rms_norm(inputs, gain_vector):
    values = inputs.astype(jnp.float32)
    scaled = values * lax.rsqrt(lax.optimization_barrier(jnp.mean(values * values, axis=-1, keepdims=True)) + EPS)
    return (scaled * gain_vector.astype(jnp.float32)).astype(jnp.bfloat16)

def rotate(values, positions):
    half_dim = values.shape[-1] // 2
    exponents = jnp.arange(half_dim, dtype=jnp.float32) * (2.0 / values.shape[-1])
    frequency = jnp.power(THETA, -exponents)
    angles = positions.astype(jnp.float32)[..., None, None] * frequency
    cosines = jnp.cos(angles)
    sine_part = jnp.sin(angles)
    front_half = values[..., :half_dim]
    back_half = values[..., half_dim:]
    return jnp.concatenate([front_half * cosines - back_half * sine_part, back_half * cosines + front_half * sine_part], axis=-1)

def one_request(packed, cache_keys, cache_values):
    table_row, length, queries = packed
    score_scale = 1.0 / HD ** 0.5
    safe_rows = jnp.maximum(table_row, 0)
    keys_here = cache_keys[safe_rows].reshape(LONG_PAGES, PAGE, HEADS, HD).astype(jnp.float32)
    values_here = cache_values[safe_rows].reshape(LONG_PAGES, PAGE, HEADS, HD).astype(jnp.float32)
    scores = jnp.einsum('shd,pkhd->pshk', queries.astype(jnp.float32), keys_here) * score_scale
    token_pos = jnp.arange(LONG_PAGES, dtype=jnp.int32)[:, None] * PAGE + jnp.arange(PAGE, dtype=jnp.int32)[None, :]
    live = (table_row[:, None] >= 0) & (token_pos < length)
    page_mask = live[:, None, None, :]
    masked = jnp.where(page_mask, scores, NEG)
    page_max = lax.optimization_barrier(jnp.max(masked, axis=-1))
    weights = jnp.where(page_mask, jnp.exp(masked - page_max[..., None]), 0.0)
    page_sum = lax.optimization_barrier(jnp.sum(weights, axis=-1))
    rounded = lax.optimization_barrier(weights.astype(jnp.bfloat16)).astype(jnp.float32)
    page_out = jnp.einsum('pshk,pkhd->pshd', rounded, values_here)
    cache_max = lax.optimization_barrier(jnp.max(page_max, axis=0))
    factors = jnp.exp(page_max - cache_max[None])
    cache_out = jnp.einsum('psh,pshd->shd', factors, page_out, precision=HIGHEST)
    cache_sum = lax.optimization_barrier(jnp.sum(factors * page_sum, axis=0))
    return (cache_out, cache_max, cache_sum)

def reference(tokens_in, attn_norm, qkv_weight, qkv_bias, out_weight, cache_keys, cache_values, page_table, cache_lengths, mlp_norm, routes, route_gates, expert_w_gate, expert_w_up, expert_w_down, shared_w_gate, shared_w_up, shared_w_down, shared_switch):
    score_scale = 1.0 / HD ** 0.5
    normed = rms_norm(tokens_in, attn_norm)
    projected = jnp.einsum('rsd,dcf->rscf', normed.astype(jnp.float32), qkv_weight.astype(jnp.float32)) + qkv_bias.astype(jnp.float32)
    positions = cache_lengths[:, None] + jnp.arange(STEPS, dtype=jnp.int32)[None, :]
    head_shape = (REQS, STEPS, HEADS, HD)
    query_new = rotate(projected[:, :, 0].reshape(head_shape), positions).astype(jnp.bfloat16)
    key_new = rotate(projected[:, :, 1].reshape(head_shape), positions).astype(jnp.bfloat16)
    value_new = projected[:, :, 2].reshape(head_shape).astype(jnp.bfloat16)
    cache_out, cache_max, cache_sum = lax.map(partial(one_request, cache_keys=cache_keys, cache_values=cache_values), (page_table, cache_lengths, query_new))
    new_scores = jnp.einsum('rshd,rthd->rsht', query_new.astype(jnp.float32), key_new.astype(jnp.float32)) * score_scale
    causal = jnp.arange(STEPS)[:, None] >= jnp.arange(STEPS)[None, :]
    new_mask = causal[None, :, None, :]
    new_masked = jnp.where(new_mask, new_scores, NEG)
    new_max = lax.optimization_barrier(jnp.max(new_masked, axis=-1))
    new_weights = jnp.where(new_mask, jnp.exp(new_masked - new_max[..., None]), 0.0)
    new_sum = lax.optimization_barrier(jnp.sum(new_weights, axis=-1))
    new_rounded = lax.optimization_barrier(new_weights.astype(jnp.bfloat16)).astype(jnp.float32)
    new_out = jnp.einsum('rsht,rthd->rshd', new_rounded, value_new.astype(jnp.float32))
    top_max = jnp.maximum(cache_max, new_max)
    cache_factor = jnp.exp(cache_max - top_max)
    new_factor = jnp.exp(new_max - top_max)
    attended = (cache_out * cache_factor[..., None] + new_out * new_factor[..., None]) / (cache_sum * cache_factor + new_sum * new_factor)[..., None]
    attended = attended.astype(jnp.bfloat16).reshape(REQS * STEPS, HEADS * HD)
    resid = tokens_in.reshape(REQS * STEPS, D).astype(jnp.float32) + jnp.dot(attended, out_weight, preferred_element_type=jnp.float32)
    mixed = rms_norm(resid, mlp_norm)
    flat_routes = routes.reshape(REQS * STEPS, TOPK)
    flat_gates = route_gates.reshape(REQS * STEPS, TOPK)

    def add_expert(total, packed):
        expert_index, w_gate, w_up, w_down = packed
        gate_pre = jnp.dot(mixed, w_gate, preferred_element_type=jnp.float32)
        up_pre = jnp.dot(mixed, w_up, preferred_element_type=jnp.float32)
        hidden = (jax.nn.silu(gate_pre) * up_pre).astype(jnp.bfloat16)
        produced = jnp.dot(hidden, w_down, preferred_element_type=jnp.float32).astype(jnp.bfloat16)
        chosen = lax.optimization_barrier(jnp.sum(jnp.where(flat_routes == expert_index, flat_gates, 0.0), axis=1))
        return (total + chosen[:, None] * produced.astype(jnp.float32), None)
    moe_out, unused = lax.scan(add_expert, jnp.zeros((REQS * STEPS, D), jnp.float32), (jnp.arange(EXPERTS, dtype=jnp.int32), expert_w_gate, expert_w_up, expert_w_down))
    shared_gate_pre = jnp.dot(mixed, shared_w_gate, preferred_element_type=jnp.float32)
    shared_up_pre = jnp.dot(mixed, shared_w_up, preferred_element_type=jnp.float32)
    shared_hidden = (jax.nn.silu(shared_gate_pre) * shared_up_pre).astype(jnp.bfloat16)
    shared_value = jnp.dot(shared_hidden, shared_w_down, preferred_element_type=jnp.float32)
    switch = jax.nn.sigmoid(jnp.dot(mixed, shared_switch, preferred_element_type=jnp.float32))
    final = resid + moe_out + switch[:, None] * shared_value
    return final.astype(jnp.bfloat16).reshape(REQS, STEPS, D)
```

```python
import math

import jax
import jax.numpy as jnp
from jax import lax
from jax.sharding import PartitionSpec as P

HD = 128
TOPK = 4


NEG = -1e30
EPS = 1e-06
THETA = 1000000.0
HIGHEST = lax.Precision.HIGHEST


def rms_norm(inputs, gain_vector):
    values = inputs.astype(jnp.float32)
    scaled = values * lax.rsqrt(jnp.mean(values * values, axis=-1, keepdims=True) + EPS)
    return (scaled * gain_vector.astype(jnp.float32)).astype(jnp.bfloat16)


def rotate(values, positions):
    half_dim = values.shape[-1] // 2
    exponents = jnp.arange(half_dim, dtype=jnp.float32) * (2.0 / values.shape[-1])
    frequency = jnp.power(THETA, -exponents)
    angles = positions.astype(jnp.float32)[..., None, None] * frequency
    cosines = jnp.cos(angles)
    sine_part = jnp.sin(angles)
    front_half = values[..., :half_dim]
    back_half = values[..., half_dim:]
    return jnp.concatenate(
        [
            front_half * cosines - back_half * sine_part,
            back_half * cosines + front_half * sine_part,
        ],
        axis=-1,
    )


def bcast_a2a(values, axis, count):
    spread = jnp.broadcast_to(values[None], (count,) + values.shape)
    return lax.all_to_all(spread, axis, 0, 0, tiled=True).reshape(
        (count * values.shape[0],) + values.shape[1:]
    )


def per_device(
    tokens_in,
    attn_norm,
    qkv_weight,
    qkv_bias,
    out_weight,
    cache_keys,
    cache_values,
    page_table,
    cache_lengths,
    mlp_norm,
    routes,
    route_gates,
    expert_w_gate,
    expert_w_up,
    expert_w_down,
    shared_w_gate,
    shared_w_up,
    shared_w_down,
    shared_switch,
):
    req_rows, step_count, model_width = tokens_in.shape
    head_width = qkv_weight.shape[2]
    local_heads = head_width // HD
    req_count = lax.axis_size("req")
    tp_count = lax.axis_size("tp")
    req_index = lax.axis_index("req")
    tp_index = lax.axis_index("tp")
    all_requests = page_table.shape[0]
    pool_here = cache_keys.shape[0]
    page_len = cache_keys.shape[1]
    score_scale = 1.0 / math.sqrt(HD)
    col_share = model_width // tp_count
    row_count = req_rows * step_count
    normed = rms_norm(tokens_in, attn_norm)
    projected = jnp.einsum(
        "rsd,dcf->rscf", normed, qkv_weight, preferred_element_type=jnp.float32
    ) + qkv_bias.astype(jnp.float32)
    own_lengths = lax.dynamic_slice_in_dim(cache_lengths, req_index * req_rows, req_rows)
    positions = own_lengths[:, None] + jnp.arange(step_count, dtype=jnp.int32)[None, :]
    head_shape = (req_rows, step_count, local_heads, HD)
    query_new = rotate(projected[:, :, 0].reshape(head_shape), positions).astype(jnp.bfloat16)
    key_new = rotate(projected[:, :, 1].reshape(head_shape), positions).astype(jnp.bfloat16)
    value_new = projected[:, :, 2].reshape(head_shape).astype(jnp.bfloat16)
    query_all = bcast_a2a(query_new, "req", req_count)
    slot_ids = req_index * pool_here + jnp.arange(pool_here, dtype=jnp.int32)
    matches = (page_table[:, :, None] == slot_ids[None, None, :]).astype(jnp.int32)
    request_ids = jnp.arange(all_requests, dtype=jnp.int32)
    page_ids = jnp.arange(page_table.shape[1], dtype=jnp.int32)
    owner = jnp.sum(matches * request_ids[:, None, None], axis=(0, 1))
    logical = jnp.sum(matches * page_ids[None, :, None], axis=(0, 1))
    present = jnp.sum(matches, axis=(0, 1)) > 0
    token_pos = logical[:, None] * page_len + jnp.arange(page_len, dtype=jnp.int32)[None, :]
    live = present[:, None] & (token_pos < cache_lengths[owner][:, None])
    page_queries = query_all[owner]
    page_keys = cache_keys.reshape(pool_here, page_len, local_heads, HD)
    page_values = cache_values.reshape(pool_here, page_len, local_heads, HD)
    scores = (
        jnp.einsum("pshd,pkhd->pshk", page_queries, page_keys, preferred_element_type=jnp.float32)
        * score_scale
    )
    page_mask = live[:, None, None, :]
    masked = jnp.where(page_mask, scores, NEG)
    page_max = jnp.max(masked, axis=-1)
    weights = jnp.where(page_mask, jnp.exp(masked - page_max[..., None]), 0.0)
    page_sum = jnp.sum(weights, axis=-1)
    page_out = jnp.einsum(
        "pshk,pkhd->pshd",
        weights.astype(jnp.bfloat16),
        page_values,
        preferred_element_type=jnp.float32,
    )
    belongs = (owner[None, :] == request_ids[:, None]) & present[None, :]
    owned = belongs[:, :, None, None]
    local_max = jnp.max(jnp.where(owned, page_max[None], NEG), axis=1)
    factors = jnp.where(owned, jnp.exp(page_max[None] - local_max[:, None]), 0.0)
    local_out = jnp.einsum("rpsh,pshd->rshd", factors, page_out, precision=HIGHEST)
    local_sum = jnp.einsum("rpsh,psh->rsh", factors, page_sum, precision=HIGHEST)
    stat_width = step_count * local_heads
    out_width = stat_width * HD
    packed = jnp.concatenate(
        [
            local_out.reshape(req_count, req_rows * out_width),
            local_max.reshape(req_count, req_rows * stat_width),
            local_sum.reshape(req_count, req_rows * stat_width),
        ],
        axis=1,
    )
    gathered = lax.all_to_all(packed, "req", 0, 0, tiled=True)
    part_out = gathered[:, : req_rows * out_width].reshape(req_count, req_rows, step_count, local_heads, HD)
    part_max = gathered[:, req_rows * out_width : req_rows * (out_width + stat_width)].reshape(
        req_count, req_rows, step_count, local_heads
    )
    part_sum = gathered[:, req_rows * (out_width + stat_width) :].reshape(
        req_count, req_rows, step_count, local_heads
    )
    cache_max = jnp.max(part_max, axis=0)
    rescale = jnp.exp(part_max - cache_max[None])
    cache_out = jnp.sum(part_out * rescale[..., None], axis=0)
    cache_sum = jnp.sum(part_sum * rescale, axis=0)
    new_scores = (
        jnp.einsum("rshd,rthd->rsht", query_new, key_new, preferred_element_type=jnp.float32)
        * score_scale
    )
    causal = jnp.arange(step_count)[:, None] >= jnp.arange(step_count)[None, :]
    new_mask = causal[None, :, None, :]
    new_masked = jnp.where(new_mask, new_scores, NEG)
    new_max = jnp.max(new_masked, axis=-1)
    new_weights = jnp.where(new_mask, jnp.exp(new_masked - new_max[..., None]), 0.0)
    new_sum = jnp.sum(new_weights, axis=-1)
    new_out = jnp.einsum(
        "rsht,rthd->rshd",
        new_weights.astype(jnp.bfloat16),
        value_new,
        preferred_element_type=jnp.float32,
    )
    top_max = jnp.maximum(cache_max, new_max)
    cache_factor = jnp.exp(cache_max - top_max)
    new_factor = jnp.exp(new_max - top_max)
    attended = (cache_out * cache_factor[..., None] + new_out * new_factor[..., None]) / (
        cache_sum * cache_factor + new_sum * new_factor
    )[..., None]
    attended = attended.astype(jnp.bfloat16).reshape(row_count, head_width)
    attn_part = jnp.dot(attended, out_weight, preferred_element_type=jnp.float32)
    attn_full = jnp.sum(bcast_a2a(attn_part, "tp", tp_count).reshape(tp_count, row_count, model_width), axis=0)
    resid = tokens_in.reshape(row_count, model_width).astype(jnp.float32) + attn_full
    mixed = rms_norm(resid, mlp_norm)
    expert_count = req_count * expert_w_gate.shape[0]
    capacity = max(2, (row_count * TOPK + expert_count - 1) // expert_count)
    picks = routes.reshape(row_count * TOPK)
    gates_flat = route_gates.reshape(row_count * TOPK)
    expert_hot = (picks[:, None] == jnp.arange(expert_count, dtype=jnp.int32)[None, :]).astype(
        jnp.int32
    )
    slot_index = jnp.sum((jnp.cumsum(expert_hot, axis=0) - 1) * expert_hot, axis=1)
    destination = picks * capacity + slot_index
    dest_hot = (
        destination[:, None] == jnp.arange(expert_count * capacity, dtype=jnp.int32)[None, :]
    ).astype(jnp.float32)
    token_hot = (
        (jnp.arange(row_count * TOPK, dtype=jnp.int32) // TOPK)[:, None]
        == jnp.arange(row_count, dtype=jnp.int32)[None, :]
    ).astype(jnp.float32)
    placement = jnp.einsum("cx,ct->xt", dest_hot, token_hot, precision=HIGHEST).astype(jnp.bfloat16)
    outgoing = jnp.dot(placement, mixed, preferred_element_type=jnp.float32).astype(jnp.bfloat16)
    combine_map = jnp.einsum(
        "ct,cx->tx", token_hot, dest_hot * gates_flat[:, None], precision=HIGHEST
    )
    w_gate_here = expert_w_gate[0]
    w_up_here = expert_w_up[0]
    w_down_here = expert_w_down[0]
    mixed_cols = lax.dynamic_slice_in_dim(mixed, tp_index * col_share, col_share, 1)
    shared_send = jnp.broadcast_to(mixed_cols[None], (req_count, row_count, col_share))
    dispatch = jnp.concatenate(
        [
            outgoing.reshape(req_count, capacity * model_width),
            shared_send.reshape(req_count, row_count * col_share),
        ],
        axis=1,
    )
    received = lax.all_to_all(dispatch, "req", 0, 0, tiled=True)
    item_count = capacity
    flat_rows = received[:, : capacity * model_width].reshape(req_count * capacity, model_width)
    piece = received[:, capacity * model_width :].reshape(req_count * row_count, col_share)
    gate_pre = jnp.dot(flat_rows, w_gate_here, preferred_element_type=jnp.float32)
    up_pre = jnp.dot(flat_rows, w_up_here, preferred_element_type=jnp.float32)
    hidden = (jax.nn.silu(gate_pre) * up_pre).astype(jnp.bfloat16)
    partial_out = jnp.dot(hidden, w_down_here, preferred_element_type=jnp.float32)
    expert_rows = req_count * capacity
    partial_split = partial_out.reshape(expert_rows, tp_count, col_share).transpose(1, 0, 2)
    gate_part = jnp.dot(piece, shared_w_gate, preferred_element_type=jnp.float32)
    up_part = jnp.dot(piece, shared_w_up, preferred_element_type=jnp.float32)
    unit_count = shared_w_gate.shape[1]
    all_rows = req_count * row_count
    share_rows = all_rows // tp_count
    shared_pre = jnp.concatenate([gate_part, up_part], axis=1).reshape(
        tp_count, share_rows * 2 * unit_count
    )
    reduce_in = jnp.concatenate(
        [partial_split.reshape(tp_count, expert_rows * col_share), shared_pre], axis=1
    )
    reduce_out = jnp.sum(lax.all_to_all(reduce_in, "tp", 0, 0, tiled=True), axis=0)
    expert_sum = reduce_out[: expert_rows * col_share].reshape(expert_rows, col_share)
    shared_sum = reduce_out[expert_rows * col_share :].reshape(share_rows, 2 * unit_count)
    shared_hidden = (jax.nn.silu(shared_sum[:, :unit_count]) * shared_sum[:, unit_count:]).astype(
        jnp.bfloat16
    )
    hidden_all = bcast_a2a(shared_hidden, "tp", tp_count).reshape(all_rows, unit_count)
    shared_down = jnp.dot(hidden_all, shared_w_down, preferred_element_type=jnp.float32)
    ey = expert_sum.astype(jnp.bfloat16).astype(jnp.float32)
    back_in = jnp.concatenate(
        [
            ey.reshape(req_count, capacity * col_share),
            shared_down.reshape(req_count, row_count * col_share),
        ],
        axis=1,
    )
    back = lax.all_to_all(back_in, "req", 0, 0, tiled=True)
    returned = back[:, : capacity * col_share].reshape(expert_count * capacity, col_share)
    shared_mine = jnp.sum(
        back[:, capacity * col_share :].reshape(req_count, row_count, col_share), axis=0
    )
    moe_out = jnp.dot(combine_map, returned, precision=HIGHEST)
    switch = jax.nn.sigmoid(jnp.dot(mixed, shared_switch, preferred_element_type=jnp.float32))
    resid_mine = lax.dynamic_slice_in_dim(resid, tp_index * col_share, col_share, 1)
    final = resid_mine + moe_out + switch[:, None] * shared_mine
    return final.astype(jnp.bfloat16).reshape(req_rows, step_count, col_share)


def solution(mesh):
    return jax.shard_map(
        per_device,
        mesh=mesh,
        in_specs=(
            P("req", None, None),
            P(),
            P(None, None, "tp"),
            P(None, "tp"),
            P("tp", None),
            P("req", None, "tp"),
            P("req", None, "tp"),
            P(),
            P(),
            P(),
            P("req", None, None),
            P("req", None, None),
            P("req", None, "tp"),
            P("req", None, "tp"),
            P("req", "tp", None),
            P("tp", "req"),
            P("tp", "req"),
            P("req", "tp"),
            P(),
        ),
        out_specs=P("req", None, "tp"),
        check_vma=False,
    )
```

```python
import math

import jax
import jax.numpy as jnp
from jax import lax
from jax.sharding import PartitionSpec as P

HD = 128
TOPK = 4


NEG = -1e30
EPS = 1e-06
THETA = 1000000.0
HIGHEST = lax.Precision.HIGHEST


def rms_norm(inputs, gain_vector):
    values = inputs.astype(jnp.float32)
    scaled = values * lax.rsqrt(jnp.mean(values * values, axis=-1, keepdims=True) + EPS)
    return (scaled * gain_vector.astype(jnp.float32)).astype(jnp.bfloat16)


def rotate(values, positions):
    half_dim = values.shape[-1] // 2
    exponents = jnp.arange(half_dim, dtype=jnp.float32) * (2.0 / values.shape[-1])
    frequency = jnp.power(THETA, -exponents)
    angles = positions.astype(jnp.float32)[..., None, None] * frequency
    cosines = jnp.cos(angles)
    sine_part = jnp.sin(angles)
    front_half = values[..., :half_dim]
    back_half = values[..., half_dim:]
    return jnp.concatenate(
        [
            front_half * cosines - back_half * sine_part,
            back_half * cosines + front_half * sine_part,
        ],
        axis=-1,
    )


def bcast_a2a(values, axis, count):
    spread = jnp.broadcast_to(values[None], (count,) + values.shape)
    return lax.all_to_all(spread, axis, 0, 0, tiled=True).reshape(
        (count * values.shape[0],) + values.shape[1:]
    )


def per_device(
    tokens_in,
    attn_norm,
    qkv_weight,
    qkv_bias,
    out_weight,
    cache_keys,
    cache_values,
    page_table,
    cache_lengths,
    mlp_norm,
    routes,
    route_gates,
    expert_w_gate,
    expert_w_up,
    expert_w_down,
    shared_w_gate,
    shared_w_up,
    shared_w_down,
    shared_switch,
):
    req_rows, step_count, model_width = tokens_in.shape
    head_width = qkv_weight.shape[2]
    local_heads = head_width // HD
    req_count = lax.axis_size("req")
    tp_count = lax.axis_size("tp")
    req_index = lax.axis_index("req")
    tp_index = lax.axis_index("tp")
    all_requests = page_table.shape[0]
    pool_here = cache_keys.shape[0]
    page_len = cache_keys.shape[1]
    score_scale = 1.0 / math.sqrt(HD)
    col_share = model_width // tp_count
    row_count = req_rows * step_count
    normed = rms_norm(tokens_in, attn_norm)
    projected = jnp.einsum(
        "rsd,dcf->rscf", normed, qkv_weight, preferred_element_type=jnp.float32
    ) + qkv_bias.astype(jnp.float32)
    own_lengths = lax.dynamic_slice_in_dim(cache_lengths, req_index * req_rows, req_rows)
    positions = own_lengths[:, None] + jnp.arange(step_count, dtype=jnp.int32)[None, :]
    head_shape = (req_rows, step_count, local_heads, HD)
    query_new = rotate(projected[:, :, 0].reshape(head_shape), positions).astype(jnp.bfloat16)
    key_new = rotate(projected[:, :, 1].reshape(head_shape), positions).astype(jnp.bfloat16)
    value_new = projected[:, :, 2].reshape(head_shape).astype(jnp.bfloat16)
    query_all = bcast_a2a(query_new, "req", req_count)
    slot_ids = req_index * pool_here + jnp.arange(pool_here, dtype=jnp.int32)
    matches = (page_table[:, :, None] == slot_ids[None, None, :]).astype(jnp.int32)
    request_ids = jnp.arange(all_requests, dtype=jnp.int32)
    page_ids = jnp.arange(page_table.shape[1], dtype=jnp.int32)
    owner = jnp.sum(matches * request_ids[:, None, None], axis=(0, 1))
    logical = jnp.sum(matches * page_ids[None, :, None], axis=(0, 1))
    present = jnp.sum(matches, axis=(0, 1)) > 0
    token_pos = logical[:, None] * page_len + jnp.arange(page_len, dtype=jnp.int32)[None, :]
    live = present[:, None] & (token_pos < cache_lengths[owner][:, None])
    page_queries = query_all[owner]
    head_eye = jnp.arange(local_heads)[:, None] == jnp.arange(local_heads)[None, :]
    block_queries = jnp.where(
        head_eye[None, None, :, :, None], page_queries[:, :, :, None, :], jnp.zeros((), jnp.bfloat16)
    ).reshape(pool_here, step_count * local_heads, head_width)
    scores = (
        jnp.einsum("pxd,pkd->pxk", block_queries, cache_keys, preferred_element_type=jnp.float32)
        * score_scale
    ).reshape(pool_here, step_count, local_heads, page_len)
    page_mask = live[:, None, None, :]
    masked = jnp.where(page_mask, scores, NEG)
    page_max = jnp.max(masked, axis=-1)
    weights = jnp.where(page_mask, jnp.exp(masked - page_max[..., None]), 0.0)
    page_sum = jnp.sum(weights, axis=-1)
    wide_out = jnp.einsum(
        "pxk,pkd->pxd",
        weights.astype(jnp.bfloat16).reshape(pool_here, step_count * local_heads, page_len),
        cache_values,
        preferred_element_type=jnp.float32,
    ).reshape(pool_here, step_count, local_heads, local_heads, HD)
    page_out = jnp.sum(jnp.where(head_eye[None, None, :, :, None], wide_out, 0.0), axis=3)
    belongs = (owner[None, :] == request_ids[:, None]) & present[None, :]
    owned = belongs[:, :, None, None]
    local_max = jnp.max(jnp.where(owned, page_max[None], NEG), axis=1)
    factors = jnp.where(owned, jnp.exp(page_max[None] - local_max[:, None]), 0.0)
    local_out = jnp.einsum("rpsh,pshd->rshd", factors, page_out, precision=HIGHEST)
    local_sum = jnp.einsum("rpsh,psh->rsh", factors, page_sum, precision=HIGHEST)
    stat_width = step_count * local_heads
    stat_row = jnp.concatenate(
        [
            local_max.reshape(all_requests, stat_width),
            local_sum.reshape(all_requests, stat_width),
            jnp.zeros((all_requests, HD - 2 * stat_width), jnp.float32),
        ],
        axis=1,
    )
    packed = jnp.concatenate(
        [local_out.reshape(all_requests, stat_width, HD), stat_row[:, None, :]], axis=1
    )
    gathered = lax.all_to_all(packed, "req", 0, 0, tiled=True).reshape(
        req_count, req_rows, stat_width + 1, HD
    )
    part_out = gathered[:, :, :stat_width, :]
    part_max = gathered[:, :, stat_width, :stat_width]
    part_sum = gathered[:, :, stat_width, stat_width : 2 * stat_width]
    cache_max = jnp.max(part_max, axis=0)
    rescale = jnp.exp(part_max - cache_max[None])
    cache_out = jnp.sum(part_out * rescale[..., None], axis=0).reshape(
        req_rows, step_count, local_heads, HD
    )
    cache_sum = jnp.sum(part_sum * rescale, axis=0).reshape(req_rows, step_count, local_heads)
    cache_max = cache_max.reshape(req_rows, step_count, local_heads)
    new_scores = (
        jnp.einsum("rshd,rthd->rsht", query_new, key_new, preferred_element_type=jnp.float32)
        * score_scale
    )
    causal = jnp.arange(step_count)[:, None] >= jnp.arange(step_count)[None, :]
    new_mask = causal[None, :, None, :]
    new_masked = jnp.where(new_mask, new_scores, NEG)
    new_max = jnp.max(new_masked, axis=-1)
    new_weights = jnp.where(new_mask, jnp.exp(new_masked - new_max[..., None]), 0.0)
    new_sum = jnp.sum(new_weights, axis=-1)
    new_out = jnp.einsum(
        "rsht,rthd->rshd",
        new_weights.astype(jnp.bfloat16),
        value_new,
        preferred_element_type=jnp.float32,
    )
    top_max = jnp.maximum(cache_max, new_max)
    cache_factor = jnp.exp(cache_max - top_max)
    new_factor = jnp.exp(new_max - top_max)
    attended = (cache_out * cache_factor[..., None] + new_out * new_factor[..., None]) / (
        cache_sum * cache_factor + new_sum * new_factor
    )[..., None]
    attended = attended.astype(jnp.bfloat16).reshape(row_count, head_width)
    attn_part = jnp.dot(attended, out_weight, preferred_element_type=jnp.float32)
    attn_full = jnp.sum(bcast_a2a(attn_part, "tp", tp_count).reshape(tp_count, row_count, model_width), axis=0)
    resid = tokens_in.reshape(row_count, model_width).astype(jnp.float32) + attn_full
    mixed = rms_norm(resid, mlp_norm)
    expert_count = req_count * expert_w_gate.shape[0]
    capacity = max(2, (row_count * TOPK + expert_count - 1) // expert_count)
    picks = routes.reshape(row_count * TOPK)
    gates_flat = route_gates.reshape(row_count * TOPK)
    expert_hot = (picks[:, None] == jnp.arange(expert_count, dtype=jnp.int32)[None, :]).astype(
        jnp.int32
    )
    slot_index = jnp.sum((jnp.cumsum(expert_hot, axis=0) - 1) * expert_hot, axis=1)
    destination = picks * capacity + slot_index
    dest_hot = (
        destination[:, None] == jnp.arange(expert_count * capacity, dtype=jnp.int32)[None, :]
    ).astype(jnp.float32)
    token_hot = (
        (jnp.arange(row_count * TOPK, dtype=jnp.int32) // TOPK)[:, None]
        == jnp.arange(row_count, dtype=jnp.int32)[None, :]
    ).astype(jnp.float32)
    placement = jnp.einsum("cx,ct->xt", dest_hot, token_hot, precision=HIGHEST).astype(jnp.bfloat16)
    outgoing = jnp.dot(placement, mixed, preferred_element_type=jnp.float32).astype(jnp.bfloat16)
    combine_map = jnp.einsum(
        "ct,cx->tx", token_hot, dest_hot * gates_flat[:, None], precision=HIGHEST
    )
    w_gate_here = expert_w_gate[0]
    w_up_here = expert_w_up[0]
    w_down_here = expert_w_down[0]
    mixed_cols = lax.dynamic_slice_in_dim(mixed, tp_index * col_share, col_share, 1)
    shared_send = jnp.broadcast_to(mixed_cols[None], (req_count, row_count, col_share))
    dispatch = jnp.concatenate(
        [
            outgoing.reshape(req_count, capacity * model_width),
            shared_send.reshape(req_count, row_count * col_share),
        ],
        axis=1,
    )
    received = lax.all_to_all(dispatch, "req", 0, 0, tiled=True)
    item_count = capacity
    flat_rows = received[:, : capacity * model_width].reshape(req_count * capacity, model_width)
    piece = received[:, capacity * model_width :].reshape(req_count * row_count, col_share)
    gate_pre = jnp.dot(flat_rows, w_gate_here, preferred_element_type=jnp.float32)
    up_pre = jnp.dot(flat_rows, w_up_here, preferred_element_type=jnp.float32)
    hidden = (jax.nn.silu(gate_pre) * up_pre).astype(jnp.bfloat16)
    expert_rows = req_count * capacity
    partial_split = jnp.einsum(
        "rk,kjc->jrc",
        hidden,
        w_down_here.reshape(w_down_here.shape[0], tp_count, col_share),
        preferred_element_type=jnp.float32,
    )
    gate_part = jnp.dot(piece, shared_w_gate, preferred_element_type=jnp.float32)
    up_part = jnp.dot(piece, shared_w_up, preferred_element_type=jnp.float32)
    unit_count = shared_w_gate.shape[1]
    all_rows = req_count * row_count
    share_rows = all_rows // tp_count
    shared_pre = jnp.concatenate([gate_part, up_part], axis=1).reshape(
        tp_count, share_rows * 2 * unit_count
    )
    reduce_in = jnp.concatenate(
        [partial_split.reshape(tp_count, expert_rows * col_share), shared_pre], axis=1
    )
    reduce_out = jnp.sum(lax.all_to_all(reduce_in, "tp", 0, 0, tiled=True), axis=0)
    expert_sum = reduce_out[: expert_rows * col_share].reshape(expert_rows, col_share)
    shared_sum = reduce_out[expert_rows * col_share :].reshape(share_rows, 2 * unit_count)
    shared_hidden = (jax.nn.silu(shared_sum[:, :unit_count]) * shared_sum[:, unit_count:]).astype(
        jnp.bfloat16
    )
    hidden_all = bcast_a2a(shared_hidden, "tp", tp_count).reshape(all_rows, unit_count)
    shared_down = jnp.dot(hidden_all, shared_w_down, preferred_element_type=jnp.float32)
    ey = expert_sum.astype(jnp.bfloat16).astype(jnp.float32)
    back_in = jnp.concatenate(
        [
            ey.reshape(req_count, capacity * col_share),
            shared_down.reshape(req_count, row_count * col_share),
        ],
        axis=1,
    )
    back = lax.all_to_all(back_in, "req", 0, 0, tiled=True)
    returned = back[:, : capacity * col_share].reshape(expert_count * capacity, col_share)
    shared_mine = jnp.sum(
        back[:, capacity * col_share :].reshape(req_count, row_count, col_share), axis=0
    )
    moe_out = jnp.dot(combine_map, returned, precision=HIGHEST)
    switch = jax.nn.sigmoid(jnp.dot(mixed, shared_switch, preferred_element_type=jnp.float32))
    resid_mine = lax.dynamic_slice_in_dim(resid, tp_index * col_share, col_share, 1)
    final = resid_mine + moe_out + switch[:, None] * shared_mine
    return final.astype(jnp.bfloat16).reshape(req_rows, step_count, col_share)


def solution(mesh):
    return jax.shard_map(
        per_device,
        mesh=mesh,
        in_specs=(
            P("req", None, None),
            P(),
            P(None, None, "tp"),
            P(None, "tp"),
            P("tp", None),
            P("req", None, "tp"),
            P("req", None, "tp"),
            P(),
            P(),
            P(),
            P("req", None, None),
            P("req", None, None),
            P("req", None, "tp"),
            P("req", None, "tp"),
            P("req", "tp", None),
            P("tp", "req"),
            P("tp", "req"),
            P("req", "tp"),
            P(),
        ),
        out_specs=P("req", None, "tp"),
        check_vma=False,
    )
```

```python
import math

import jax
import jax.numpy as jnp
from jax import lax
from jax.sharding import PartitionSpec as P

HD = 128
TOPK = 4


NEG = -1e30
EPS = 1e-06
THETA = 1000000.0
HIGHEST = lax.Precision.HIGHEST


def rms_norm(inputs, gain_vector):
    values = inputs.astype(jnp.float32)
    scaled = values * lax.rsqrt(jnp.mean(values * values, axis=-1, keepdims=True) + EPS)
    return (scaled * gain_vector.astype(jnp.float32)).astype(jnp.bfloat16)


def rotate(values, positions):
    half_dim = values.shape[-1] // 2
    exponents = jnp.arange(half_dim, dtype=jnp.float32) * (2.0 / values.shape[-1])
    frequency = jnp.power(THETA, -exponents)
    angles = positions.astype(jnp.float32)[..., None, None] * frequency
    cosines = jnp.cos(angles)
    sine_part = jnp.sin(angles)
    front_half = values[..., :half_dim]
    back_half = values[..., half_dim:]
    return jnp.concatenate(
        [
            front_half * cosines - back_half * sine_part,
            back_half * cosines + front_half * sine_part,
        ],
        axis=-1,
    )


def bcast_a2a(values, axis, count):
    spread = jnp.broadcast_to(values[None], (count,) + values.shape)
    return lax.all_to_all(spread, axis, 0, 0, tiled=True).reshape(
        (count * values.shape[0],) + values.shape[1:]
    )


def per_device(
    tokens_in,
    attn_norm,
    qkv_weight,
    qkv_bias,
    out_weight,
    cache_keys,
    cache_values,
    page_table,
    cache_lengths,
    mlp_norm,
    routes,
    route_gates,
    expert_w_gate,
    expert_w_up,
    expert_w_down,
    shared_w_gate,
    shared_w_up,
    shared_w_down,
    shared_switch,
):
    req_rows, step_count, model_width = tokens_in.shape
    head_width = qkv_weight.shape[2]
    local_heads = head_width // HD
    req_count = lax.axis_size("req")
    tp_count = lax.axis_size("tp")
    req_index = lax.axis_index("req")
    tp_index = lax.axis_index("tp")
    all_requests = page_table.shape[0]
    pool_here = cache_keys.shape[0]
    page_len = cache_keys.shape[1]
    score_scale = 1.0 / math.sqrt(HD)
    col_share = model_width // tp_count
    row_count = req_rows * step_count
    normed = rms_norm(tokens_in, attn_norm)
    projected = jnp.einsum(
        "rsd,dcf->rscf", normed, qkv_weight, preferred_element_type=jnp.float32
    ) + qkv_bias.astype(jnp.float32)
    own_lengths = lax.dynamic_slice_in_dim(cache_lengths, req_index * req_rows, req_rows)
    positions = own_lengths[:, None] + jnp.arange(step_count, dtype=jnp.int32)[None, :]
    head_shape = (req_rows, step_count, local_heads, HD)
    query_new = rotate(projected[:, :, 0].reshape(head_shape), positions).astype(jnp.bfloat16)
    key_new = rotate(projected[:, :, 1].reshape(head_shape), positions).astype(jnp.bfloat16)
    value_new = projected[:, :, 2].reshape(head_shape).astype(jnp.bfloat16)
    query_all = bcast_a2a(query_new, "req", req_count)
    slot_ids = req_index * pool_here + jnp.arange(pool_here, dtype=jnp.int32)
    matches = (page_table[:, :, None] == slot_ids[None, None, :]).astype(jnp.int32)
    request_ids = jnp.arange(all_requests, dtype=jnp.int32)
    page_ids = jnp.arange(page_table.shape[1], dtype=jnp.int32)
    owner = jnp.sum(matches * request_ids[:, None, None], axis=(0, 1))
    logical = jnp.sum(matches * page_ids[None, :, None], axis=(0, 1))
    present = jnp.sum(matches, axis=(0, 1)) > 0
    token_pos = logical[:, None] * page_len + jnp.arange(page_len, dtype=jnp.int32)[None, :]
    live = present[:, None] & (token_pos < cache_lengths[owner][:, None])
    page_queries = query_all[owner]
    page_keys = cache_keys.reshape(pool_here, page_len, local_heads, HD)
    page_values = cache_values.reshape(pool_here, page_len, local_heads, HD)
    scores = (
        jnp.einsum("pshd,pkhd->pshk", page_queries, page_keys, preferred_element_type=jnp.float32)
        * score_scale
    )
    page_mask = live[:, None, None, :]
    masked = jnp.where(page_mask, scores, NEG)
    page_max = jnp.max(masked, axis=-1)
    weights = jnp.where(page_mask, jnp.exp(masked - page_max[..., None]), 0.0)
    page_sum = jnp.sum(weights, axis=-1)
    page_out = jnp.einsum(
        "pshk,pkhd->pshd",
        weights.astype(jnp.bfloat16),
        page_values,
        preferred_element_type=jnp.float32,
    )
    belongs = (owner[None, :] == request_ids[:, None]) & present[None, :]
    owned = belongs[:, :, None, None]
    local_max = jnp.max(jnp.where(owned, page_max[None], NEG), axis=1)
    factors = jnp.where(owned, jnp.exp(page_max[None] - local_max[:, None]), 0.0)
    local_out = jnp.einsum("rpsh,pshd->rshd", factors, page_out, precision=HIGHEST)
    local_sum = jnp.einsum("rpsh,psh->rsh", factors, page_sum, precision=HIGHEST)
    stat_width = step_count * local_heads
    stat_row = jnp.concatenate(
        [
            local_max.reshape(all_requests, stat_width),
            local_sum.reshape(all_requests, stat_width),
            jnp.zeros((all_requests, HD - 2 * stat_width), jnp.float32),
        ],
        axis=1,
    )
    packed = jnp.concatenate(
        [local_out.reshape(all_requests, stat_width, HD), stat_row[:, None, :]], axis=1
    )
    gathered = lax.all_to_all(packed, "req", 0, 0, tiled=True).reshape(
        req_count, req_rows, stat_width + 1, HD
    )
    part_out = gathered[:, :, :stat_width, :]
    part_max = gathered[:, :, stat_width, :stat_width]
    part_sum = gathered[:, :, stat_width, stat_width : 2 * stat_width]
    cache_max = jnp.max(part_max, axis=0)
    rescale = jnp.exp(part_max - cache_max[None])
    cache_out = jnp.sum(part_out * rescale[..., None], axis=0).reshape(
        req_rows, step_count, local_heads, HD
    )
    cache_sum = jnp.sum(part_sum * rescale, axis=0).reshape(req_rows, step_count, local_heads)
    cache_max = cache_max.reshape(req_rows, step_count, local_heads)
    new_scores = (
        jnp.einsum("rshd,rthd->rsht", query_new, key_new, preferred_element_type=jnp.float32)
        * score_scale
    )
    causal = jnp.arange(step_count)[:, None] >= jnp.arange(step_count)[None, :]
    new_mask = causal[None, :, None, :]
    new_masked = jnp.where(new_mask, new_scores, NEG)
    new_max = jnp.max(new_masked, axis=-1)
    new_weights = jnp.where(new_mask, jnp.exp(new_masked - new_max[..., None]), 0.0)
    new_sum = jnp.sum(new_weights, axis=-1)
    new_out = jnp.einsum(
        "rsht,rthd->rshd",
        new_weights.astype(jnp.bfloat16),
        value_new,
        preferred_element_type=jnp.float32,
    )
    top_max = jnp.maximum(cache_max, new_max)
    cache_factor = jnp.exp(cache_max - top_max)
    new_factor = jnp.exp(new_max - top_max)
    attended = (cache_out * cache_factor[..., None] + new_out * new_factor[..., None]) / (
        cache_sum * cache_factor + new_sum * new_factor
    )[..., None]
    attended = attended.astype(jnp.bfloat16).reshape(row_count, head_width)
    attn_part = jnp.dot(attended, out_weight, preferred_element_type=jnp.float32)
    attn_full = jnp.sum(bcast_a2a(attn_part, "tp", tp_count).reshape(tp_count, row_count, model_width), axis=0)
    resid = tokens_in.reshape(row_count, model_width).astype(jnp.float32) + attn_full
    mixed = rms_norm(resid, mlp_norm)
    expert_count = req_count * expert_w_gate.shape[0]
    capacity = max(2, (row_count * TOPK + expert_count - 1) // expert_count)
    picks = routes.reshape(row_count * TOPK)
    gates_flat = route_gates.reshape(row_count * TOPK)
    expert_hot = (picks[:, None] == jnp.arange(expert_count, dtype=jnp.int32)[None, :]).astype(
        jnp.int32
    )
    slot_index = jnp.sum((jnp.cumsum(expert_hot, axis=0) - 1) * expert_hot, axis=1)
    destination = picks * capacity + slot_index
    dest_hot = (
        destination[:, None] == jnp.arange(expert_count * capacity, dtype=jnp.int32)[None, :]
    ).astype(jnp.float32)
    token_hot = (
        (jnp.arange(row_count * TOPK, dtype=jnp.int32) // TOPK)[:, None]
        == jnp.arange(row_count, dtype=jnp.int32)[None, :]
    ).astype(jnp.float32)
    placement = jnp.einsum("cx,ct->xt", dest_hot, token_hot, precision=HIGHEST).astype(jnp.bfloat16)
    outgoing = jnp.dot(placement, mixed, preferred_element_type=jnp.float32).astype(jnp.bfloat16)
    combine_map = jnp.einsum(
        "ct,cx->tx", token_hot, dest_hot * gates_flat[:, None], precision=HIGHEST
    )
    w_gate_here = expert_w_gate[0]
    w_up_here = expert_w_up[0]
    w_down_here = expert_w_down[0]
    mixed_cols = lax.dynamic_slice_in_dim(mixed, tp_index * col_share, col_share, 1)
    shared_send = jnp.broadcast_to(mixed_cols[None], (req_count, row_count, col_share))
    dispatch = jnp.concatenate(
        [
            outgoing.reshape(req_count, capacity * model_width),
            shared_send.reshape(req_count, row_count * col_share),
        ],
        axis=1,
    )
    received = lax.all_to_all(dispatch, "req", 0, 0, tiled=True)
    item_count = capacity
    flat_rows = received[:, : capacity * model_width].reshape(req_count * capacity, model_width)
    piece = received[:, capacity * model_width :].reshape(req_count * row_count, col_share)
    gate_pre = jnp.dot(flat_rows, w_gate_here, preferred_element_type=jnp.float32)
    up_pre = jnp.dot(flat_rows, w_up_here, preferred_element_type=jnp.float32)
    hidden = (jax.nn.silu(gate_pre) * up_pre).astype(jnp.bfloat16)
    partial_out = jnp.dot(hidden, w_down_here, preferred_element_type=jnp.float32)
    expert_rows = req_count * capacity
    partial_split = partial_out.reshape(expert_rows, tp_count, col_share).transpose(1, 0, 2)
    gate_part = jnp.dot(piece, shared_w_gate, preferred_element_type=jnp.float32)
    up_part = jnp.dot(piece, shared_w_up, preferred_element_type=jnp.float32)
    unit_count = shared_w_gate.shape[1]
    all_rows = req_count * row_count
    share_rows = all_rows // tp_count
    shared_pre = jnp.concatenate([gate_part, up_part], axis=1).reshape(
        tp_count, share_rows * 2 * unit_count
    )
    reduce_in = jnp.concatenate(
        [partial_split.reshape(tp_count, expert_rows * col_share), shared_pre], axis=1
    )
    reduce_out = jnp.sum(lax.all_to_all(reduce_in, "tp", 0, 0, tiled=True), axis=0)
    expert_sum = reduce_out[: expert_rows * col_share].reshape(expert_rows, col_share)
    shared_sum = reduce_out[expert_rows * col_share :].reshape(share_rows, 2 * unit_count)
    shared_hidden = (jax.nn.silu(shared_sum[:, :unit_count]) * shared_sum[:, unit_count:]).astype(
        jnp.bfloat16
    )
    hidden_all = bcast_a2a(shared_hidden, "tp", tp_count).reshape(all_rows, unit_count)
    shared_down = jnp.dot(hidden_all, shared_w_down, preferred_element_type=jnp.float32)
    ey = expert_sum.astype(jnp.bfloat16).astype(jnp.float32)
    back_in = jnp.concatenate(
        [
            ey.reshape(req_count, capacity * col_share),
            shared_down.reshape(req_count, row_count * col_share),
        ],
        axis=1,
    )
    back = lax.all_to_all(back_in, "req", 0, 0, tiled=True)
    returned = back[:, : capacity * col_share].reshape(expert_count * capacity, col_share)
    shared_mine = jnp.sum(
        back[:, capacity * col_share :].reshape(req_count, row_count, col_share), axis=0
    )
    moe_out = jnp.dot(combine_map, returned, precision=HIGHEST)
    switch = jax.nn.sigmoid(jnp.dot(mixed, shared_switch, preferred_element_type=jnp.float32))
    resid_mine = lax.dynamic_slice_in_dim(resid, tp_index * col_share, col_share, 1)
    final = resid_mine + moe_out + switch[:, None] * shared_mine
    return final.astype(jnp.bfloat16).reshape(req_rows, step_count, col_share)


def solution(mesh):
    return jax.shard_map(
        per_device,
        mesh=mesh,
        in_specs=(
            P("req", None, None),
            P(),
            P(None, None, "tp"),
            P(None, "tp"),
            P("tp", None),
            P("req", None, "tp"),
            P("req", None, "tp"),
            P(),
            P(),
            P(),
            P("req", None, None),
            P("req", None, None),
            P("req", None, "tp"),
            P("req", None, "tp"),
            P("req", "tp", None),
            P("tp", "req"),
            P("tp", "req"),
            P("req", "tp"),
            P(),
        ),
        out_specs=P("req", None, "tp"),
        check_vma=False,
    )
```

```python
import math

import jax
import jax.numpy as jnp
from jax import lax
from jax.sharding import PartitionSpec as P

HD = 128
TOPK = 4


NEG = -1e30
EPS = 1e-06
THETA = 1000000.0
HIGHEST = lax.Precision.HIGHEST


def rms_norm(inputs, gain_vector):
    values = inputs.astype(jnp.float32)
    scaled = values * lax.rsqrt(jnp.mean(values * values, axis=-1, keepdims=True) + EPS)
    return (scaled * gain_vector.astype(jnp.float32)).astype(jnp.bfloat16)


def rotate(values, positions):
    half_dim = values.shape[-1] // 2
    exponents = jnp.arange(half_dim, dtype=jnp.float32) * (2.0 / values.shape[-1])
    frequency = jnp.power(THETA, -exponents)
    angles = positions.astype(jnp.float32)[..., None, None] * frequency
    cosines = jnp.cos(angles)
    sine_part = jnp.sin(angles)
    front_half = values[..., :half_dim]
    back_half = values[..., half_dim:]
    return jnp.concatenate(
        [
            front_half * cosines - back_half * sine_part,
            back_half * cosines + front_half * sine_part,
        ],
        axis=-1,
    )


def bcast_a2a(values, axis, count):
    spread = jnp.broadcast_to(values[None], (count,) + values.shape)
    return lax.all_to_all(spread, axis, 0, 0, tiled=True).reshape(
        (count * values.shape[0],) + values.shape[1:]
    )


def per_device(
    tokens_in,
    attn_norm,
    qkv_weight,
    qkv_bias,
    out_weight,
    cache_keys,
    cache_values,
    page_table,
    cache_lengths,
    mlp_norm,
    routes,
    route_gates,
    expert_w_gate,
    expert_w_up,
    expert_w_down,
    shared_w_gate,
    shared_w_up,
    shared_w_down,
    shared_switch,
):
    req_rows, step_count, model_width = tokens_in.shape
    head_width = qkv_weight.shape[2]
    local_heads = head_width // HD
    req_count = lax.axis_size("req")
    tp_count = lax.axis_size("tp")
    req_index = lax.axis_index("req")
    tp_index = lax.axis_index("tp")
    all_requests = page_table.shape[0]
    pool_here = cache_keys.shape[0]
    page_len = cache_keys.shape[1]
    score_scale = 1.0 / math.sqrt(HD)
    col_share = model_width // tp_count
    row_count = req_rows * step_count
    normed = rms_norm(tokens_in, attn_norm)
    projected = jnp.einsum(
        "rsd,dcf->rscf", normed, qkv_weight, preferred_element_type=jnp.float32
    ) + qkv_bias.astype(jnp.float32)
    own_lengths = lax.dynamic_slice_in_dim(cache_lengths, req_index * req_rows, req_rows)
    positions = own_lengths[:, None] + jnp.arange(step_count, dtype=jnp.int32)[None, :]
    head_shape = (req_rows, step_count, local_heads, HD)
    query_new = rotate(projected[:, :, 0].reshape(head_shape), positions).astype(jnp.bfloat16)
    key_new = rotate(projected[:, :, 1].reshape(head_shape), positions).astype(jnp.bfloat16)
    value_new = projected[:, :, 2].reshape(head_shape).astype(jnp.bfloat16)
    query_all = bcast_a2a(query_new, "req", req_count)
    slot_ids = req_index * pool_here + jnp.arange(pool_here, dtype=jnp.int32)
    matches = (page_table[:, :, None] == slot_ids[None, None, :]).astype(jnp.int32)
    request_ids = jnp.arange(all_requests, dtype=jnp.int32)
    page_ids = jnp.arange(page_table.shape[1], dtype=jnp.int32)
    owner = jnp.sum(matches * request_ids[:, None, None], axis=(0, 1))
    logical = jnp.sum(matches * page_ids[None, :, None], axis=(0, 1))
    present = jnp.sum(matches, axis=(0, 1)) > 0
    token_pos = logical[:, None] * page_len + jnp.arange(page_len, dtype=jnp.int32)[None, :]
    live = present[:, None] & (token_pos < cache_lengths[owner][:, None])
    page_queries = query_all[owner]
    page_keys = cache_keys.reshape(pool_here, page_len, local_heads, HD)
    page_values = cache_values.reshape(pool_here, page_len, local_heads, HD)
    scores = (
        jnp.einsum("pshd,pkhd->pshk", page_queries, page_keys, preferred_element_type=jnp.float32)
        * score_scale
    )
    page_mask = live[:, None, None, :]
    masked = jnp.where(page_mask, scores, NEG)
    page_max = jnp.max(masked, axis=-1)
    weights = jnp.where(page_mask, jnp.exp(masked - page_max[..., None]), 0.0)
    page_sum = jnp.sum(weights, axis=-1)
    page_out = jnp.einsum(
        "pshk,pkhd->pshd",
        weights.astype(jnp.bfloat16),
        page_values,
        preferred_element_type=jnp.float32,
    )
    belongs = (owner[None, :] == request_ids[:, None]) & present[None, :]
    owned = belongs[:, :, None, None]
    local_max = jnp.max(jnp.where(owned, page_max[None], NEG), axis=1)
    factors = jnp.where(owned, jnp.exp(page_max[None] - local_max[:, None]), 0.0)
    local_out = jnp.einsum("rpsh,pshd->rshd", factors, page_out, precision=HIGHEST)
    local_sum = jnp.einsum("rpsh,psh->rsh", factors, page_sum, precision=HIGHEST)
    stat_width = step_count * local_heads
    stat_row = jnp.concatenate(
        [
            local_max.reshape(all_requests, stat_width),
            local_sum.reshape(all_requests, stat_width),
            jnp.zeros((all_requests, HD - 2 * stat_width), jnp.float32),
        ],
        axis=1,
    )
    packed = jnp.concatenate(
        [local_out.reshape(all_requests, stat_width, HD), stat_row[:, None, :]], axis=1
    )
    gathered = lax.all_to_all(packed, "req", 0, 0, tiled=True).reshape(
        req_count, req_rows, stat_width + 1, HD
    )
    part_out = gathered[:, :, :stat_width, :]
    part_max = gathered[:, :, stat_width, :stat_width]
    part_sum = gathered[:, :, stat_width, stat_width : 2 * stat_width]
    cache_max = jnp.max(part_max, axis=0)
    rescale = jnp.exp(part_max - cache_max[None])
    cache_out = jnp.sum(part_out * rescale[..., None], axis=0).reshape(
        req_rows, step_count, local_heads, HD
    )
    cache_sum = jnp.sum(part_sum * rescale, axis=0).reshape(req_rows, step_count, local_heads)
    cache_max = cache_max.reshape(req_rows, step_count, local_heads)
    new_scores = (
        jnp.einsum("rshd,rthd->rsht", query_new, key_new, preferred_element_type=jnp.float32)
        * score_scale
    )
    causal = jnp.arange(step_count)[:, None] >= jnp.arange(step_count)[None, :]
    new_mask = causal[None, :, None, :]
    new_masked = jnp.where(new_mask, new_scores, NEG)
    new_max = jnp.max(new_masked, axis=-1)
    new_weights = jnp.where(new_mask, jnp.exp(new_masked - new_max[..., None]), 0.0)
    new_sum = jnp.sum(new_weights, axis=-1)
    new_out = jnp.einsum(
        "rsht,rthd->rshd",
        new_weights.astype(jnp.bfloat16),
        value_new,
        preferred_element_type=jnp.float32,
    )
    top_max = jnp.maximum(cache_max, new_max)
    cache_factor = jnp.exp(cache_max - top_max)
    new_factor = jnp.exp(new_max - top_max)
    attended = (cache_out * cache_factor[..., None] + new_out * new_factor[..., None]) / (
        cache_sum * cache_factor + new_sum * new_factor
    )[..., None]
    attended = attended.astype(jnp.bfloat16).reshape(row_count, head_width)
    attn_part = jnp.dot(attended, out_weight, preferred_element_type=jnp.float32)
    attn_full = jnp.sum(bcast_a2a(attn_part, "tp", tp_count).reshape(tp_count, row_count, model_width), axis=0)
    resid = tokens_in.reshape(row_count, model_width).astype(jnp.float32) + attn_full
    mixed = rms_norm(resid, mlp_norm)
    expert_count = req_count * expert_w_gate.shape[0]
    capacity = max(2, (row_count * TOPK + expert_count - 1) // expert_count)
    picks = routes.reshape(row_count * TOPK)
    gates_flat = route_gates.reshape(row_count * TOPK)
    expert_hot = (picks[:, None] == jnp.arange(expert_count, dtype=jnp.int32)[None, :]).astype(
        jnp.int32
    )
    slot_index = jnp.sum((jnp.cumsum(expert_hot, axis=0) - 1) * expert_hot, axis=1)
    destination = picks * capacity + slot_index
    dest_hot = (
        destination[:, None] == jnp.arange(expert_count * capacity, dtype=jnp.int32)[None, :]
    ).astype(jnp.float32)
    token_hot = (
        (jnp.arange(row_count * TOPK, dtype=jnp.int32) // TOPK)[:, None]
        == jnp.arange(row_count, dtype=jnp.int32)[None, :]
    ).astype(jnp.float32)
    placement = jnp.einsum("cx,ct->xt", dest_hot, token_hot, precision=HIGHEST).astype(jnp.bfloat16)
    outgoing = jnp.dot(placement, mixed, preferred_element_type=jnp.float32).astype(jnp.bfloat16)
    combine_map = jnp.einsum(
        "ct,cx->tx", token_hot, dest_hot * gates_flat[:, None], precision=HIGHEST
    )
    w_gate_here = expert_w_gate[0]
    w_up_here = expert_w_up[0]
    w_down_here = expert_w_down[0]
    mixed_cols = lax.dynamic_slice_in_dim(mixed, tp_index * col_share, col_share, 1)
    shared_send = jnp.broadcast_to(mixed_cols[None], (req_count, row_count, col_share))
    dispatch = jnp.concatenate(
        [
            outgoing.reshape(req_count, capacity * model_width),
            shared_send.reshape(req_count, row_count * col_share),
        ],
        axis=1,
    )
    received = lax.all_to_all(dispatch, "req", 0, 0, tiled=True)
    item_count = capacity
    flat_rows = received[:, : capacity * model_width].reshape(req_count * capacity, model_width)
    piece = received[:, capacity * model_width :].reshape(req_count * row_count, col_share)
    gate_pre = jnp.dot(flat_rows, w_gate_here, preferred_element_type=jnp.float32)
    up_pre = jnp.dot(flat_rows, w_up_here, preferred_element_type=jnp.float32)
    hidden = (jax.nn.silu(gate_pre) * up_pre).astype(jnp.bfloat16)
    partial_out = jnp.dot(hidden, w_down_here, preferred_element_type=jnp.float32)
    expert_rows = req_count * capacity
    partial_split = partial_out.reshape(expert_rows, tp_count, col_share).transpose(1, 0, 2)
    gate_part = jnp.dot(piece, shared_w_gate, preferred_element_type=jnp.float32)
    up_part = jnp.dot(piece, shared_w_up, preferred_element_type=jnp.float32)
    unit_count = shared_w_gate.shape[1]
    all_rows = req_count * row_count
    expert_high = partial_split.astype(jnp.bfloat16)
    expert_low = (partial_split - expert_high.astype(jnp.float32)).astype(jnp.bfloat16)
    shared_pre = jnp.concatenate([gate_part, up_part], axis=1).astype(jnp.bfloat16)
    reduce_in = jnp.concatenate(
        [
            expert_high.reshape(tp_count, expert_rows * col_share),
            expert_low.reshape(tp_count, expert_rows * col_share),
            jnp.broadcast_to(
                shared_pre.reshape(1, all_rows * 2 * unit_count),
                (tp_count, all_rows * 2 * unit_count),
            ),
        ],
        axis=1,
    )
    reduce_out = lax.all_to_all(reduce_in, "tp", 0, 0, tiled=True).astype(jnp.float32)
    expert_part = expert_rows * col_share
    expert_sum = jnp.sum(
        reduce_out[:, :expert_part] + reduce_out[:, expert_part : 2 * expert_part], axis=0
    ).reshape(expert_rows, col_share)
    shared_sum = jnp.sum(reduce_out[:, 2 * expert_part :], axis=0).reshape(all_rows, 2 * unit_count)
    hidden_all = (jax.nn.silu(shared_sum[:, :unit_count]) * shared_sum[:, unit_count:]).astype(
        jnp.bfloat16
    )
    shared_down = jnp.dot(hidden_all, shared_w_down, preferred_element_type=jnp.float32)
    ey = expert_sum.astype(jnp.bfloat16).astype(jnp.float32)
    back_in = jnp.concatenate(
        [
            ey.reshape(req_count, capacity * col_share),
            shared_down.reshape(req_count, row_count * col_share),
        ],
        axis=1,
    )
    back = lax.all_to_all(back_in, "req", 0, 0, tiled=True)
    returned = back[:, : capacity * col_share].reshape(expert_count * capacity, col_share)
    shared_mine = jnp.sum(
        back[:, capacity * col_share :].reshape(req_count, row_count, col_share), axis=0
    )
    moe_out = jnp.dot(combine_map, returned, precision=HIGHEST)
    switch = jax.nn.sigmoid(jnp.dot(mixed, shared_switch, preferred_element_type=jnp.float32))
    resid_mine = lax.dynamic_slice_in_dim(resid, tp_index * col_share, col_share, 1)
    final = resid_mine + moe_out + switch[:, None] * shared_mine
    return final.astype(jnp.bfloat16).reshape(req_rows, step_count, col_share)


def solution(mesh):
    return jax.shard_map(
        per_device,
        mesh=mesh,
        in_specs=(
            P("req", None, None),
            P(),
            P(None, None, "tp"),
            P(None, "tp"),
            P("tp", None),
            P("req", None, "tp"),
            P("req", None, "tp"),
            P(),
            P(),
            P(),
            P("req", None, None),
            P("req", None, None),
            P("req", None, "tp"),
            P("req", None, "tp"),
            P("req", "tp", None),
            P("tp", "req"),
            P("tp", "req"),
            P("req", "tp"),
            P(),
        ),
        out_specs=P("req", None, "tp"),
        check_vma=False,
    )
```

```python
import math

import jax
import jax.numpy as jnp
from jax import lax
from jax.sharding import PartitionSpec as P

HD = 128
TOPK = 4


NEG = -1e30
EPS = 1e-06
THETA = 1000000.0
HIGHEST = lax.Precision.HIGHEST


def rms_norm(inputs, gain_vector):
    values = inputs.astype(jnp.float32)
    scaled = values * lax.rsqrt(jnp.mean(values * values, axis=-1, keepdims=True) + EPS)
    return (scaled * gain_vector.astype(jnp.float32)).astype(jnp.bfloat16)


def rotate(values, positions):
    half_dim = values.shape[-1] // 2
    exponents = jnp.arange(half_dim, dtype=jnp.float32) * (2.0 / values.shape[-1])
    frequency = jnp.power(THETA, -exponents)
    angles = positions.astype(jnp.float32)[..., None, None] * frequency
    cosines = jnp.cos(angles)
    sine_part = jnp.sin(angles)
    front_half = values[..., :half_dim]
    back_half = values[..., half_dim:]
    return jnp.concatenate(
        [
            front_half * cosines - back_half * sine_part,
            back_half * cosines + front_half * sine_part,
        ],
        axis=-1,
    )


def bcast_a2a(values, axis, count):
    spread = jnp.broadcast_to(values[None], (count,) + values.shape)
    return lax.all_to_all(spread, axis, 0, 0, tiled=True).reshape(
        (count * values.shape[0],) + values.shape[1:]
    )


def per_device(
    tokens_in,
    attn_norm,
    qkv_weight,
    qkv_bias,
    out_weight,
    cache_keys,
    cache_values,
    page_table,
    cache_lengths,
    mlp_norm,
    routes,
    route_gates,
    expert_w_gate,
    expert_w_up,
    expert_w_down,
    shared_w_gate,
    shared_w_up,
    shared_w_down,
    shared_switch,
):
    req_rows, step_count, model_width = tokens_in.shape
    head_width = qkv_weight.shape[2]
    local_heads = head_width // HD
    req_count = lax.axis_size("req")
    tp_count = lax.axis_size("tp")
    req_index = lax.axis_index("req")
    tp_index = lax.axis_index("tp")
    all_requests = page_table.shape[0]
    pool_here = cache_keys.shape[0]
    page_len = cache_keys.shape[1]
    score_scale = 1.0 / math.sqrt(HD)
    col_share = model_width // tp_count
    row_count = req_rows * step_count
    normed = rms_norm(tokens_in, attn_norm)
    own_lengths = lax.dynamic_slice_in_dim(cache_lengths, req_index * req_rows, req_rows)
    positions = own_lengths[:, None] + jnp.arange(step_count, dtype=jnp.int32)[None, :]
    head_shape = (req_rows, step_count, local_heads, HD)

    def project(part, rows):
        return jnp.einsum(
            "rsd,df->rsf", rows, qkv_weight[:, part], preferred_element_type=jnp.float32
        ) + qkv_bias[part].astype(jnp.float32)

    query_new = rotate(project(0, normed).reshape(head_shape), positions).astype(jnp.bfloat16)
    query_spread = jnp.broadcast_to(query_new[None], (req_count,) + query_new.shape)
    normed_late, query_spread = lax.optimization_barrier((normed, query_spread))
    query_all = lax.all_to_all(query_spread, "req", 0, 0, tiled=True).reshape(
        (req_count * req_rows,) + query_new.shape[1:]
    )
    key_new = rotate(project(1, normed_late).reshape(head_shape), positions).astype(jnp.bfloat16)
    value_new = project(2, normed_late).reshape(head_shape).astype(jnp.bfloat16)
    slot_ids = req_index * pool_here + jnp.arange(pool_here, dtype=jnp.int32)
    matches = (page_table[:, :, None] == slot_ids[None, None, :]).astype(jnp.int32)
    request_ids = jnp.arange(all_requests, dtype=jnp.int32)
    page_ids = jnp.arange(page_table.shape[1], dtype=jnp.int32)
    owner = jnp.sum(matches * request_ids[:, None, None], axis=(0, 1))
    logical = jnp.sum(matches * page_ids[None, :, None], axis=(0, 1))
    present = jnp.sum(matches, axis=(0, 1)) > 0
    token_pos = logical[:, None] * page_len + jnp.arange(page_len, dtype=jnp.int32)[None, :]
    live = present[:, None] & (token_pos < cache_lengths[owner][:, None])
    page_queries = query_all[owner]
    page_keys = cache_keys.reshape(pool_here, page_len, local_heads, HD)
    page_values = cache_values.reshape(pool_here, page_len, local_heads, HD)
    scores = (
        jnp.einsum("pshd,pkhd->pshk", page_queries, page_keys, preferred_element_type=jnp.float32)
        * score_scale
    )
    page_mask = live[:, None, None, :]
    masked = jnp.where(page_mask, scores, NEG)
    page_max = jnp.max(masked, axis=-1)
    weights = jnp.where(page_mask, jnp.exp(masked - page_max[..., None]), 0.0)
    page_sum = jnp.sum(weights, axis=-1)
    page_out = jnp.einsum(
        "pshk,pkhd->pshd",
        weights.astype(jnp.bfloat16),
        page_values,
        preferred_element_type=jnp.float32,
    )
    belongs = (owner[None, :] == request_ids[:, None]) & present[None, :]
    owned = belongs[:, :, None, None]
    local_max = jnp.max(jnp.where(owned, page_max[None], NEG), axis=1)
    factors = jnp.where(owned, jnp.exp(page_max[None] - local_max[:, None]), 0.0)
    local_out = jnp.einsum("rpsh,pshd->rshd", factors, page_out, precision=HIGHEST)
    local_sum = jnp.einsum("rpsh,psh->rsh", factors, page_sum, precision=HIGHEST)
    stat_width = step_count * local_heads
    stat_row = jnp.concatenate(
        [
            local_max.reshape(all_requests, stat_width),
            local_sum.reshape(all_requests, stat_width),
            jnp.zeros((all_requests, HD - 2 * stat_width), jnp.float32),
        ],
        axis=1,
    )
    packed = jnp.concatenate(
        [local_out.reshape(all_requests, stat_width, HD), stat_row[:, None, :]], axis=1
    )
    gathered = lax.all_to_all(packed, "req", 0, 0, tiled=True).reshape(
        req_count, req_rows, stat_width + 1, HD
    )
    part_out = gathered[:, :, :stat_width, :]
    part_max = gathered[:, :, stat_width, :stat_width]
    part_sum = gathered[:, :, stat_width, stat_width : 2 * stat_width]
    cache_max = jnp.max(part_max, axis=0)
    rescale = jnp.exp(part_max - cache_max[None])
    cache_out = jnp.sum(part_out * rescale[..., None], axis=0).reshape(
        req_rows, step_count, local_heads, HD
    )
    cache_sum = jnp.sum(part_sum * rescale, axis=0).reshape(req_rows, step_count, local_heads)
    cache_max = cache_max.reshape(req_rows, step_count, local_heads)
    new_scores = (
        jnp.einsum("rshd,rthd->rsht", query_new, key_new, preferred_element_type=jnp.float32)
        * score_scale
    )
    causal = jnp.arange(step_count)[:, None] >= jnp.arange(step_count)[None, :]
    new_mask = causal[None, :, None, :]
    new_masked = jnp.where(new_mask, new_scores, NEG)
    new_max = jnp.max(new_masked, axis=-1)
    new_weights = jnp.where(new_mask, jnp.exp(new_masked - new_max[..., None]), 0.0)
    new_sum = jnp.sum(new_weights, axis=-1)
    new_out = jnp.einsum(
        "rsht,rthd->rshd",
        new_weights.astype(jnp.bfloat16),
        value_new,
        preferred_element_type=jnp.float32,
    )
    top_max = jnp.maximum(cache_max, new_max)
    cache_factor = jnp.exp(cache_max - top_max)
    new_factor = jnp.exp(new_max - top_max)
    attended = (cache_out * cache_factor[..., None] + new_out * new_factor[..., None]) / (
        cache_sum * cache_factor + new_sum * new_factor
    )[..., None]
    attended = attended.astype(jnp.bfloat16).reshape(row_count, head_width)
    attn_part = jnp.dot(attended, out_weight, preferred_element_type=jnp.float32)
    attn_full = jnp.sum(bcast_a2a(attn_part, "tp", tp_count).reshape(tp_count, row_count, model_width), axis=0)
    resid = tokens_in.reshape(row_count, model_width).astype(jnp.float32) + attn_full
    mixed = rms_norm(resid, mlp_norm)
    expert_count = req_count * expert_w_gate.shape[0]
    capacity = max(2, (row_count * TOPK + expert_count - 1) // expert_count)
    picks = routes.reshape(row_count * TOPK)
    gates_flat = route_gates.reshape(row_count * TOPK)
    expert_hot = (picks[:, None] == jnp.arange(expert_count, dtype=jnp.int32)[None, :]).astype(
        jnp.int32
    )
    slot_index = jnp.sum((jnp.cumsum(expert_hot, axis=0) - 1) * expert_hot, axis=1)
    destination = picks * capacity + slot_index
    dest_hot = (
        destination[:, None] == jnp.arange(expert_count * capacity, dtype=jnp.int32)[None, :]
    ).astype(jnp.float32)
    token_hot = (
        (jnp.arange(row_count * TOPK, dtype=jnp.int32) // TOPK)[:, None]
        == jnp.arange(row_count, dtype=jnp.int32)[None, :]
    ).astype(jnp.float32)
    placement = jnp.einsum("cx,ct->xt", dest_hot, token_hot, precision=HIGHEST).astype(jnp.bfloat16)
    outgoing = jnp.dot(placement, mixed, preferred_element_type=jnp.float32).astype(jnp.bfloat16)
    combine_map = jnp.einsum(
        "ct,cx->tx", token_hot, dest_hot * gates_flat[:, None], precision=HIGHEST
    )
    w_gate_here = expert_w_gate[0]
    w_up_here = expert_w_up[0]
    w_down_here = expert_w_down[0]
    mixed_cols = lax.dynamic_slice_in_dim(mixed, tp_index * col_share, col_share, 1)
    shared_send = jnp.broadcast_to(mixed_cols[None], (req_count, row_count, col_share))
    dispatch = jnp.concatenate(
        [
            outgoing.reshape(req_count, capacity * model_width),
            shared_send.reshape(req_count, row_count * col_share),
        ],
        axis=1,
    )
    received = lax.all_to_all(dispatch, "req", 0, 0, tiled=True)
    item_count = capacity
    flat_rows = received[:, : capacity * model_width].reshape(req_count * capacity, model_width)
    piece = received[:, capacity * model_width :].reshape(req_count * row_count, col_share)
    gate_pre = jnp.dot(flat_rows, w_gate_here, preferred_element_type=jnp.float32)
    up_pre = jnp.dot(flat_rows, w_up_here, preferred_element_type=jnp.float32)
    hidden = (jax.nn.silu(gate_pre) * up_pre).astype(jnp.bfloat16)
    partial_out = jnp.dot(hidden, w_down_here, preferred_element_type=jnp.float32)
    expert_rows = req_count * capacity
    partial_split = partial_out.reshape(expert_rows, tp_count, col_share).transpose(1, 0, 2)
    gate_part = jnp.dot(piece, shared_w_gate, preferred_element_type=jnp.float32)
    up_part = jnp.dot(piece, shared_w_up, preferred_element_type=jnp.float32)
    unit_count = shared_w_gate.shape[1]
    all_rows = req_count * row_count
    share_rows = all_rows // tp_count
    shared_pre = jnp.concatenate([gate_part, up_part], axis=1).reshape(
        tp_count, share_rows * 2 * unit_count
    )
    reduce_in = jnp.concatenate(
        [partial_split.reshape(tp_count, expert_rows * col_share), shared_pre], axis=1
    )
    reduce_out = jnp.sum(lax.all_to_all(reduce_in, "tp", 0, 0, tiled=True), axis=0)
    expert_sum = reduce_out[: expert_rows * col_share].reshape(expert_rows, col_share)
    shared_sum = reduce_out[expert_rows * col_share :].reshape(share_rows, 2 * unit_count)
    shared_hidden = (jax.nn.silu(shared_sum[:, :unit_count]) * shared_sum[:, unit_count:]).astype(
        jnp.bfloat16
    )
    hidden_all = bcast_a2a(shared_hidden, "tp", tp_count).reshape(all_rows, unit_count)
    shared_down = jnp.dot(hidden_all, shared_w_down, preferred_element_type=jnp.float32)
    ey = expert_sum.astype(jnp.bfloat16).astype(jnp.float32)
    back_in = jnp.concatenate(
        [
            ey.reshape(req_count, capacity * col_share),
            shared_down.reshape(req_count, row_count * col_share),
        ],
        axis=1,
    )
    back = lax.all_to_all(back_in, "req", 0, 0, tiled=True)
    returned = back[:, : capacity * col_share].reshape(expert_count * capacity, col_share)
    shared_mine = jnp.sum(
        back[:, capacity * col_share :].reshape(req_count, row_count, col_share), axis=0
    )
    moe_out = jnp.dot(combine_map, returned, precision=HIGHEST)
    switch = jax.nn.sigmoid(jnp.dot(mixed, shared_switch, preferred_element_type=jnp.float32))
    resid_mine = lax.dynamic_slice_in_dim(resid, tp_index * col_share, col_share, 1)
    final = resid_mine + moe_out + switch[:, None] * shared_mine
    return final.astype(jnp.bfloat16).reshape(req_rows, step_count, col_share)


def solution(mesh):
    return jax.shard_map(
        per_device,
        mesh=mesh,
        in_specs=(
            P("req", None, None),
            P(),
            P(None, None, "tp"),
            P(None, "tp"),
            P("tp", None),
            P("req", None, "tp"),
            P("req", None, "tp"),
            P(),
            P(),
            P(),
            P("req", None, None),
            P("req", None, None),
            P("req", None, "tp"),
            P("req", None, "tp"),
            P("req", "tp", None),
            P("tp", "req"),
            P("tp", "req"),
            P("req", "tp"),
            P(),
        ),
        out_specs=P("req", None, "tp"),
        check_vma=False,
    )
```

```python
import math

import jax
import jax.numpy as jnp
from jax import lax
from jax.sharding import PartitionSpec as P

HD = 128
TOPK = 4


NEG = -1e30
EPS = 1e-06
THETA = 1000000.0
HIGHEST = lax.Precision.HIGHEST


def rms_norm(inputs, gain_vector):
    values = inputs.astype(jnp.float32)
    scaled = values * lax.rsqrt(jnp.mean(values * values, axis=-1, keepdims=True) + EPS)
    return (scaled * gain_vector.astype(jnp.float32)).astype(jnp.bfloat16)


def rotate(values, positions):
    half_dim = values.shape[-1] // 2
    exponents = jnp.arange(half_dim, dtype=jnp.float32) * (2.0 / values.shape[-1])
    frequency = jnp.power(THETA, -exponents)
    angles = positions.astype(jnp.float32)[..., None, None] * frequency
    cosines = jnp.cos(angles)
    sine_part = jnp.sin(angles)
    front_half = values[..., :half_dim]
    back_half = values[..., half_dim:]
    return jnp.concatenate(
        [
            front_half * cosines - back_half * sine_part,
            back_half * cosines + front_half * sine_part,
        ],
        axis=-1,
    )


def shift_exchange(chunks, axis, count, spread=False):
    me = lax.axis_index(axis)
    pieces = [chunks if spread else lax.dynamic_index_in_dim(chunks, me, 0, keepdims=False)]
    for shift in range(1, count):
        send = chunks if spread else lax.dynamic_index_in_dim(
            chunks, (me + shift) % count, 0, keepdims=False
        )
        pairs = [(source, (source + shift) % count) for source in range(count)]
        pieces.append(lax.ppermute(send, axis, pairs))
    return pieces


def by_source(pieces, axis, count):
    me = lax.axis_index(axis)
    stacked = jnp.stack(pieces)
    order = (me - jnp.arange(count, dtype=jnp.int32)) % count
    return jnp.take(stacked, order, axis=0)


def bcast_a2a(values, axis, count):
    spread = jnp.broadcast_to(values[None], (count,) + values.shape)
    return lax.all_to_all(spread, axis, 0, 0, tiled=True).reshape(
        (count * values.shape[0],) + values.shape[1:]
    )


def per_device(
    tokens_in,
    attn_norm,
    qkv_weight,
    qkv_bias,
    out_weight,
    cache_keys,
    cache_values,
    page_table,
    cache_lengths,
    mlp_norm,
    routes,
    route_gates,
    expert_w_gate,
    expert_w_up,
    expert_w_down,
    shared_w_gate,
    shared_w_up,
    shared_w_down,
    shared_switch,
):
    req_rows, step_count, model_width = tokens_in.shape
    head_width = qkv_weight.shape[2]
    local_heads = head_width // HD
    req_count = lax.axis_size("req")
    tp_count = lax.axis_size("tp")
    req_index = lax.axis_index("req")
    tp_index = lax.axis_index("tp")
    all_requests = page_table.shape[0]
    pool_here = cache_keys.shape[0]
    page_len = cache_keys.shape[1]
    score_scale = 1.0 / math.sqrt(HD)
    col_share = model_width // tp_count
    row_count = req_rows * step_count
    normed = rms_norm(tokens_in, attn_norm)
    own_lengths = lax.dynamic_slice_in_dim(cache_lengths, req_index * req_rows, req_rows)
    positions = own_lengths[:, None] + jnp.arange(step_count, dtype=jnp.int32)[None, :]
    head_shape = (req_rows, step_count, local_heads, HD)

    def project(part, rows):
        return jnp.einsum(
            "rsd,df->rsf", rows, qkv_weight[:, part], preferred_element_type=jnp.float32
        ) + qkv_bias[part].astype(jnp.float32)

    query_new = rotate(project(0, normed).reshape(head_shape), positions).astype(jnp.bfloat16)
    query_spread = jnp.broadcast_to(query_new[None], (req_count,) + query_new.shape)
    normed_late, query_spread = lax.optimization_barrier((normed, query_spread))
    query_all = lax.all_to_all(query_spread, "req", 0, 0, tiled=True).reshape(
        (req_count * req_rows,) + query_new.shape[1:]
    )
    key_new = rotate(project(1, normed_late).reshape(head_shape), positions).astype(jnp.bfloat16)
    value_new = project(2, normed_late).reshape(head_shape).astype(jnp.bfloat16)
    slot_ids = req_index * pool_here + jnp.arange(pool_here, dtype=jnp.int32)
    matches = (page_table[:, :, None] == slot_ids[None, None, :]).astype(jnp.int32)
    request_ids = jnp.arange(all_requests, dtype=jnp.int32)
    page_ids = jnp.arange(page_table.shape[1], dtype=jnp.int32)
    owner = jnp.sum(matches * request_ids[:, None, None], axis=(0, 1))
    logical = jnp.sum(matches * page_ids[None, :, None], axis=(0, 1))
    present = jnp.sum(matches, axis=(0, 1)) > 0
    token_pos = logical[:, None] * page_len + jnp.arange(page_len, dtype=jnp.int32)[None, :]
    live = present[:, None] & (token_pos < cache_lengths[owner][:, None])
    page_queries = query_all[owner]
    page_keys = cache_keys.reshape(pool_here, page_len, local_heads, HD)
    page_values = cache_values.reshape(pool_here, page_len, local_heads, HD)
    scores = (
        jnp.einsum("pshd,pkhd->pshk", page_queries, page_keys, preferred_element_type=jnp.float32)
        * score_scale
    )
    page_mask = live[:, None, None, :]
    masked = jnp.where(page_mask, scores, NEG)
    page_max = jnp.max(masked, axis=-1)
    weights = jnp.where(page_mask, jnp.exp(masked - page_max[..., None]), 0.0)
    page_sum = jnp.sum(weights, axis=-1)
    page_out = jnp.einsum(
        "pshk,pkhd->pshd",
        weights.astype(jnp.bfloat16),
        page_values,
        preferred_element_type=jnp.float32,
    )
    belongs = (owner[None, :] == request_ids[:, None]) & present[None, :]
    owned = belongs[:, :, None, None]
    local_max = jnp.max(jnp.where(owned, page_max[None], NEG), axis=1)
    factors = jnp.where(owned, jnp.exp(page_max[None] - local_max[:, None]), 0.0)
    local_out = jnp.einsum("rpsh,pshd->rshd", factors, page_out, precision=HIGHEST)
    local_sum = jnp.einsum("rpsh,psh->rsh", factors, page_sum, precision=HIGHEST)
    stat_width = step_count * local_heads
    stat_row = jnp.concatenate(
        [
            local_max.reshape(all_requests, stat_width),
            local_sum.reshape(all_requests, stat_width),
            jnp.zeros((all_requests, HD - 2 * stat_width), jnp.float32),
        ],
        axis=1,
    )
    packed = jnp.concatenate(
        [local_out.reshape(all_requests, stat_width, HD), stat_row[:, None, :]], axis=1
    )
    gathered = lax.all_to_all(packed, "req", 0, 0, tiled=True).reshape(
        req_count, req_rows, stat_width + 1, HD
    )
    part_out = gathered[:, :, :stat_width, :]
    part_max = gathered[:, :, stat_width, :stat_width]
    part_sum = gathered[:, :, stat_width, stat_width : 2 * stat_width]
    cache_max = jnp.max(part_max, axis=0)
    rescale = jnp.exp(part_max - cache_max[None])
    cache_out = jnp.sum(part_out * rescale[..., None], axis=0).reshape(
        req_rows, step_count, local_heads, HD
    )
    cache_sum = jnp.sum(part_sum * rescale, axis=0).reshape(req_rows, step_count, local_heads)
    cache_max = cache_max.reshape(req_rows, step_count, local_heads)
    new_scores = (
        jnp.einsum("rshd,rthd->rsht", query_new, key_new, preferred_element_type=jnp.float32)
        * score_scale
    )
    causal = jnp.arange(step_count)[:, None] >= jnp.arange(step_count)[None, :]
    new_mask = causal[None, :, None, :]
    new_masked = jnp.where(new_mask, new_scores, NEG)
    new_max = jnp.max(new_masked, axis=-1)
    new_weights = jnp.where(new_mask, jnp.exp(new_masked - new_max[..., None]), 0.0)
    new_sum = jnp.sum(new_weights, axis=-1)
    new_out = jnp.einsum(
        "rsht,rthd->rshd",
        new_weights.astype(jnp.bfloat16),
        value_new,
        preferred_element_type=jnp.float32,
    )
    top_max = jnp.maximum(cache_max, new_max)
    cache_factor = jnp.exp(cache_max - top_max)
    new_factor = jnp.exp(new_max - top_max)
    attended = (cache_out * cache_factor[..., None] + new_out * new_factor[..., None]) / (
        cache_sum * cache_factor + new_sum * new_factor
    )[..., None]
    attended = attended.astype(jnp.bfloat16).reshape(row_count, head_width)
    attn_part = jnp.dot(attended, out_weight, preferred_element_type=jnp.float32)
    attn_full = jnp.sum(
        by_source(shift_exchange(attn_part, "tp", tp_count, spread=True), "tp", tp_count), axis=0
    )
    resid = tokens_in.reshape(row_count, model_width).astype(jnp.float32) + attn_full
    mixed = rms_norm(resid, mlp_norm)
    expert_count = req_count * expert_w_gate.shape[0]
    capacity = max(2, (row_count * TOPK + expert_count - 1) // expert_count)
    picks = routes.reshape(row_count * TOPK)
    gates_flat = route_gates.reshape(row_count * TOPK)
    expert_hot = (picks[:, None] == jnp.arange(expert_count, dtype=jnp.int32)[None, :]).astype(
        jnp.int32
    )
    slot_index = jnp.sum((jnp.cumsum(expert_hot, axis=0) - 1) * expert_hot, axis=1)
    destination = picks * capacity + slot_index
    dest_hot = (
        destination[:, None] == jnp.arange(expert_count * capacity, dtype=jnp.int32)[None, :]
    ).astype(jnp.float32)
    token_hot = (
        (jnp.arange(row_count * TOPK, dtype=jnp.int32) // TOPK)[:, None]
        == jnp.arange(row_count, dtype=jnp.int32)[None, :]
    ).astype(jnp.float32)
    placement = jnp.einsum("cx,ct->xt", dest_hot, token_hot, precision=HIGHEST).astype(jnp.bfloat16)
    outgoing = jnp.dot(placement, mixed, preferred_element_type=jnp.float32).astype(jnp.bfloat16)
    combine_map = jnp.einsum(
        "ct,cx->tx", token_hot, dest_hot * gates_flat[:, None], precision=HIGHEST
    )
    w_gate_here = expert_w_gate[0]
    w_up_here = expert_w_up[0]
    w_down_here = expert_w_down[0]
    mixed_cols = lax.dynamic_slice_in_dim(mixed, tp_index * col_share, col_share, 1)
    shared_send = jnp.broadcast_to(mixed_cols[None], (req_count, row_count, col_share))
    dispatch = jnp.concatenate(
        [
            outgoing.reshape(req_count, capacity * model_width),
            shared_send.reshape(req_count, row_count * col_share),
        ],
        axis=1,
    )
    received = lax.all_to_all(dispatch, "req", 0, 0, tiled=True)
    item_count = capacity
    flat_rows = received[:, : capacity * model_width].reshape(req_count * capacity, model_width)
    piece = received[:, capacity * model_width :].reshape(req_count * row_count, col_share)
    gate_pre = jnp.dot(flat_rows, w_gate_here, preferred_element_type=jnp.float32)
    up_pre = jnp.dot(flat_rows, w_up_here, preferred_element_type=jnp.float32)
    hidden = (jax.nn.silu(gate_pre) * up_pre).astype(jnp.bfloat16)
    partial_out = jnp.dot(hidden, w_down_here, preferred_element_type=jnp.float32)
    expert_rows = req_count * capacity
    partial_split = partial_out.reshape(expert_rows, tp_count, col_share).transpose(1, 0, 2)
    gate_part = jnp.dot(piece, shared_w_gate, preferred_element_type=jnp.float32)
    up_part = jnp.dot(piece, shared_w_up, preferred_element_type=jnp.float32)
    unit_count = shared_w_gate.shape[1]
    all_rows = req_count * row_count
    share_rows = all_rows // tp_count
    shared_pre = jnp.concatenate([gate_part, up_part], axis=1).reshape(
        tp_count, share_rows * 2 * unit_count
    )
    reduce_in = jnp.concatenate(
        [partial_split.reshape(tp_count, expert_rows * col_share), shared_pre], axis=1
    )
    reduce_out = sum(shift_exchange(reduce_in, "tp", tp_count))
    expert_sum = reduce_out[: expert_rows * col_share].reshape(expert_rows, col_share)
    shared_sum = reduce_out[expert_rows * col_share :].reshape(share_rows, 2 * unit_count)
    shared_hidden = (jax.nn.silu(shared_sum[:, :unit_count]) * shared_sum[:, unit_count:]).astype(
        jnp.bfloat16
    )
    hidden_all = by_source(
        shift_exchange(shared_hidden, "tp", tp_count, spread=True), "tp", tp_count
    ).reshape(all_rows, unit_count)
    shared_down = jnp.dot(hidden_all, shared_w_down, preferred_element_type=jnp.float32)
    ey = expert_sum.astype(jnp.bfloat16).astype(jnp.float32)
    back_in = jnp.concatenate(
        [
            ey.reshape(req_count, capacity * col_share),
            shared_down.reshape(req_count, row_count * col_share),
        ],
        axis=1,
    )
    back = lax.all_to_all(back_in, "req", 0, 0, tiled=True)
    returned = back[:, : capacity * col_share].reshape(expert_count * capacity, col_share)
    shared_mine = jnp.sum(
        back[:, capacity * col_share :].reshape(req_count, row_count, col_share), axis=0
    )
    moe_out = jnp.dot(combine_map, returned, precision=HIGHEST)
    switch = jax.nn.sigmoid(jnp.dot(mixed, shared_switch, preferred_element_type=jnp.float32))
    resid_mine = lax.dynamic_slice_in_dim(resid, tp_index * col_share, col_share, 1)
    final = resid_mine + moe_out + switch[:, None] * shared_mine
    return final.astype(jnp.bfloat16).reshape(req_rows, step_count, col_share)


def solution(mesh):
    return jax.shard_map(
        per_device,
        mesh=mesh,
        in_specs=(
            P("req", None, None),
            P(),
            P(None, None, "tp"),
            P(None, "tp"),
            P("tp", None),
            P("req", None, "tp"),
            P("req", None, "tp"),
            P(),
            P(),
            P(),
            P("req", None, None),
            P("req", None, None),
            P("req", None, "tp"),
            P("req", None, "tp"),
            P("req", "tp", None),
            P("tp", "req"),
            P("tp", "req"),
            P("req", "tp"),
            P(),
        ),
        out_specs=P("req", None, "tp"),
        check_vma=False,
    )
```

```python
import math

import jax
import jax.numpy as jnp
from jax import lax
from jax.sharding import PartitionSpec as P

HD = 128
TOPK = 4
LANES = 128


NEG = -1e30
EPS = 1e-06
THETA = 1000000.0
HIGHEST = lax.Precision.HIGHEST


def rms_norm(inputs, gain_vector):
    values = inputs.astype(jnp.float32)
    scaled = values * lax.rsqrt(jnp.mean(values * values, axis=-1, keepdims=True) + EPS)
    return (scaled * gain_vector.astype(jnp.float32)).astype(jnp.bfloat16)


def rotate(values, positions):
    half_dim = values.shape[-1] // 2
    exponents = jnp.arange(half_dim, dtype=jnp.float32) * (2.0 / values.shape[-1])
    frequency = jnp.power(THETA, -exponents)
    angles = positions.astype(jnp.float32)[..., None, None] * frequency
    cosines = jnp.cos(angles)
    sine_part = jnp.sin(angles)
    front_half = values[..., :half_dim]
    back_half = values[..., half_dim:]
    return jnp.concatenate(
        [
            front_half * cosines - back_half * sine_part,
            back_half * cosines + front_half * sine_part,
        ],
        axis=-1,
    )


def shift_exchange(chunks, axis, count, spread=False):
    me = lax.axis_index(axis)
    pieces = [chunks if spread else lax.dynamic_index_in_dim(chunks, me, 0, keepdims=False)]
    for shift in range(1, count):
        send = chunks if spread else lax.dynamic_index_in_dim(
            chunks, (me + shift) % count, 0, keepdims=False
        )
        pairs = [(source, (source + shift) % count) for source in range(count)]
        pieces.append(lax.ppermute(send, axis, pairs))
    return pieces


def by_source(pieces, axis, count):
    me = lax.axis_index(axis)
    stacked = jnp.stack(pieces)
    order = (me - jnp.arange(count, dtype=jnp.int32)) % count
    return jnp.take(stacked, order, axis=0)


def bcast_a2a(values, axis, count):
    spread = jnp.broadcast_to(values[None], (count,) + values.shape)
    return lax.all_to_all(spread, axis, 0, 0, tiled=True).reshape(
        (count * values.shape[0],) + values.shape[1:]
    )


def per_device(
    tokens_in,
    attn_norm,
    qkv_weight,
    qkv_bias,
    out_weight,
    cache_keys,
    cache_values,
    page_table,
    cache_lengths,
    mlp_norm,
    routes,
    route_gates,
    expert_w_gate,
    expert_w_up,
    expert_w_down,
    shared_w_gate,
    shared_w_up,
    shared_w_down,
    shared_switch,
):
    req_rows, step_count, model_width = tokens_in.shape
    head_width = qkv_weight.shape[2]
    local_heads = head_width // HD
    req_count = lax.axis_size("req")
    tp_count = lax.axis_size("tp")
    req_index = lax.axis_index("req")
    tp_index = lax.axis_index("tp")
    all_requests = page_table.shape[0]
    pool_here = cache_keys.shape[0]
    page_len = cache_keys.shape[1]
    score_scale = 1.0 / math.sqrt(HD)
    col_share = model_width // tp_count
    row_count = req_rows * step_count
    normed = rms_norm(tokens_in, attn_norm)
    own_lengths = lax.dynamic_slice_in_dim(cache_lengths, req_index * req_rows, req_rows)
    positions = own_lengths[:, None] + jnp.arange(step_count, dtype=jnp.int32)[None, :]
    head_shape = (req_rows, step_count, local_heads, HD)

    def project(part, rows):
        return jnp.einsum(
            "rsd,df->rsf", rows, qkv_weight[:, part], preferred_element_type=jnp.float32
        ) + qkv_bias[part].astype(jnp.float32)

    query_new = rotate(project(0, normed).reshape(head_shape), positions).astype(jnp.bfloat16)
    query_spread = jnp.broadcast_to(query_new[None], (req_count,) + query_new.shape)
    normed_late, query_spread = lax.optimization_barrier((normed, query_spread))
    query_all = lax.all_to_all(query_spread, "req", 0, 0, tiled=True).reshape(
        (req_count * req_rows,) + query_new.shape[1:]
    )
    key_value = jnp.einsum(
        "rsd,dcf->rscf", normed_late, qkv_weight[:, 1:], preferred_element_type=jnp.float32
    ) + qkv_bias[1:].astype(jnp.float32)
    key_new = rotate(key_value[:, :, 0].reshape(head_shape), positions).astype(jnp.bfloat16)
    value_new = key_value[:, :, 1].reshape(head_shape).astype(jnp.bfloat16)
    slot_ids = req_index * pool_here + jnp.arange(pool_here, dtype=jnp.int32)
    matches = (page_table[:, :, None] == slot_ids[None, None, :]).astype(jnp.int32)
    request_ids = jnp.arange(all_requests, dtype=jnp.int32)
    page_ids = jnp.arange(page_table.shape[1], dtype=jnp.int32)
    owner = jnp.sum(matches * request_ids[:, None, None], axis=(0, 1))
    logical = jnp.sum(matches * page_ids[None, :, None], axis=(0, 1))
    present = jnp.sum(matches, axis=(0, 1)) > 0
    token_pos = logical[:, None] * page_len + jnp.arange(page_len, dtype=jnp.int32)[None, :]
    live = present[:, None] & (token_pos < cache_lengths[owner][:, None])
    page_queries = query_all[owner]
    page_keys = cache_keys.reshape(pool_here, page_len, local_heads, HD)
    page_values = cache_values.reshape(pool_here, page_len, local_heads, HD)
    scores = (
        jnp.einsum("pshd,pkhd->pshk", page_queries, page_keys, preferred_element_type=jnp.float32)
        * score_scale
    )
    page_mask = live[:, None, None, :]
    masked = jnp.where(page_mask, scores, NEG)
    page_max = jnp.max(masked, axis=-1)
    weights = jnp.where(page_mask, jnp.exp(masked - page_max[..., None]), 0.0)
    page_sum = jnp.sum(weights, axis=-1)
    page_out = jnp.einsum(
        "pshk,pkhd->pshd",
        weights.astype(jnp.bfloat16),
        page_values,
        preferred_element_type=jnp.float32,
    )
    belongs = (owner[None, :] == request_ids[:, None]) & present[None, :]
    owned = belongs[:, :, None, None]
    local_max = jnp.max(jnp.where(owned, page_max[None], NEG), axis=1)
    factors = jnp.where(owned, jnp.exp(page_max[None] - local_max[:, None]), 0.0)
    local_out = jnp.einsum("rpsh,pshd->rshd", factors, page_out, precision=HIGHEST)
    local_sum = jnp.einsum("rpsh,psh->rsh", factors, page_sum, precision=HIGHEST)
    stat_width = step_count * local_heads
    stat_row = jnp.concatenate(
        [
            local_max.reshape(all_requests, stat_width),
            local_sum.reshape(all_requests, stat_width),
            jnp.zeros((all_requests, HD - 2 * stat_width), jnp.float32),
        ],
        axis=1,
    )
    packed = jnp.concatenate(
        [local_out.reshape(all_requests, stat_width, HD), stat_row[:, None, :]], axis=1
    )
    gathered = lax.all_to_all(packed, "req", 0, 0, tiled=True).reshape(
        req_count, req_rows, stat_width + 1, HD
    )
    part_out = gathered[:, :, :stat_width, :]
    part_max = gathered[:, :, stat_width, :stat_width]
    part_sum = gathered[:, :, stat_width, stat_width : 2 * stat_width]
    cache_max = jnp.max(part_max, axis=0)
    rescale = jnp.exp(part_max - cache_max[None])
    cache_out = jnp.sum(part_out * rescale[..., None], axis=0).reshape(
        req_rows, step_count, local_heads, HD
    )
    cache_sum = jnp.sum(part_sum * rescale, axis=0).reshape(req_rows, step_count, local_heads)
    cache_max = cache_max.reshape(req_rows, step_count, local_heads)
    new_scores = (
        jnp.einsum("rshd,rthd->rsht", query_new, key_new, preferred_element_type=jnp.float32)
        * score_scale
    )
    causal = jnp.arange(step_count)[:, None] >= jnp.arange(step_count)[None, :]
    new_mask = causal[None, :, None, :]
    new_masked = jnp.where(new_mask, new_scores, NEG)
    new_max = jnp.max(new_masked, axis=-1)
    new_weights = jnp.where(new_mask, jnp.exp(new_masked - new_max[..., None]), 0.0)
    new_sum = jnp.sum(new_weights, axis=-1)
    new_out = jnp.einsum(
        "rsht,rthd->rshd",
        new_weights.astype(jnp.bfloat16),
        value_new,
        preferred_element_type=jnp.float32,
    )
    top_max = jnp.maximum(cache_max, new_max)
    cache_factor = jnp.exp(cache_max - top_max)
    new_factor = jnp.exp(new_max - top_max)
    attended = (cache_out * cache_factor[..., None] + new_out * new_factor[..., None]) / (
        cache_sum * cache_factor + new_sum * new_factor
    )[..., None]
    attended = attended.astype(jnp.bfloat16).reshape(row_count, head_width)
    attn_part = jnp.dot(attended, out_weight, preferred_element_type=jnp.float32)
    attn_full = jnp.sum(
        by_source(shift_exchange(attn_part, "tp", tp_count, spread=True), "tp", tp_count), axis=0
    )
    resid = tokens_in.reshape(row_count, model_width).astype(jnp.float32) + attn_full
    mixed = rms_norm(resid, mlp_norm)
    expert_count = req_count * expert_w_gate.shape[0]
    capacity = max(2, (row_count * TOPK + expert_count - 1) // expert_count)
    picks = routes.reshape(row_count * TOPK)
    gates_flat = route_gates.reshape(row_count * TOPK)
    expert_hot = (picks[:, None] == jnp.arange(expert_count, dtype=jnp.int32)[None, :]).astype(
        jnp.int32
    )
    slot_index = jnp.sum((jnp.cumsum(expert_hot, axis=0) - 1) * expert_hot, axis=1)
    destination = picks * capacity + slot_index
    dest_hot = (
        destination[:, None] == jnp.arange(expert_count * capacity, dtype=jnp.int32)[None, :]
    ).astype(jnp.float32)
    token_hot = (
        (jnp.arange(row_count * TOPK, dtype=jnp.int32) // TOPK)[:, None]
        == jnp.arange(row_count, dtype=jnp.int32)[None, :]
    ).astype(jnp.float32)
    placement = jnp.einsum("cx,ct->xt", dest_hot, token_hot, precision=HIGHEST).astype(jnp.bfloat16)
    outgoing = jnp.dot(placement, mixed, preferred_element_type=jnp.float32).astype(jnp.bfloat16)
    combine_map = jnp.einsum(
        "ct,cx->tx", token_hot, dest_hot * gates_flat[:, None], precision=HIGHEST
    )
    w_gate_here = expert_w_gate[0]
    w_up_here = expert_w_up[0]
    w_down_here = expert_w_down[0]
    mixed_cols = lax.dynamic_slice_in_dim(mixed, tp_index * col_share, col_share, 1)
    shared_send = jnp.broadcast_to(mixed_cols[None], (req_count, row_count, col_share))
    moe_lines = capacity * model_width // LANES
    dispatch = jnp.concatenate(
        [
            outgoing.reshape(req_count, moe_lines, LANES),
            shared_send.reshape(req_count, row_count * col_share // LANES, LANES),
        ],
        axis=1,
    )
    received = lax.all_to_all(dispatch, "req", 0, 0, tiled=True)
    flat_rows = received[:, :moe_lines].reshape(req_count * capacity, model_width)
    piece = received[:, moe_lines:].reshape(req_count * row_count, col_share)
    gate_pre = jnp.dot(flat_rows, w_gate_here, preferred_element_type=jnp.float32)
    up_pre = jnp.dot(flat_rows, w_up_here, preferred_element_type=jnp.float32)
    hidden = (jax.nn.silu(gate_pre) * up_pre).astype(jnp.bfloat16)
    partial_out = jnp.dot(hidden, w_down_here, preferred_element_type=jnp.float32)
    expert_rows = req_count * capacity
    gate_part = jnp.dot(piece, shared_w_gate, preferred_element_type=jnp.float32)
    up_part = jnp.dot(piece, shared_w_up, preferred_element_type=jnp.float32)
    unit_count = shared_w_gate.shape[1]
    all_rows = req_count * row_count
    share_rows = all_rows // tp_count
    shared_pre = jnp.concatenate([gate_part, up_part], axis=1)
    expert_lines = expert_rows * col_share // LANES

    def reduce_send(target):
        return jnp.concatenate(
            [
                lax.dynamic_slice_in_dim(partial_out, target * col_share, col_share, 1).reshape(
                    expert_lines, LANES
                ),
                lax.dynamic_slice_in_dim(shared_pre, target * share_rows, share_rows, 0).reshape(
                    share_rows * 2 * unit_count // LANES, LANES
                ),
            ],
            axis=0,
        )

    reduce_pieces = [reduce_send(tp_index)]
    for shift in range(1, tp_count):
        pairs = [(source, (source + shift) % tp_count) for source in range(tp_count)]
        reduce_pieces.append(
            lax.ppermute(reduce_send((tp_index + shift) % tp_count), "tp", pairs)
        )
    reduce_out = sum(reduce_pieces)
    expert_sum = reduce_out[:expert_lines].reshape(expert_rows, col_share)
    shared_sum = reduce_out[expert_lines:].reshape(share_rows, 2 * unit_count)
    shared_hidden = (jax.nn.silu(shared_sum[:, :unit_count]) * shared_sum[:, unit_count:]).astype(
        jnp.bfloat16
    )
    hidden_all = by_source(
        shift_exchange(shared_hidden, "tp", tp_count, spread=True), "tp", tp_count
    ).reshape(all_rows, unit_count)
    shared_down = jnp.dot(hidden_all, shared_w_down, preferred_element_type=jnp.float32)
    ey = expert_sum.astype(jnp.bfloat16).astype(jnp.float32)
    ey_lines = capacity * col_share // LANES
    back_in = jnp.concatenate(
        [
            ey.reshape(req_count, ey_lines, LANES),
            shared_down.reshape(req_count, row_count * col_share // LANES, LANES),
        ],
        axis=1,
    )
    back = lax.all_to_all(back_in, "req", 0, 0, tiled=True)
    returned = back[:, :ey_lines].reshape(expert_count * capacity, col_share)
    shared_mine = jnp.sum(back[:, ey_lines:].reshape(req_count, row_count, col_share), axis=0)
    moe_out = jnp.dot(combine_map, returned, precision=HIGHEST)
    switch = jax.nn.sigmoid(jnp.dot(mixed, shared_switch, preferred_element_type=jnp.float32))
    resid_mine = lax.dynamic_slice_in_dim(resid, tp_index * col_share, col_share, 1)
    final = resid_mine + moe_out + switch[:, None] * shared_mine
    return final.astype(jnp.bfloat16).reshape(req_rows, step_count, col_share)


def solution(mesh):
    return jax.shard_map(
        per_device,
        mesh=mesh,
        in_specs=(
            P("req", None, None),
            P(),
            P(None, None, "tp"),
            P(None, "tp"),
            P("tp", None),
            P("req", None, "tp"),
            P("req", None, "tp"),
            P(),
            P(),
            P(),
            P("req", None, None),
            P("req", None, None),
            P("req", None, "tp"),
            P("req", None, "tp"),
            P("req", "tp", None),
            P("tp", "req"),
            P("tp", "req"),
            P("req", "tp"),
            P(),
        ),
        out_specs=P("req", None, "tp"),
        check_vma=False,
    )
```

```python
import math

import jax
import jax.numpy as jnp
from jax import lax
from jax.sharding import PartitionSpec as P

HD = 128
TOPK = 4
LANES = 128


NEG = -1e30
EPS = 1e-06
THETA = 1000000.0
HIGHEST = lax.Precision.HIGHEST


def rms_norm(inputs, gain_vector):
    values = inputs.astype(jnp.float32)
    scaled = values * lax.rsqrt(jnp.mean(values * values, axis=-1, keepdims=True) + EPS)
    return (scaled * gain_vector.astype(jnp.float32)).astype(jnp.bfloat16)


def rotate(values, positions):
    half_dim = values.shape[-1] // 2
    exponents = jnp.arange(half_dim, dtype=jnp.float32) * (2.0 / values.shape[-1])
    frequency = jnp.power(THETA, -exponents)
    angles = positions.astype(jnp.float32)[..., None, None] * frequency
    cosines = jnp.cos(angles)
    sine_part = jnp.sin(angles)
    front_half = values[..., :half_dim]
    back_half = values[..., half_dim:]
    return jnp.concatenate(
        [
            front_half * cosines - back_half * sine_part,
            back_half * cosines + front_half * sine_part,
        ],
        axis=-1,
    )


def shift_exchange(chunks, axis, count, spread=False):
    me = lax.axis_index(axis)
    pieces = [chunks if spread else lax.dynamic_index_in_dim(chunks, me, 0, keepdims=False)]
    for shift in range(1, count):
        send = chunks if spread else lax.dynamic_index_in_dim(
            chunks, (me + shift) % count, 0, keepdims=False
        )
        pairs = [(source, (source + shift) % count) for source in range(count)]
        pieces.append(lax.ppermute(send, axis, pairs))
    return pieces


def by_source(pieces, axis, count):
    me = lax.axis_index(axis)
    stacked = jnp.stack(pieces)
    order = (me - jnp.arange(count, dtype=jnp.int32)) % count
    return jnp.take(stacked, order, axis=0)


def bcast_a2a(values, axis, count):
    spread = jnp.broadcast_to(values[None], (count,) + values.shape)
    return lax.all_to_all(spread, axis, 0, 0, tiled=True).reshape(
        (count * values.shape[0],) + values.shape[1:]
    )


def per_device(
    tokens_in,
    attn_norm,
    qkv_weight,
    qkv_bias,
    out_weight,
    cache_keys,
    cache_values,
    page_table,
    cache_lengths,
    mlp_norm,
    routes,
    route_gates,
    expert_w_gate,
    expert_w_up,
    expert_w_down,
    shared_w_gate,
    shared_w_up,
    shared_w_down,
    shared_switch,
):
    req_rows, step_count, model_width = tokens_in.shape
    head_width = qkv_weight.shape[2]
    local_heads = head_width // HD
    req_count = lax.axis_size("req")
    tp_count = lax.axis_size("tp")
    req_index = lax.axis_index("req")
    tp_index = lax.axis_index("tp")
    all_requests = page_table.shape[0]
    pool_here = cache_keys.shape[0]
    page_len = cache_keys.shape[1]
    score_scale = 1.0 / math.sqrt(HD)
    col_share = model_width // tp_count
    row_count = req_rows * step_count
    normed = rms_norm(tokens_in, attn_norm)
    own_lengths = lax.dynamic_slice_in_dim(cache_lengths, req_index * req_rows, req_rows)
    positions = own_lengths[:, None] + jnp.arange(step_count, dtype=jnp.int32)[None, :]
    head_shape = (req_rows, step_count, local_heads, HD)

    def project(part, rows):
        return jnp.einsum(
            "rsd,df->rsf", rows, qkv_weight[:, part], preferred_element_type=jnp.float32
        ) + qkv_bias[part].astype(jnp.float32)

    query_new = rotate(project(0, normed).reshape(head_shape), positions).astype(jnp.bfloat16)
    query_spread = jnp.broadcast_to(query_new[None], (req_count,) + query_new.shape)
    normed_late, query_spread = lax.optimization_barrier((normed, query_spread))
    query_all = lax.all_to_all(query_spread, "req", 0, 0, tiled=True).reshape(
        (req_count * req_rows,) + query_new.shape[1:]
    )
    key_value = jnp.einsum(
        "rsd,dcf->rscf", normed_late, qkv_weight[:, 1:], preferred_element_type=jnp.float32
    ) + qkv_bias[1:].astype(jnp.float32)
    key_new = rotate(key_value[:, :, 0].reshape(head_shape), positions).astype(jnp.bfloat16)
    value_new = key_value[:, :, 1].reshape(head_shape).astype(jnp.bfloat16)
    slot_ids = req_index * pool_here + jnp.arange(pool_here, dtype=jnp.int32)
    matches = (page_table[:, :, None] == slot_ids[None, None, :]).astype(jnp.int32)
    request_ids = jnp.arange(all_requests, dtype=jnp.int32)
    page_ids = jnp.arange(page_table.shape[1], dtype=jnp.int32)
    owner = jnp.sum(matches * request_ids[:, None, None], axis=(0, 1))
    logical = jnp.sum(matches * page_ids[None, :, None], axis=(0, 1))
    present = jnp.sum(matches, axis=(0, 1)) > 0
    token_pos = logical[:, None] * page_len + jnp.arange(page_len, dtype=jnp.int32)[None, :]
    live = present[:, None] & (token_pos < cache_lengths[owner][:, None])
    page_queries = query_all[owner]
    page_keys = cache_keys.reshape(pool_here, page_len, local_heads, HD)
    page_values = cache_values.reshape(pool_here, page_len, local_heads, HD)
    scores = (
        jnp.einsum("pshd,pkhd->pshk", page_queries, page_keys, preferred_element_type=jnp.float32)
        * score_scale
    )
    page_mask = live[:, None, None, :]
    masked = jnp.where(page_mask, scores, NEG)
    page_max = jnp.max(masked, axis=-1)
    weights = jnp.where(page_mask, jnp.exp(masked - page_max[..., None]), 0.0)
    page_sum = jnp.sum(weights, axis=-1)
    page_out = jnp.einsum(
        "pshk,pkhd->pshd",
        weights.astype(jnp.bfloat16),
        page_values,
        preferred_element_type=jnp.float32,
    )
    belongs = (owner[None, :] == request_ids[:, None]) & present[None, :]
    owned = belongs[:, :, None, None]
    local_max = jnp.max(jnp.where(owned, page_max[None], NEG), axis=1)
    factors = jnp.where(owned, jnp.exp(page_max[None] - local_max[:, None]), 0.0)
    local_out = jnp.einsum("rpsh,pshd->rshd", factors, page_out, precision=HIGHEST)
    local_sum = jnp.einsum("rpsh,psh->rsh", factors, page_sum, precision=HIGHEST)
    stat_width = step_count * local_heads
    stat_row = jnp.concatenate(
        [
            local_max.reshape(all_requests, stat_width),
            local_sum.reshape(all_requests, stat_width),
            jnp.zeros((all_requests, HD - 2 * stat_width), jnp.float32),
        ],
        axis=1,
    )
    packed = jnp.concatenate(
        [local_out.reshape(all_requests, stat_width, HD), stat_row[:, None, :]], axis=1
    )
    gathered = lax.all_to_all(packed, "req", 0, 0, tiled=True).reshape(
        req_count, req_rows, stat_width + 1, HD
    )
    part_out = gathered[:, :, :stat_width, :]
    part_max = gathered[:, :, stat_width, :stat_width]
    part_sum = gathered[:, :, stat_width, stat_width : 2 * stat_width]
    cache_max = jnp.max(part_max, axis=0)
    rescale = jnp.exp(part_max - cache_max[None])
    cache_out = jnp.sum(part_out * rescale[..., None], axis=0).reshape(
        req_rows, step_count, local_heads, HD
    )
    cache_sum = jnp.sum(part_sum * rescale, axis=0).reshape(req_rows, step_count, local_heads)
    cache_max = cache_max.reshape(req_rows, step_count, local_heads)
    new_scores = (
        jnp.einsum("rshd,rthd->rsht", query_new, key_new, preferred_element_type=jnp.float32)
        * score_scale
    )
    causal = jnp.arange(step_count)[:, None] >= jnp.arange(step_count)[None, :]
    new_mask = causal[None, :, None, :]
    new_masked = jnp.where(new_mask, new_scores, NEG)
    new_max = jnp.max(new_masked, axis=-1)
    new_weights = jnp.where(new_mask, jnp.exp(new_masked - new_max[..., None]), 0.0)
    new_sum = jnp.sum(new_weights, axis=-1)
    new_out = jnp.einsum(
        "rsht,rthd->rshd",
        new_weights.astype(jnp.bfloat16),
        value_new,
        preferred_element_type=jnp.float32,
    )
    top_max = jnp.maximum(cache_max, new_max)
    cache_factor = jnp.exp(cache_max - top_max)
    new_factor = jnp.exp(new_max - top_max)
    attended = (cache_out * cache_factor[..., None] + new_out * new_factor[..., None]) / (
        cache_sum * cache_factor + new_sum * new_factor
    )[..., None]
    attended = attended.astype(jnp.bfloat16).reshape(row_count, head_width)
    attn_part = jnp.dot(attended, out_weight, preferred_element_type=jnp.float32)
    attn_full = jnp.sum(
        by_source(shift_exchange(attn_part, "tp", tp_count, spread=True), "tp", tp_count), axis=0
    )
    resid = tokens_in.reshape(row_count, model_width).astype(jnp.float32) + attn_full
    mixed = rms_norm(resid, mlp_norm)
    expert_count = req_count * expert_w_gate.shape[0]
    capacity = max(2, (row_count * TOPK + expert_count - 1) // expert_count)
    picks = routes.reshape(row_count * TOPK)
    gates_flat = route_gates.reshape(row_count * TOPK)
    expert_hot = (picks[:, None] == jnp.arange(expert_count, dtype=jnp.int32)[None, :]).astype(
        jnp.int32
    )
    slot_index = jnp.sum((jnp.cumsum(expert_hot, axis=0) - 1) * expert_hot, axis=1)
    destination = picks * capacity + slot_index
    dest_hot = (
        destination[:, None] == jnp.arange(expert_count * capacity, dtype=jnp.int32)[None, :]
    ).astype(jnp.float32)
    token_hot = (
        (jnp.arange(row_count * TOPK, dtype=jnp.int32) // TOPK)[:, None]
        == jnp.arange(row_count, dtype=jnp.int32)[None, :]
    ).astype(jnp.float32)
    placement = jnp.einsum("cx,ct->xt", dest_hot, token_hot, precision=HIGHEST).astype(jnp.bfloat16)
    outgoing = jnp.dot(placement, mixed, preferred_element_type=jnp.float32).astype(jnp.bfloat16)
    combine_map = jnp.einsum(
        "ct,cx->tx", token_hot, dest_hot * gates_flat[:, None], precision=HIGHEST
    )
    w_gate_here = expert_w_gate[0]
    w_up_here = expert_w_up[0]
    w_down_here = expert_w_down[0]
    mixed_cols = lax.dynamic_slice_in_dim(mixed, tp_index * col_share, col_share, 1)
    shared_send = jnp.broadcast_to(mixed_cols[None], (req_count, row_count, col_share))
    moe_lines = capacity * model_width // LANES
    dispatch = jnp.concatenate(
        [
            outgoing.reshape(req_count, moe_lines, LANES),
            shared_send.reshape(req_count, row_count * col_share // LANES, LANES),
        ],
        axis=1,
    )
    received = lax.all_to_all(dispatch, "req", 0, 0, tiled=True)
    flat_rows = received[:, :moe_lines].reshape(req_count * capacity, model_width)
    piece = received[:, moe_lines:].reshape(req_count * row_count, col_share)
    gate_pre = jnp.dot(flat_rows, w_gate_here, preferred_element_type=jnp.float32)
    up_pre = jnp.dot(flat_rows, w_up_here, preferred_element_type=jnp.float32)
    hidden = (jax.nn.silu(gate_pre) * up_pre).astype(jnp.bfloat16)
    partial_out = jnp.dot(hidden, w_down_here, preferred_element_type=jnp.float32)
    expert_rows = req_count * capacity
    partial_split = partial_out.reshape(expert_rows, tp_count, col_share).transpose(1, 0, 2)
    gate_part = jnp.dot(piece, shared_w_gate, preferred_element_type=jnp.float32)
    up_part = jnp.dot(piece, shared_w_up, preferred_element_type=jnp.float32)
    unit_count = shared_w_gate.shape[1]
    all_rows = req_count * row_count
    share_rows = all_rows // tp_count
    shared_pre = jnp.concatenate([gate_part, up_part], axis=1).reshape(
        tp_count, share_rows * 2 * unit_count
    )
    reduce_in = jnp.concatenate(
        [partial_split.reshape(tp_count, expert_rows * col_share), shared_pre], axis=1
    )
    reduce_out = sum(shift_exchange(reduce_in, "tp", tp_count))
    expert_sum = reduce_out[: expert_rows * col_share].reshape(expert_rows, col_share)
    shared_sum = reduce_out[expert_rows * col_share :].reshape(share_rows, 2 * unit_count)
    shared_hidden = (jax.nn.silu(shared_sum[:, :unit_count]) * shared_sum[:, unit_count:]).astype(
        jnp.bfloat16
    )
    hidden_all = by_source(
        shift_exchange(shared_hidden, "tp", tp_count, spread=True), "tp", tp_count
    ).reshape(all_rows, unit_count)
    shared_down = jnp.dot(hidden_all, shared_w_down, preferred_element_type=jnp.float32)
    ey = expert_sum.astype(jnp.bfloat16).astype(jnp.float32)
    ey_lines = capacity * col_share // LANES
    back_in = jnp.concatenate(
        [
            ey.reshape(req_count, ey_lines, LANES),
            shared_down.reshape(req_count, row_count * col_share // LANES, LANES),
        ],
        axis=1,
    )
    back = lax.all_to_all(back_in, "req", 0, 0, tiled=True)
    returned = back[:, :ey_lines].reshape(expert_count * capacity, col_share)
    shared_mine = jnp.sum(back[:, ey_lines:].reshape(req_count, row_count, col_share), axis=0)
    moe_out = jnp.dot(combine_map, returned, precision=HIGHEST)
    switch = jax.nn.sigmoid(jnp.dot(mixed, shared_switch, preferred_element_type=jnp.float32))
    resid_mine = lax.dynamic_slice_in_dim(resid, tp_index * col_share, col_share, 1)
    final = resid_mine + moe_out + switch[:, None] * shared_mine
    return final.astype(jnp.bfloat16).reshape(req_rows, step_count, col_share)


def solution(mesh):
    return jax.shard_map(
        per_device,
        mesh=mesh,
        in_specs=(
            P("req", None, None),
            P(),
            P(None, None, "tp"),
            P(None, "tp"),
            P("tp", None),
            P("req", None, "tp"),
            P("req", None, "tp"),
            P(),
            P(),
            P(),
            P("req", None, None),
            P("req", None, None),
            P("req", None, "tp"),
            P("req", None, "tp"),
            P("req", "tp", None),
            P("tp", "req"),
            P("tp", "req"),
            P("req", "tp"),
            P(),
        ),
        out_specs=P("req", None, "tp"),
        check_vma=False,
    )
```

```python
import math

import jax
import jax.numpy as jnp
from jax import lax
from jax.sharding import PartitionSpec as P

HD = 128
TOPK = 4
LANES = 128


NEG = -1e30
EPS = 1e-06
THETA = 1000000.0
HIGHEST = lax.Precision.HIGHEST


def rms_norm(inputs, gain_vector):
    values = inputs.astype(jnp.float32)
    scaled = values * lax.rsqrt(jnp.mean(values * values, axis=-1, keepdims=True) + EPS)
    return (scaled * gain_vector.astype(jnp.float32)).astype(jnp.bfloat16)


def rotate(values, positions):
    half_dim = values.shape[-1] // 2
    exponents = jnp.arange(half_dim, dtype=jnp.float32) * (2.0 / values.shape[-1])
    frequency = jnp.power(THETA, -exponents)
    angles = positions.astype(jnp.float32)[..., None, None] * frequency
    cosines = jnp.cos(angles)
    sine_part = jnp.sin(angles)
    front_half = values[..., :half_dim]
    back_half = values[..., half_dim:]
    return jnp.concatenate(
        [
            front_half * cosines - back_half * sine_part,
            back_half * cosines + front_half * sine_part,
        ],
        axis=-1,
    )


def shift_exchange(chunks, axis, count, spread=False):
    me = lax.axis_index(axis)
    pieces = [chunks if spread else lax.dynamic_index_in_dim(chunks, me, 0, keepdims=False)]
    for shift in range(1, count):
        send = chunks if spread else lax.dynamic_index_in_dim(
            chunks, (me + shift) % count, 0, keepdims=False
        )
        pairs = [(source, (source + shift) % count) for source in range(count)]
        pieces.append(lax.ppermute(send, axis, pairs))
    return pieces


def by_source(pieces, axis, count):
    me = lax.axis_index(axis)
    stacked = jnp.stack(pieces)
    order = (me - jnp.arange(count, dtype=jnp.int32)) % count
    return jnp.take(stacked, order, axis=0)


def bcast_a2a(values, axis, count):
    spread = jnp.broadcast_to(values[None], (count,) + values.shape)
    return lax.all_to_all(spread, axis, 0, 0, tiled=True).reshape(
        (count * values.shape[0],) + values.shape[1:]
    )


def per_device(
    tokens_in,
    attn_norm,
    qkv_weight,
    qkv_bias,
    out_weight,
    cache_keys,
    cache_values,
    page_table,
    cache_lengths,
    mlp_norm,
    routes,
    route_gates,
    expert_w_gate,
    expert_w_up,
    expert_w_down,
    shared_w_gate,
    shared_w_up,
    shared_w_down,
    shared_switch,
):
    req_rows, step_count, model_width = tokens_in.shape
    head_width = qkv_weight.shape[2]
    local_heads = head_width // HD
    req_count = lax.axis_size("req")
    tp_count = lax.axis_size("tp")
    req_index = lax.axis_index("req")
    tp_index = lax.axis_index("tp")
    all_requests = page_table.shape[0]
    pool_here = cache_keys.shape[0]
    page_len = cache_keys.shape[1]
    score_scale = 1.0 / math.sqrt(HD)
    col_share = model_width // tp_count
    row_count = req_rows * step_count
    normed = rms_norm(tokens_in, attn_norm)
    own_lengths = lax.dynamic_slice_in_dim(cache_lengths, req_index * req_rows, req_rows)
    positions = own_lengths[:, None] + jnp.arange(step_count, dtype=jnp.int32)[None, :]
    head_shape = (req_rows, step_count, local_heads, HD)

    def project(part, rows):
        return jnp.einsum(
            "rsd,df->rsf", rows, qkv_weight[:, part], preferred_element_type=jnp.float32
        ) + qkv_bias[part].astype(jnp.float32)

    query_new = rotate(project(0, normed).reshape(head_shape), positions).astype(jnp.bfloat16)
    query_spread = jnp.broadcast_to(query_new[None], (req_count,) + query_new.shape)
    normed_late, query_spread = lax.optimization_barrier((normed, query_spread))
    query_all = lax.all_to_all(query_spread, "req", 0, 0, tiled=True).reshape(
        (req_count * req_rows,) + query_new.shape[1:]
    )
    key_value = jnp.einsum(
        "rsd,dcf->rscf", normed_late, qkv_weight[:, 1:], preferred_element_type=jnp.float32
    ) + qkv_bias[1:].astype(jnp.float32)
    key_new = rotate(key_value[:, :, 0].reshape(head_shape), positions).astype(jnp.bfloat16)
    value_new = key_value[:, :, 1].reshape(head_shape).astype(jnp.bfloat16)
    slot_ids = req_index * pool_here + jnp.arange(pool_here, dtype=jnp.int32)
    matches = (page_table[:, :, None] == slot_ids[None, None, :]).astype(jnp.int32)
    request_ids = jnp.arange(all_requests, dtype=jnp.int32)
    page_ids = jnp.arange(page_table.shape[1], dtype=jnp.int32)
    owner = jnp.sum(matches * request_ids[:, None, None], axis=(0, 1))
    logical = jnp.sum(matches * page_ids[None, :, None], axis=(0, 1))
    present = jnp.sum(matches, axis=(0, 1)) > 0
    token_pos = logical[:, None] * page_len + jnp.arange(page_len, dtype=jnp.int32)[None, :]
    live = present[:, None] & (token_pos < cache_lengths[owner][:, None])
    page_queries = query_all[owner]
    page_keys = cache_keys.reshape(pool_here, page_len, local_heads, HD)
    page_values = cache_values.reshape(pool_here, page_len, local_heads, HD)
    scores = (
        jnp.einsum("pshd,pkhd->pshk", page_queries, page_keys, preferred_element_type=jnp.float32)
        * score_scale
    )
    page_mask = live[:, None, None, :]
    masked = jnp.where(page_mask, scores, NEG)
    page_max = jnp.max(masked, axis=-1)
    weights = jnp.where(page_mask, jnp.exp(masked - page_max[..., None]), 0.0)
    page_sum = jnp.sum(weights, axis=-1)
    page_out = jnp.einsum(
        "pshk,pkhd->pshd",
        weights.astype(jnp.bfloat16),
        page_values,
        preferred_element_type=jnp.float32,
    )
    belongs = (owner[None, :] == request_ids[:, None]) & present[None, :]
    owned = belongs[:, :, None, None]
    local_max = jnp.max(jnp.where(owned, page_max[None], NEG), axis=1)
    factors = jnp.where(owned, jnp.exp(page_max[None] - local_max[:, None]), 0.0)
    local_out = jnp.einsum("rpsh,pshd->rshd", factors, page_out, precision=HIGHEST)
    local_sum = jnp.einsum("rpsh,psh->rsh", factors, page_sum, precision=HIGHEST)
    stat_width = step_count * local_heads
    stat_row = jnp.concatenate(
        [
            local_max.reshape(all_requests, stat_width),
            local_sum.reshape(all_requests, stat_width),
            jnp.zeros((all_requests, HD - 2 * stat_width), jnp.float32),
        ],
        axis=1,
    )
    packed = jnp.concatenate(
        [local_out.reshape(all_requests, stat_width, HD), stat_row[:, None, :]], axis=1
    )
    gathered = lax.all_to_all(packed, "req", 0, 0, tiled=True).reshape(
        req_count, req_rows, stat_width + 1, HD
    )
    part_out = gathered[:, :, :stat_width, :]
    part_max = gathered[:, :, stat_width, :stat_width]
    part_sum = gathered[:, :, stat_width, stat_width : 2 * stat_width]
    cache_max = jnp.max(part_max, axis=0)
    rescale = jnp.exp(part_max - cache_max[None])
    cache_out = jnp.sum(part_out * rescale[..., None], axis=0).reshape(
        req_rows, step_count, local_heads, HD
    )
    cache_sum = jnp.sum(part_sum * rescale, axis=0).reshape(req_rows, step_count, local_heads)
    cache_max = cache_max.reshape(req_rows, step_count, local_heads)
    new_scores = (
        jnp.einsum("rshd,rthd->rsht", query_new, key_new, preferred_element_type=jnp.float32)
        * score_scale
    )
    causal = jnp.arange(step_count)[:, None] >= jnp.arange(step_count)[None, :]
    new_mask = causal[None, :, None, :]
    new_masked = jnp.where(new_mask, new_scores, NEG)
    new_max = jnp.max(new_masked, axis=-1)
    new_weights = jnp.where(new_mask, jnp.exp(new_masked - new_max[..., None]), 0.0)
    new_sum = jnp.sum(new_weights, axis=-1)
    new_out = jnp.einsum(
        "rsht,rthd->rshd",
        new_weights.astype(jnp.bfloat16),
        value_new,
        preferred_element_type=jnp.float32,
    )
    top_max = jnp.maximum(cache_max, new_max)
    cache_factor = jnp.exp(cache_max - top_max)
    new_factor = jnp.exp(new_max - top_max)
    attended = (cache_out * cache_factor[..., None] + new_out * new_factor[..., None]) / (
        cache_sum * cache_factor + new_sum * new_factor
    )[..., None]
    attended = attended.astype(jnp.bfloat16).reshape(row_count, head_width)
    attn_part = jnp.dot(attended, out_weight, preferred_element_type=jnp.float32)
    attn_full = jnp.sum(
        by_source(shift_exchange(attn_part, "tp", tp_count, spread=True), "tp", tp_count), axis=0
    )
    resid = tokens_in.reshape(row_count, model_width).astype(jnp.float32) + attn_full
    mixed = rms_norm(resid, mlp_norm)
    expert_count = req_count * expert_w_gate.shape[0]
    capacity = max(2, (row_count * TOPK + expert_count - 1) // expert_count)
    picks = routes.reshape(row_count * TOPK)
    gates_flat = route_gates.reshape(row_count * TOPK)
    expert_hot = (picks[:, None] == jnp.arange(expert_count, dtype=jnp.int32)[None, :]).astype(
        jnp.int32
    )
    slot_index = jnp.sum((jnp.cumsum(expert_hot, axis=0) - 1) * expert_hot, axis=1)
    destination = picks * capacity + slot_index
    dest_hot = (
        destination[:, None] == jnp.arange(expert_count * capacity, dtype=jnp.int32)[None, :]
    ).astype(jnp.float32)
    token_hot = (
        (jnp.arange(row_count * TOPK, dtype=jnp.int32) // TOPK)[:, None]
        == jnp.arange(row_count, dtype=jnp.int32)[None, :]
    ).astype(jnp.float32)
    placement = jnp.einsum("cx,ct->xt", dest_hot, token_hot, precision=HIGHEST).astype(jnp.bfloat16)
    outgoing = jnp.dot(placement, mixed, preferred_element_type=jnp.float32).astype(jnp.bfloat16)
    combine_map = jnp.einsum(
        "ct,cx->tx", token_hot, dest_hot * gates_flat[:, None], precision=HIGHEST
    )
    w_gate_here = expert_w_gate[0]
    w_up_here = expert_w_up[0]
    w_down_here = expert_w_down[0]
    mixed_cols = lax.dynamic_slice_in_dim(mixed, tp_index * col_share, col_share, 1)
    shared_send = jnp.broadcast_to(mixed_cols[None], (req_count, row_count, col_share))
    moe_lines = capacity * model_width // LANES
    dispatch = jnp.concatenate(
        [
            outgoing.reshape(req_count, moe_lines, LANES),
            shared_send.reshape(req_count, row_count * col_share // LANES, LANES),
        ],
        axis=1,
    )
    received = lax.all_to_all(dispatch, "req", 0, 0, tiled=True)
    flat_rows = received[:, :moe_lines].reshape(req_count * capacity, model_width)
    piece = received[:, moe_lines:].reshape(req_count * row_count, col_share)
    expert_rows = req_count * capacity
    gate_part = jnp.dot(piece, shared_w_gate, preferred_element_type=jnp.float32)
    up_part = jnp.dot(piece, shared_w_up, preferred_element_type=jnp.float32)
    unit_count = shared_w_gate.shape[1]
    all_rows = req_count * row_count
    share_rows = all_rows // tp_count
    shared_pre = jnp.concatenate([gate_part, up_part], axis=1).reshape(
        tp_count, share_rows * 2 * unit_count
    )
    flat_rows, shared_pre = lax.optimization_barrier((flat_rows, shared_pre))
    gate_pre = jnp.dot(flat_rows, w_gate_here, preferred_element_type=jnp.float32)
    up_pre = jnp.dot(flat_rows, w_up_here, preferred_element_type=jnp.float32)
    hidden = (jax.nn.silu(gate_pre) * up_pre).astype(jnp.bfloat16)
    shared_sum = sum(shift_exchange(shared_pre, "tp", tp_count)).reshape(
        share_rows, 2 * unit_count
    )
    hidden, shared_sum = lax.optimization_barrier((hidden, shared_sum))
    partial_out = jnp.dot(hidden, w_down_here, preferred_element_type=jnp.float32)
    partial_split = partial_out.reshape(expert_rows, tp_count, col_share).transpose(1, 0, 2)
    expert_sum = sum(
        shift_exchange(partial_split.reshape(tp_count, expert_rows * col_share), "tp", tp_count)
    ).reshape(expert_rows, col_share)
    shared_hidden = (jax.nn.silu(shared_sum[:, :unit_count]) * shared_sum[:, unit_count:]).astype(
        jnp.bfloat16
    )
    hidden_all = by_source(
        shift_exchange(shared_hidden, "tp", tp_count, spread=True), "tp", tp_count
    ).reshape(all_rows, unit_count)
    shared_down = jnp.dot(hidden_all, shared_w_down, preferred_element_type=jnp.float32)
    ey = expert_sum.astype(jnp.bfloat16).astype(jnp.float32)
    ey_lines = capacity * col_share // LANES
    back_in = jnp.concatenate(
        [
            ey.reshape(req_count, ey_lines, LANES),
            shared_down.reshape(req_count, row_count * col_share // LANES, LANES),
        ],
        axis=1,
    )
    back = lax.all_to_all(back_in, "req", 0, 0, tiled=True)
    returned = back[:, :ey_lines].reshape(expert_count * capacity, col_share)
    shared_mine = jnp.sum(back[:, ey_lines:].reshape(req_count, row_count, col_share), axis=0)
    moe_out = jnp.dot(combine_map, returned, precision=HIGHEST)
    switch = jax.nn.sigmoid(jnp.dot(mixed, shared_switch, preferred_element_type=jnp.float32))
    resid_mine = lax.dynamic_slice_in_dim(resid, tp_index * col_share, col_share, 1)
    final = resid_mine + moe_out + switch[:, None] * shared_mine
    return final.astype(jnp.bfloat16).reshape(req_rows, step_count, col_share)


def solution(mesh):
    return jax.shard_map(
        per_device,
        mesh=mesh,
        in_specs=(
            P("req", None, None),
            P(),
            P(None, None, "tp"),
            P(None, "tp"),
            P("tp", None),
            P("req", None, "tp"),
            P("req", None, "tp"),
            P(),
            P(),
            P(),
            P("req", None, None),
            P("req", None, None),
            P("req", None, "tp"),
            P("req", None, "tp"),
            P("req", "tp", None),
            P("tp", "req"),
            P("tp", "req"),
            P("req", "tp"),
            P(),
        ),
        out_specs=P("req", None, "tp"),
        check_vma=False,
    )
```

```python
import math

import jax
import jax.numpy as jnp
from jax import lax
from jax.sharding import PartitionSpec as P

HD = 128
TOPK = 4
LANES = 128


NEG = -1e30
EPS = 1e-06
THETA = 1000000.0
HIGHEST = lax.Precision.HIGHEST


def rms_norm(inputs, gain_vector):
    values = inputs.astype(jnp.float32)
    scaled = values * lax.rsqrt(jnp.mean(values * values, axis=-1, keepdims=True) + EPS)
    return (scaled * gain_vector.astype(jnp.float32)).astype(jnp.bfloat16)


def rotate(values, positions):
    half_dim = values.shape[-1] // 2
    exponents = jnp.arange(half_dim, dtype=jnp.float32) * (2.0 / values.shape[-1])
    frequency = jnp.power(THETA, -exponents)
    angles = positions.astype(jnp.float32)[..., None, None] * frequency
    cosines = jnp.cos(angles)
    sine_part = jnp.sin(angles)
    front_half = values[..., :half_dim]
    back_half = values[..., half_dim:]
    return jnp.concatenate(
        [
            front_half * cosines - back_half * sine_part,
            back_half * cosines + front_half * sine_part,
        ],
        axis=-1,
    )


def shift_exchange(chunks, axis, count, spread=False):
    me = lax.axis_index(axis)
    pieces = [chunks if spread else lax.dynamic_index_in_dim(chunks, me, 0, keepdims=False)]
    for shift in range(1, count):
        send = chunks if spread else lax.dynamic_index_in_dim(
            chunks, (me + shift) % count, 0, keepdims=False
        )
        pairs = [(source, (source + shift) % count) for source in range(count)]
        pieces.append(lax.ppermute(send, axis, pairs))
    return pieces


def by_source(pieces, axis, count):
    me = lax.axis_index(axis)
    stacked = jnp.stack(pieces)
    order = (me - jnp.arange(count, dtype=jnp.int32)) % count
    return jnp.take(stacked, order, axis=0)


def bcast_a2a(values, axis, count):
    spread = jnp.broadcast_to(values[None], (count,) + values.shape)
    return lax.all_to_all(spread, axis, 0, 0, tiled=True).reshape(
        (count * values.shape[0],) + values.shape[1:]
    )


def per_device(
    tokens_in,
    attn_norm,
    qkv_weight,
    qkv_bias,
    out_weight,
    cache_keys,
    cache_values,
    page_table,
    cache_lengths,
    mlp_norm,
    routes,
    route_gates,
    expert_w_gate,
    expert_w_up,
    expert_w_down,
    shared_w_gate,
    shared_w_up,
    shared_w_down,
    shared_switch,
):
    req_rows, step_count, model_width = tokens_in.shape
    head_width = qkv_weight.shape[2]
    local_heads = head_width // HD
    req_count = lax.axis_size("req")
    tp_count = lax.axis_size("tp")
    req_index = lax.axis_index("req")
    tp_index = lax.axis_index("tp")
    all_requests = page_table.shape[0]
    pool_here = cache_keys.shape[0]
    page_len = cache_keys.shape[1]
    score_scale = 1.0 / math.sqrt(HD)
    col_share = model_width // tp_count
    row_count = req_rows * step_count
    normed = rms_norm(tokens_in, attn_norm)
    own_lengths = lax.dynamic_slice_in_dim(cache_lengths, req_index * req_rows, req_rows)
    positions = own_lengths[:, None] + jnp.arange(step_count, dtype=jnp.int32)[None, :]
    head_shape = (req_rows, step_count, local_heads, HD)

    def project(part, rows):
        return jnp.einsum(
            "rsd,df->rsf", rows, qkv_weight[:, part], preferred_element_type=jnp.float32
        ) + qkv_bias[part].astype(jnp.float32)

    query_new = rotate(project(0, normed).reshape(head_shape), positions).astype(jnp.bfloat16)
    query_spread = jnp.broadcast_to(query_new[None], (req_count,) + query_new.shape)
    normed_late, query_spread = lax.optimization_barrier((normed, query_spread))
    query_all = lax.all_to_all(query_spread, "req", 0, 0, tiled=True).reshape(
        (req_count * req_rows,) + query_new.shape[1:]
    )
    key_value = jnp.einsum(
        "rsd,dcf->rscf", normed_late, qkv_weight[:, 1:], preferred_element_type=jnp.float32
    ) + qkv_bias[1:].astype(jnp.float32)
    key_new = rotate(key_value[:, :, 0].reshape(head_shape), positions).astype(jnp.bfloat16)
    value_new = key_value[:, :, 1].reshape(head_shape).astype(jnp.bfloat16)
    slot_ids = req_index * pool_here + jnp.arange(pool_here, dtype=jnp.int32)
    matches = (page_table[:, :, None] == slot_ids[None, None, :]).astype(jnp.int32)
    request_ids = jnp.arange(all_requests, dtype=jnp.int32)
    page_ids = jnp.arange(page_table.shape[1], dtype=jnp.int32)
    owner = jnp.sum(matches * request_ids[:, None, None], axis=(0, 1))
    logical = jnp.sum(matches * page_ids[None, :, None], axis=(0, 1))
    present = jnp.sum(matches, axis=(0, 1)) > 0
    token_pos = logical[:, None] * page_len + jnp.arange(page_len, dtype=jnp.int32)[None, :]
    live = present[:, None] & (token_pos < cache_lengths[owner][:, None])
    page_queries = query_all[owner]
    page_values = cache_values.reshape(pool_here, page_len, local_heads, HD)
    head_eye = jnp.arange(local_heads)[:, None] == jnp.arange(local_heads)[None, :]
    block_queries = jnp.where(
        head_eye[None, None, :, :, None], page_queries[:, :, :, None, :], jnp.zeros((), jnp.bfloat16)
    ).reshape(pool_here, step_count * local_heads, head_width)
    scores = (
        jnp.einsum("pxd,pkd->pxk", block_queries, cache_keys, preferred_element_type=jnp.float32)
        * score_scale
    ).reshape(pool_here, step_count, local_heads, page_len)
    page_mask = live[:, None, None, :]
    masked = jnp.where(page_mask, scores, NEG)
    page_max = jnp.max(masked, axis=-1)
    weights = jnp.where(page_mask, jnp.exp(masked - page_max[..., None]), 0.0)
    page_sum = jnp.sum(weights, axis=-1)
    page_out = jnp.einsum(
        "pshk,pkhd->pshd",
        weights.astype(jnp.bfloat16),
        page_values,
        preferred_element_type=jnp.float32,
    )
    belongs = (owner[None, :] == request_ids[:, None]) & present[None, :]
    owned = belongs[:, :, None, None]
    local_max = jnp.max(jnp.where(owned, page_max[None], NEG), axis=1)
    factors = jnp.where(owned, jnp.exp(page_max[None] - local_max[:, None]), 0.0)
    local_out = jnp.einsum("rpsh,pshd->rshd", factors, page_out, precision=HIGHEST)
    local_sum = jnp.einsum("rpsh,psh->rsh", factors, page_sum, precision=HIGHEST)
    stat_width = step_count * local_heads
    stat_row = jnp.concatenate(
        [
            local_max.reshape(all_requests, stat_width),
            local_sum.reshape(all_requests, stat_width),
            jnp.zeros((all_requests, HD - 2 * stat_width), jnp.float32),
        ],
        axis=1,
    )
    packed = jnp.concatenate(
        [local_out.reshape(all_requests, stat_width, HD), stat_row[:, None, :]], axis=1
    )
    gathered = lax.all_to_all(packed, "req", 0, 0, tiled=True).reshape(
        req_count, req_rows, stat_width + 1, HD
    )
    part_out = gathered[:, :, :stat_width, :]
    part_max = gathered[:, :, stat_width, :stat_width]
    part_sum = gathered[:, :, stat_width, stat_width : 2 * stat_width]
    cache_max = jnp.max(part_max, axis=0)
    rescale = jnp.exp(part_max - cache_max[None])
    cache_out = jnp.sum(part_out * rescale[..., None], axis=0).reshape(
        req_rows, step_count, local_heads, HD
    )
    cache_sum = jnp.sum(part_sum * rescale, axis=0).reshape(req_rows, step_count, local_heads)
    cache_max = cache_max.reshape(req_rows, step_count, local_heads)
    new_scores = (
        jnp.einsum("rshd,rthd->rsht", query_new, key_new, preferred_element_type=jnp.float32)
        * score_scale
    )
    causal = jnp.arange(step_count)[:, None] >= jnp.arange(step_count)[None, :]
    new_mask = causal[None, :, None, :]
    new_masked = jnp.where(new_mask, new_scores, NEG)
    new_max = jnp.max(new_masked, axis=-1)
    new_weights = jnp.where(new_mask, jnp.exp(new_masked - new_max[..., None]), 0.0)
    new_sum = jnp.sum(new_weights, axis=-1)
    new_out = jnp.einsum(
        "rsht,rthd->rshd",
        new_weights.astype(jnp.bfloat16),
        value_new,
        preferred_element_type=jnp.float32,
    )
    top_max = jnp.maximum(cache_max, new_max)
    cache_factor = jnp.exp(cache_max - top_max)
    new_factor = jnp.exp(new_max - top_max)
    attended = (cache_out * cache_factor[..., None] + new_out * new_factor[..., None]) / (
        cache_sum * cache_factor + new_sum * new_factor
    )[..., None]
    attended = attended.astype(jnp.bfloat16).reshape(row_count, head_width)
    attn_part = jnp.dot(attended, out_weight, preferred_element_type=jnp.float32)
    attn_full = jnp.sum(
        by_source(shift_exchange(attn_part, "tp", tp_count, spread=True), "tp", tp_count), axis=0
    )
    resid = tokens_in.reshape(row_count, model_width).astype(jnp.float32) + attn_full
    mixed = rms_norm(resid, mlp_norm)
    expert_count = req_count * expert_w_gate.shape[0]
    capacity = max(2, (row_count * TOPK + expert_count - 1) // expert_count)
    picks = routes.reshape(row_count * TOPK)
    gates_flat = route_gates.reshape(row_count * TOPK)
    expert_hot = (picks[:, None] == jnp.arange(expert_count, dtype=jnp.int32)[None, :]).astype(
        jnp.int32
    )
    slot_index = jnp.sum((jnp.cumsum(expert_hot, axis=0) - 1) * expert_hot, axis=1)
    destination = picks * capacity + slot_index
    dest_hot = (
        destination[:, None] == jnp.arange(expert_count * capacity, dtype=jnp.int32)[None, :]
    ).astype(jnp.float32)
    token_hot = (
        (jnp.arange(row_count * TOPK, dtype=jnp.int32) // TOPK)[:, None]
        == jnp.arange(row_count, dtype=jnp.int32)[None, :]
    ).astype(jnp.float32)
    placement = jnp.einsum("cx,ct->xt", dest_hot, token_hot, precision=HIGHEST).astype(jnp.bfloat16)
    outgoing = jnp.dot(placement, mixed, preferred_element_type=jnp.float32).astype(jnp.bfloat16)
    combine_map = jnp.einsum(
        "ct,cx->tx", token_hot, dest_hot * gates_flat[:, None], precision=HIGHEST
    )
    w_gate_here = expert_w_gate[0]
    w_up_here = expert_w_up[0]
    w_down_here = expert_w_down[0]
    mixed_cols = lax.dynamic_slice_in_dim(mixed, tp_index * col_share, col_share, 1)
    shared_send = jnp.broadcast_to(mixed_cols[None], (req_count, row_count, col_share))
    moe_lines = capacity * model_width // LANES
    dispatch = jnp.concatenate(
        [
            outgoing.reshape(req_count, moe_lines, LANES),
            shared_send.reshape(req_count, row_count * col_share // LANES, LANES),
        ],
        axis=1,
    )
    received = lax.all_to_all(dispatch, "req", 0, 0, tiled=True)
    flat_rows = received[:, :moe_lines].reshape(req_count * capacity, model_width)
    piece = received[:, moe_lines:].reshape(req_count * row_count, col_share)
    expert_rows = req_count * capacity
    gate_part = jnp.dot(piece, shared_w_gate, preferred_element_type=jnp.float32)
    up_part = jnp.dot(piece, shared_w_up, preferred_element_type=jnp.float32)
    unit_count = shared_w_gate.shape[1]
    all_rows = req_count * row_count
    share_rows = all_rows // tp_count
    shared_pre = jnp.concatenate([gate_part, up_part], axis=1).reshape(
        tp_count, share_rows * 2 * unit_count
    )
    flat_rows, shared_pre = lax.optimization_barrier((flat_rows, shared_pre))
    gate_pre = jnp.dot(flat_rows, w_gate_here, preferred_element_type=jnp.float32)
    up_pre = jnp.dot(flat_rows, w_up_here, preferred_element_type=jnp.float32)
    hidden = (jax.nn.silu(gate_pre) * up_pre).astype(jnp.bfloat16)
    shared_sum = sum(shift_exchange(shared_pre, "tp", tp_count)).reshape(
        share_rows, 2 * unit_count
    )
    hidden, shared_sum = lax.optimization_barrier((hidden, shared_sum))
    partial_out = jnp.dot(hidden, w_down_here, preferred_element_type=jnp.float32)
    partial_split = partial_out.reshape(expert_rows, tp_count, col_share).transpose(1, 0, 2)
    expert_sum = sum(
        shift_exchange(partial_split.reshape(tp_count, expert_rows * col_share), "tp", tp_count)
    ).reshape(expert_rows, col_share)
    shared_hidden = (jax.nn.silu(shared_sum[:, :unit_count]) * shared_sum[:, unit_count:]).astype(
        jnp.bfloat16
    )
    hidden_all = by_source(
        shift_exchange(shared_hidden, "tp", tp_count, spread=True), "tp", tp_count
    ).reshape(all_rows, unit_count)
    shared_down = jnp.dot(hidden_all, shared_w_down, preferred_element_type=jnp.float32)
    ey = expert_sum.astype(jnp.bfloat16).astype(jnp.float32)
    ey_lines = capacity * col_share // LANES
    back_in = jnp.concatenate(
        [
            ey.reshape(req_count, ey_lines, LANES),
            shared_down.reshape(req_count, row_count * col_share // LANES, LANES),
        ],
        axis=1,
    )
    back = lax.all_to_all(back_in, "req", 0, 0, tiled=True)
    returned = back[:, :ey_lines].reshape(expert_count * capacity, col_share)
    shared_mine = jnp.sum(back[:, ey_lines:].reshape(req_count, row_count, col_share), axis=0)
    moe_out = jnp.dot(combine_map, returned, precision=HIGHEST)
    switch = jax.nn.sigmoid(jnp.dot(mixed, shared_switch, preferred_element_type=jnp.float32))
    resid_mine = lax.dynamic_slice_in_dim(resid, tp_index * col_share, col_share, 1)
    final = resid_mine + moe_out + switch[:, None] * shared_mine
    return final.astype(jnp.bfloat16).reshape(req_rows, step_count, col_share)


def solution(mesh):
    return jax.shard_map(
        per_device,
        mesh=mesh,
        in_specs=(
            P("req", None, None),
            P(),
            P(None, None, "tp"),
            P(None, "tp"),
            P("tp", None),
            P("req", None, "tp"),
            P("req", None, "tp"),
            P(),
            P(),
            P(),
            P("req", None, None),
            P("req", None, None),
            P("req", None, "tp"),
            P("req", None, "tp"),
            P("req", "tp", None),
            P("tp", "req"),
            P("tp", "req"),
            P("req", "tp"),
            P(),
        ),
        out_specs=P("req", None, "tp"),
        check_vma=False,
    )
```

```python
import math

import jax
import jax.numpy as jnp
from jax import lax
from jax.sharding import PartitionSpec as P

HD = 128
TOPK = 4
LANES = 128


NEG = -1e30
EPS = 1e-06
THETA = 1000000.0
HIGHEST = lax.Precision.HIGHEST


def rms_norm(inputs, gain_vector):
    values = inputs.astype(jnp.float32)
    scaled = values * lax.rsqrt(jnp.mean(values * values, axis=-1, keepdims=True) + EPS)
    return (scaled * gain_vector.astype(jnp.float32)).astype(jnp.bfloat16)


def rotate(values, positions):
    half_dim = values.shape[-1] // 2
    exponents = jnp.arange(half_dim, dtype=jnp.float32) * (2.0 / values.shape[-1])
    frequency = jnp.power(THETA, -exponents)
    angles = positions.astype(jnp.float32)[..., None, None] * frequency
    cosines = jnp.cos(angles)
    sine_part = jnp.sin(angles)
    front_half = values[..., :half_dim]
    back_half = values[..., half_dim:]
    return jnp.concatenate(
        [
            front_half * cosines - back_half * sine_part,
            back_half * cosines + front_half * sine_part,
        ],
        axis=-1,
    )


def shift_exchange(chunks, axis, count, spread=False):
    me = lax.axis_index(axis)
    pieces = [chunks if spread else lax.dynamic_index_in_dim(chunks, me, 0, keepdims=False)]
    for shift in range(1, count):
        send = chunks if spread else lax.dynamic_index_in_dim(
            chunks, (me + shift) % count, 0, keepdims=False
        )
        pairs = [(source, (source + shift) % count) for source in range(count)]
        pieces.append(lax.ppermute(send, axis, pairs))
    return pieces


def by_source(pieces, axis, count):
    me = lax.axis_index(axis)
    stacked = jnp.stack(pieces)
    order = (me - jnp.arange(count, dtype=jnp.int32)) % count
    return jnp.take(stacked, order, axis=0)


def bcast_a2a(values, axis, count):
    spread = jnp.broadcast_to(values[None], (count,) + values.shape)
    return lax.all_to_all(spread, axis, 0, 0, tiled=True).reshape(
        (count * values.shape[0],) + values.shape[1:]
    )


def per_device(
    tokens_in,
    attn_norm,
    qkv_weight,
    qkv_bias,
    out_weight,
    cache_keys,
    cache_values,
    page_table,
    cache_lengths,
    mlp_norm,
    routes,
    route_gates,
    expert_w_gate,
    expert_w_up,
    expert_w_down,
    shared_w_gate,
    shared_w_up,
    shared_w_down,
    shared_switch,
):
    req_rows, step_count, model_width = tokens_in.shape
    head_width = qkv_weight.shape[2]
    local_heads = head_width // HD
    req_count = lax.axis_size("req")
    tp_count = lax.axis_size("tp")
    req_index = lax.axis_index("req")
    tp_index = lax.axis_index("tp")
    all_requests = page_table.shape[0]
    pool_here = cache_keys.shape[0]
    page_len = cache_keys.shape[1]
    score_scale = 1.0 / math.sqrt(HD)
    col_share = model_width // tp_count
    row_count = req_rows * step_count
    normed = rms_norm(tokens_in, attn_norm)
    own_lengths = lax.dynamic_slice_in_dim(cache_lengths, req_index * req_rows, req_rows)
    positions = own_lengths[:, None] + jnp.arange(step_count, dtype=jnp.int32)[None, :]
    head_shape = (req_rows, step_count, local_heads, HD)

    def project(part, rows):
        return jnp.einsum(
            "rsd,df->rsf", rows, qkv_weight[:, part], preferred_element_type=jnp.float32
        ) + qkv_bias[part].astype(jnp.float32)

    query_new = rotate(project(0, normed).reshape(head_shape), positions).astype(jnp.bfloat16)
    query_spread = jnp.broadcast_to(query_new[None], (req_count,) + query_new.shape)
    normed_late, query_spread = lax.optimization_barrier((normed, query_spread))
    query_all = lax.all_to_all(query_spread, "req", 0, 0, tiled=True).reshape(
        (req_count * req_rows,) + query_new.shape[1:]
    )
    key_value = jnp.einsum(
        "rsd,dcf->rscf", normed_late, qkv_weight[:, 1:], preferred_element_type=jnp.float32
    ) + qkv_bias[1:].astype(jnp.float32)
    key_new = rotate(key_value[:, :, 0].reshape(head_shape), positions).astype(jnp.bfloat16)
    value_new = key_value[:, :, 1].reshape(head_shape).astype(jnp.bfloat16)
    slot_ids = req_index * pool_here + jnp.arange(pool_here, dtype=jnp.int32)
    matches = (page_table[:, :, None] == slot_ids[None, None, :]).astype(jnp.int32)
    request_ids = jnp.arange(all_requests, dtype=jnp.int32)
    page_ids = jnp.arange(page_table.shape[1], dtype=jnp.int32)
    owner = jnp.sum(matches * request_ids[:, None, None], axis=(0, 1))
    logical = jnp.sum(matches * page_ids[None, :, None], axis=(0, 1))
    present = jnp.sum(matches, axis=(0, 1)) > 0
    token_pos = logical[:, None] * page_len + jnp.arange(page_len, dtype=jnp.int32)[None, :]
    live = present[:, None] & (token_pos < cache_lengths[owner][:, None])
    page_queries = query_all[owner]
    page_values = cache_values.reshape(pool_here, page_len, local_heads, HD)
    head_eye = jnp.arange(local_heads)[:, None] == jnp.arange(local_heads)[None, :]
    block_queries = jnp.where(
        head_eye[None, None, :, :, None], page_queries[:, :, :, None, :], jnp.zeros((), jnp.bfloat16)
    ).reshape(pool_here, step_count * local_heads, head_width)
    scores = (
        jnp.einsum("pxd,pkd->pxk", block_queries, cache_keys, preferred_element_type=jnp.float32)
        * score_scale
    ).reshape(pool_here, step_count, local_heads, page_len)
    page_mask = live[:, None, None, :]
    masked = jnp.where(page_mask, scores, NEG)
    page_max = jnp.max(masked, axis=-1)
    weights = jnp.where(page_mask, jnp.exp(masked - page_max[..., None]), 0.0)
    page_sum = jnp.sum(weights, axis=-1)
    page_out = jnp.einsum(
        "pshk,pkhd->pshd",
        weights.astype(jnp.bfloat16),
        page_values,
        preferred_element_type=jnp.float32,
    )
    belongs = (owner[None, :] == request_ids[:, None]) & present[None, :]
    owned = belongs[:, :, None, None]
    local_max = jnp.max(jnp.where(owned, page_max[None], NEG), axis=1)
    factors = jnp.where(owned, jnp.exp(page_max[None] - local_max[:, None]), 0.0)
    local_out = jnp.einsum("rpsh,pshd->rshd", factors, page_out, precision=HIGHEST)
    local_sum = jnp.einsum("rpsh,psh->rsh", factors, page_sum, precision=HIGHEST)
    stat_width = step_count * local_heads
    stat_row = jnp.concatenate(
        [
            local_max.reshape(all_requests, stat_width),
            local_sum.reshape(all_requests, stat_width),
            jnp.zeros((all_requests, HD - 2 * stat_width), jnp.float32),
        ],
        axis=1,
    )
    packed = jnp.concatenate(
        [local_out.reshape(all_requests, stat_width, HD), stat_row[:, None, :]], axis=1
    )
    gathered = lax.all_to_all(packed, "req", 0, 0, tiled=True).reshape(
        req_count, req_rows, stat_width + 1, HD
    )
    part_out = gathered[:, :, :stat_width, :]
    part_max = gathered[:, :, stat_width, :stat_width]
    part_sum = gathered[:, :, stat_width, stat_width : 2 * stat_width]
    cache_max = jnp.max(part_max, axis=0)
    rescale = jnp.exp(part_max - cache_max[None])
    cache_out = jnp.sum(part_out * rescale[..., None], axis=0).reshape(
        req_rows, step_count, local_heads, HD
    )
    cache_sum = jnp.sum(part_sum * rescale, axis=0).reshape(req_rows, step_count, local_heads)
    cache_max = cache_max.reshape(req_rows, step_count, local_heads)
    new_scores = (
        jnp.einsum("rshd,rthd->rsht", query_new, key_new, preferred_element_type=jnp.float32)
        * score_scale
    )
    causal = jnp.arange(step_count)[:, None] >= jnp.arange(step_count)[None, :]
    new_mask = causal[None, :, None, :]
    new_masked = jnp.where(new_mask, new_scores, NEG)
    new_max = jnp.max(new_masked, axis=-1)
    new_weights = jnp.where(new_mask, jnp.exp(new_masked - new_max[..., None]), 0.0)
    new_sum = jnp.sum(new_weights, axis=-1)
    new_out = jnp.einsum(
        "rsht,rthd->rshd",
        new_weights.astype(jnp.bfloat16),
        value_new,
        preferred_element_type=jnp.float32,
    )
    top_max = jnp.maximum(cache_max, new_max)
    cache_factor = jnp.exp(cache_max - top_max)
    new_factor = jnp.exp(new_max - top_max)
    attended = (cache_out * cache_factor[..., None] + new_out * new_factor[..., None]) / (
        cache_sum * cache_factor + new_sum * new_factor
    )[..., None]
    attended = attended.astype(jnp.bfloat16).reshape(row_count, head_width)
    attn_part = jnp.dot(attended, out_weight, preferred_element_type=jnp.float32)
    attn_full = jnp.sum(
        by_source(shift_exchange(attn_part, "tp", tp_count, spread=True), "tp", tp_count), axis=0
    )
    resid = tokens_in.reshape(row_count, model_width).astype(jnp.float32) + attn_full
    mixed = rms_norm(resid, mlp_norm)
    expert_count = req_count * expert_w_gate.shape[0]
    capacity = max(2, (row_count * TOPK + expert_count - 1) // expert_count)
    picks = routes.reshape(row_count * TOPK)
    gates_flat = route_gates.reshape(row_count * TOPK)
    expert_hot = (picks[:, None] == jnp.arange(expert_count, dtype=jnp.int32)[None, :]).astype(
        jnp.int32
    )
    slot_index = jnp.sum((jnp.cumsum(expert_hot, axis=0) - 1) * expert_hot, axis=1)
    destination = picks * capacity + slot_index
    dest_hot = (
        destination[:, None] == jnp.arange(expert_count * capacity, dtype=jnp.int32)[None, :]
    ).astype(jnp.float32)
    token_hot = (
        (jnp.arange(row_count * TOPK, dtype=jnp.int32) // TOPK)[:, None]
        == jnp.arange(row_count, dtype=jnp.int32)[None, :]
    ).astype(jnp.float32)
    placement = jnp.einsum("cx,ct->xt", dest_hot, token_hot, precision=HIGHEST).astype(jnp.bfloat16)
    outgoing = jnp.dot(placement, mixed, preferred_element_type=jnp.float32).astype(jnp.bfloat16)
    combine_map = jnp.einsum(
        "ct,cx->tx", token_hot, dest_hot * gates_flat[:, None], precision=HIGHEST
    )
    w_gate_here = expert_w_gate[0]
    w_up_here = expert_w_up[0]
    w_down_here = expert_w_down[0]
    mixed_cols = lax.dynamic_slice_in_dim(mixed, tp_index * col_share, col_share, 1)
    shared_send = jnp.broadcast_to(mixed_cols[None], (req_count, row_count, col_share))
    moe_lines = capacity * model_width // LANES
    dispatch = jnp.concatenate(
        [
            outgoing.reshape(req_count, moe_lines, LANES),
            shared_send.reshape(req_count, row_count * col_share // LANES, LANES),
        ],
        axis=1,
    )
    received = lax.all_to_all(dispatch, "req", 0, 0, tiled=True)
    flat_rows = received[:, :moe_lines].reshape(req_count * capacity, model_width)
    piece = received[:, moe_lines:].reshape(req_count * row_count, col_share)
    expert_rows = req_count * capacity
    gate_part = jnp.dot(piece, shared_w_gate, preferred_element_type=jnp.float32)
    up_part = jnp.dot(piece, shared_w_up, preferred_element_type=jnp.float32)
    unit_count = shared_w_gate.shape[1]
    all_rows = req_count * row_count
    share_rows = all_rows // tp_count
    shared_pre = jnp.concatenate([gate_part, up_part], axis=1).reshape(
        tp_count, share_rows * 2 * unit_count
    )
    flat_rows, shared_pre = lax.optimization_barrier((flat_rows, shared_pre))
    gate_pre = jnp.dot(flat_rows, w_gate_here, preferred_element_type=jnp.float32)
    up_pre = jnp.dot(flat_rows, w_up_here, preferred_element_type=jnp.float32)
    hidden = (jax.nn.silu(gate_pre) * up_pre).astype(jnp.bfloat16)
    shared_sum = sum(shift_exchange(shared_pre, "tp", tp_count)).reshape(
        share_rows, 2 * unit_count
    )
    partial_out = jnp.dot(hidden, w_down_here, preferred_element_type=jnp.float32)
    partial_out, shared_sum = lax.optimization_barrier((partial_out, shared_sum))
    partial_split = partial_out.reshape(expert_rows, tp_count, col_share).transpose(1, 0, 2)
    expert_sum = sum(
        shift_exchange(partial_split.reshape(tp_count, expert_rows * col_share), "tp", tp_count)
    ).reshape(expert_rows, col_share)
    shared_hidden = (jax.nn.silu(shared_sum[:, :unit_count]) * shared_sum[:, unit_count:]).astype(
        jnp.bfloat16
    )
    hidden_all = by_source(
        shift_exchange(shared_hidden, "tp", tp_count, spread=True), "tp", tp_count
    ).reshape(all_rows, unit_count)
    shared_down = jnp.dot(hidden_all, shared_w_down, preferred_element_type=jnp.float32)
    ey = expert_sum.astype(jnp.bfloat16).astype(jnp.float32)
    ey_lines = capacity * col_share // LANES
    back_in = jnp.concatenate(
        [
            ey.reshape(req_count, ey_lines, LANES),
            shared_down.reshape(req_count, row_count * col_share // LANES, LANES),
        ],
        axis=1,
    )
    back = lax.all_to_all(back_in, "req", 0, 0, tiled=True)
    returned = back[:, :ey_lines].reshape(expert_count * capacity, col_share)
    shared_mine = jnp.sum(back[:, ey_lines:].reshape(req_count, row_count, col_share), axis=0)
    moe_out = jnp.dot(combine_map, returned, precision=HIGHEST)
    switch = jax.nn.sigmoid(jnp.dot(mixed, shared_switch, preferred_element_type=jnp.float32))
    resid_mine = lax.dynamic_slice_in_dim(resid, tp_index * col_share, col_share, 1)
    final = resid_mine + moe_out + switch[:, None] * shared_mine
    return final.astype(jnp.bfloat16).reshape(req_rows, step_count, col_share)


def solution(mesh):
    return jax.shard_map(
        per_device,
        mesh=mesh,
        in_specs=(
            P("req", None, None),
            P(),
            P(None, None, "tp"),
            P(None, "tp"),
            P("tp", None),
            P("req", None, "tp"),
            P("req", None, "tp"),
            P(),
            P(),
            P(),
            P("req", None, None),
            P("req", None, None),
            P("req", None, "tp"),
            P("req", None, "tp"),
            P("req", "tp", None),
            P("tp", "req"),
            P("tp", "req"),
            P("req", "tp"),
            P(),
        ),
        out_specs=P("req", None, "tp"),
        check_vma=False,
    )
```

```python
import math

import jax
import jax.numpy as jnp
from jax import lax
from jax.sharding import PartitionSpec as P

HD = 128
TOPK = 4
LANES = 128


NEG = -1e30
EPS = 1e-06
THETA = 1000000.0
HIGHEST = lax.Precision.HIGHEST


def rms_norm(inputs, gain_vector):
    values = inputs.astype(jnp.float32)
    scaled = values * lax.rsqrt(jnp.mean(values * values, axis=-1, keepdims=True) + EPS)
    return (scaled * gain_vector.astype(jnp.float32)).astype(jnp.bfloat16)


def rotate(values, positions):
    half_dim = values.shape[-1] // 2
    exponents = jnp.arange(half_dim, dtype=jnp.float32) * (2.0 / values.shape[-1])
    frequency = jnp.power(THETA, -exponents)
    angles = positions.astype(jnp.float32)[..., None, None] * frequency
    cosines = jnp.cos(angles)
    sine_part = jnp.sin(angles)
    front_half = values[..., :half_dim]
    back_half = values[..., half_dim:]
    return jnp.concatenate(
        [
            front_half * cosines - back_half * sine_part,
            back_half * cosines + front_half * sine_part,
        ],
        axis=-1,
    )


def shift_exchange(chunks, axis, count, spread=False):
    me = lax.axis_index(axis)
    pieces = [chunks if spread else lax.dynamic_index_in_dim(chunks, me, 0, keepdims=False)]
    for shift in range(1, count):
        send = chunks if spread else lax.dynamic_index_in_dim(
            chunks, (me + shift) % count, 0, keepdims=False
        )
        pairs = [(source, (source + shift) % count) for source in range(count)]
        pieces.append(lax.ppermute(send, axis, pairs))
    return pieces


def by_source(pieces, axis, count):
    me = lax.axis_index(axis)
    stacked = jnp.stack(pieces)
    order = (me - jnp.arange(count, dtype=jnp.int32)) % count
    return jnp.take(stacked, order, axis=0)


def bcast_a2a(values, axis, count):
    spread = jnp.broadcast_to(values[None], (count,) + values.shape)
    return lax.all_to_all(spread, axis, 0, 0, tiled=True).reshape(
        (count * values.shape[0],) + values.shape[1:]
    )


def per_device(
    tokens_in,
    attn_norm,
    qkv_weight,
    qkv_bias,
    out_weight,
    cache_keys,
    cache_values,
    page_table,
    cache_lengths,
    mlp_norm,
    routes,
    route_gates,
    expert_w_gate,
    expert_w_up,
    expert_w_down,
    shared_w_gate,
    shared_w_up,
    shared_w_down,
    shared_switch,
):
    req_rows, step_count, model_width = tokens_in.shape
    head_width = qkv_weight.shape[2]
    local_heads = head_width // HD
    req_count = lax.axis_size("req")
    tp_count = lax.axis_size("tp")
    req_index = lax.axis_index("req")
    tp_index = lax.axis_index("tp")
    all_requests = page_table.shape[0]
    pool_here = cache_keys.shape[0]
    page_len = cache_keys.shape[1]
    score_scale = 1.0 / math.sqrt(HD)
    col_share = model_width // tp_count
    row_count = req_rows * step_count
    normed = rms_norm(tokens_in, attn_norm)
    own_lengths = lax.dynamic_slice_in_dim(cache_lengths, req_index * req_rows, req_rows)
    positions = own_lengths[:, None] + jnp.arange(step_count, dtype=jnp.int32)[None, :]
    head_shape = (req_rows, step_count, local_heads, HD)

    tokens_all = bcast_a2a(tokens_in, "req", req_count)
    normed_all = rms_norm(tokens_all, attn_norm)
    query_proj = jnp.einsum(
        "rsd,df->rsf", normed_all, qkv_weight[:, 0], preferred_element_type=jnp.float32
    ) + qkv_bias[0].astype(jnp.float32)
    all_positions = cache_lengths[:, None] + jnp.arange(step_count, dtype=jnp.int32)[None, :]
    query_all = rotate(
        query_proj.reshape(all_requests, step_count, local_heads, HD), all_positions
    ).astype(jnp.bfloat16)
    query_new = lax.dynamic_slice_in_dim(query_all, req_index * req_rows, req_rows)
    normed_late = normed
    key_value = jnp.einsum(
        "rsd,dcf->rscf", normed_late, qkv_weight[:, 1:], preferred_element_type=jnp.float32
    ) + qkv_bias[1:].astype(jnp.float32)
    key_new = rotate(key_value[:, :, 0].reshape(head_shape), positions).astype(jnp.bfloat16)
    value_new = key_value[:, :, 1].reshape(head_shape).astype(jnp.bfloat16)
    slot_ids = req_index * pool_here + jnp.arange(pool_here, dtype=jnp.int32)
    matches = (page_table[:, :, None] == slot_ids[None, None, :]).astype(jnp.int32)
    request_ids = jnp.arange(all_requests, dtype=jnp.int32)
    page_ids = jnp.arange(page_table.shape[1], dtype=jnp.int32)
    owner = jnp.sum(matches * request_ids[:, None, None], axis=(0, 1))
    logical = jnp.sum(matches * page_ids[None, :, None], axis=(0, 1))
    present = jnp.sum(matches, axis=(0, 1)) > 0
    token_pos = logical[:, None] * page_len + jnp.arange(page_len, dtype=jnp.int32)[None, :]
    live = present[:, None] & (token_pos < cache_lengths[owner][:, None])
    page_queries = query_all[owner]
    page_values = cache_values.reshape(pool_here, page_len, local_heads, HD)
    head_eye = jnp.arange(local_heads)[:, None] == jnp.arange(local_heads)[None, :]
    block_queries = jnp.where(
        head_eye[None, None, :, :, None], page_queries[:, :, :, None, :], jnp.zeros((), jnp.bfloat16)
    ).reshape(pool_here, step_count * local_heads, head_width)
    scores = (
        jnp.einsum("pxd,pkd->pxk", block_queries, cache_keys, preferred_element_type=jnp.float32)
        * score_scale
    ).reshape(pool_here, step_count, local_heads, page_len)
    page_mask = live[:, None, None, :]
    masked = jnp.where(page_mask, scores, NEG)
    page_max = jnp.max(masked, axis=-1)
    weights = jnp.where(page_mask, jnp.exp(masked - page_max[..., None]), 0.0)
    page_sum = jnp.sum(weights, axis=-1)
    page_out = jnp.einsum(
        "pshk,pkhd->pshd",
        weights.astype(jnp.bfloat16),
        page_values,
        preferred_element_type=jnp.float32,
    )
    belongs = (owner[None, :] == request_ids[:, None]) & present[None, :]
    owned = belongs[:, :, None, None]
    local_max = jnp.max(jnp.where(owned, page_max[None], NEG), axis=1)
    factors = jnp.where(owned, jnp.exp(page_max[None] - local_max[:, None]), 0.0)
    local_out = jnp.einsum("rpsh,pshd->rshd", factors, page_out, precision=HIGHEST)
    local_sum = jnp.einsum("rpsh,psh->rsh", factors, page_sum, precision=HIGHEST)
    stat_width = step_count * local_heads
    stat_row = jnp.concatenate(
        [
            local_max.reshape(all_requests, stat_width),
            local_sum.reshape(all_requests, stat_width),
            jnp.zeros((all_requests, HD - 2 * stat_width), jnp.float32),
        ],
        axis=1,
    )
    packed = jnp.concatenate(
        [local_out.reshape(all_requests, stat_width, HD), stat_row[:, None, :]], axis=1
    )
    gathered = lax.all_to_all(packed, "req", 0, 0, tiled=True).reshape(
        req_count, req_rows, stat_width + 1, HD
    )
    part_out = gathered[:, :, :stat_width, :]
    part_max = gathered[:, :, stat_width, :stat_width]
    part_sum = gathered[:, :, stat_width, stat_width : 2 * stat_width]
    cache_max = jnp.max(part_max, axis=0)
    rescale = jnp.exp(part_max - cache_max[None])
    cache_out = jnp.sum(part_out * rescale[..., None], axis=0).reshape(
        req_rows, step_count, local_heads, HD
    )
    cache_sum = jnp.sum(part_sum * rescale, axis=0).reshape(req_rows, step_count, local_heads)
    cache_max = cache_max.reshape(req_rows, step_count, local_heads)
    new_scores = (
        jnp.einsum("rshd,rthd->rsht", query_new, key_new, preferred_element_type=jnp.float32)
        * score_scale
    )
    causal = jnp.arange(step_count)[:, None] >= jnp.arange(step_count)[None, :]
    new_mask = causal[None, :, None, :]
    new_masked = jnp.where(new_mask, new_scores, NEG)
    new_max = jnp.max(new_masked, axis=-1)
    new_weights = jnp.where(new_mask, jnp.exp(new_masked - new_max[..., None]), 0.0)
    new_sum = jnp.sum(new_weights, axis=-1)
    new_out = jnp.einsum(
        "rsht,rthd->rshd",
        new_weights.astype(jnp.bfloat16),
        value_new,
        preferred_element_type=jnp.float32,
    )
    top_max = jnp.maximum(cache_max, new_max)
    cache_factor = jnp.exp(cache_max - top_max)
    new_factor = jnp.exp(new_max - top_max)
    attended = (cache_out * cache_factor[..., None] + new_out * new_factor[..., None]) / (
        cache_sum * cache_factor + new_sum * new_factor
    )[..., None]
    attended = attended.astype(jnp.bfloat16).reshape(row_count, head_width)
    attn_part = jnp.dot(attended, out_weight, preferred_element_type=jnp.float32)
    attn_full = jnp.sum(
        by_source(shift_exchange(attn_part, "tp", tp_count, spread=True), "tp", tp_count), axis=0
    )
    resid = tokens_in.reshape(row_count, model_width).astype(jnp.float32) + attn_full
    mixed = rms_norm(resid, mlp_norm)
    expert_count = req_count * expert_w_gate.shape[0]
    capacity = max(2, (row_count * TOPK + expert_count - 1) // expert_count)
    picks = routes.reshape(row_count * TOPK)
    gates_flat = route_gates.reshape(row_count * TOPK)
    expert_hot = (picks[:, None] == jnp.arange(expert_count, dtype=jnp.int32)[None, :]).astype(
        jnp.int32
    )
    slot_index = jnp.sum((jnp.cumsum(expert_hot, axis=0) - 1) * expert_hot, axis=1)
    destination = picks * capacity + slot_index
    dest_hot = (
        destination[:, None] == jnp.arange(expert_count * capacity, dtype=jnp.int32)[None, :]
    ).astype(jnp.float32)
    token_hot = (
        (jnp.arange(row_count * TOPK, dtype=jnp.int32) // TOPK)[:, None]
        == jnp.arange(row_count, dtype=jnp.int32)[None, :]
    ).astype(jnp.float32)
    placement = jnp.einsum("cx,ct->xt", dest_hot, token_hot, precision=HIGHEST).astype(jnp.bfloat16)
    outgoing = jnp.dot(placement, mixed, preferred_element_type=jnp.float32).astype(jnp.bfloat16)
    combine_map = jnp.einsum(
        "ct,cx->tx", token_hot, dest_hot * gates_flat[:, None], precision=HIGHEST
    )
    w_gate_here = expert_w_gate[0]
    w_up_here = expert_w_up[0]
    w_down_here = expert_w_down[0]
    mixed_cols = lax.dynamic_slice_in_dim(mixed, tp_index * col_share, col_share, 1)
    shared_send = jnp.broadcast_to(mixed_cols[None], (req_count, row_count, col_share))
    moe_lines = capacity * model_width // LANES
    dispatch = jnp.concatenate(
        [
            outgoing.reshape(req_count, moe_lines, LANES),
            shared_send.reshape(req_count, row_count * col_share // LANES, LANES),
        ],
        axis=1,
    )
    received = lax.all_to_all(dispatch, "req", 0, 0, tiled=True)
    flat_rows = received[:, :moe_lines].reshape(req_count * capacity, model_width)
    piece = received[:, moe_lines:].reshape(req_count * row_count, col_share)
    expert_rows = req_count * capacity
    gate_part = jnp.dot(piece, shared_w_gate, preferred_element_type=jnp.float32)
    up_part = jnp.dot(piece, shared_w_up, preferred_element_type=jnp.float32)
    unit_count = shared_w_gate.shape[1]
    all_rows = req_count * row_count
    share_rows = all_rows // tp_count
    shared_pre = jnp.concatenate([gate_part, up_part], axis=1).reshape(
        tp_count, share_rows * 2 * unit_count
    )
    flat_rows, shared_pre = lax.optimization_barrier((flat_rows, shared_pre))
    gate_pre = jnp.dot(flat_rows, w_gate_here, preferred_element_type=jnp.float32)
    up_pre = jnp.dot(flat_rows, w_up_here, preferred_element_type=jnp.float32)
    hidden = (jax.nn.silu(gate_pre) * up_pre).astype(jnp.bfloat16)
    shared_sum = sum(shift_exchange(shared_pre, "tp", tp_count)).reshape(
        share_rows, 2 * unit_count
    )
    partial_out = jnp.dot(hidden, w_down_here, preferred_element_type=jnp.float32)
    partial_out, shared_sum = lax.optimization_barrier((partial_out, shared_sum))
    partial_split = partial_out.reshape(expert_rows, tp_count, col_share).transpose(1, 0, 2)
    expert_sum = sum(
        shift_exchange(partial_split.reshape(tp_count, expert_rows * col_share), "tp", tp_count)
    ).reshape(expert_rows, col_share)
    shared_hidden = (jax.nn.silu(shared_sum[:, :unit_count]) * shared_sum[:, unit_count:]).astype(
        jnp.bfloat16
    )
    hidden_all = by_source(
        shift_exchange(shared_hidden, "tp", tp_count, spread=True), "tp", tp_count
    ).reshape(all_rows, unit_count)
    shared_down = jnp.dot(hidden_all, shared_w_down, preferred_element_type=jnp.float32)
    ey = expert_sum.astype(jnp.bfloat16).astype(jnp.float32)
    ey_lines = capacity * col_share // LANES
    back_in = jnp.concatenate(
        [
            ey.reshape(req_count, ey_lines, LANES),
            shared_down.reshape(req_count, row_count * col_share // LANES, LANES),
        ],
        axis=1,
    )
    back = lax.all_to_all(back_in, "req", 0, 0, tiled=True)
    returned = back[:, :ey_lines].reshape(expert_count * capacity, col_share)
    shared_mine = jnp.sum(back[:, ey_lines:].reshape(req_count, row_count, col_share), axis=0)
    moe_out = jnp.dot(combine_map, returned, precision=HIGHEST)
    switch = jax.nn.sigmoid(jnp.dot(mixed, shared_switch, preferred_element_type=jnp.float32))
    resid_mine = lax.dynamic_slice_in_dim(resid, tp_index * col_share, col_share, 1)
    final = resid_mine + moe_out + switch[:, None] * shared_mine
    return final.astype(jnp.bfloat16).reshape(req_rows, step_count, col_share)


def solution(mesh):
    return jax.shard_map(
        per_device,
        mesh=mesh,
        in_specs=(
            P("req", None, None),
            P(),
            P(None, None, "tp"),
            P(None, "tp"),
            P("tp", None),
            P("req", None, "tp"),
            P("req", None, "tp"),
            P(),
            P(),
            P(),
            P("req", None, None),
            P("req", None, None),
            P("req", None, "tp"),
            P("req", None, "tp"),
            P("req", "tp", None),
            P("tp", "req"),
            P("tp", "req"),
            P("req", "tp"),
            P(),
        ),
        out_specs=P("req", None, "tp"),
        check_vma=False,
    )
```

```python
import math

import jax
import jax.numpy as jnp
from jax import lax
from jax.sharding import PartitionSpec as P

HD = 128
TOPK = 4
LANES = 128


NEG = -1e30
EPS = 1e-06
THETA = 1000000.0
HIGHEST = lax.Precision.HIGHEST


def rms_norm(inputs, gain_vector):
    values = inputs.astype(jnp.float32)
    scaled = values * lax.rsqrt(jnp.mean(values * values, axis=-1, keepdims=True) + EPS)
    return (scaled * gain_vector.astype(jnp.float32)).astype(jnp.bfloat16)


def rotate(values, positions):
    half_dim = values.shape[-1] // 2
    exponents = jnp.arange(half_dim, dtype=jnp.float32) * (2.0 / values.shape[-1])
    frequency = jnp.power(THETA, -exponents)
    angles = positions.astype(jnp.float32)[..., None, None] * frequency
    cosines = jnp.cos(angles)
    sine_part = jnp.sin(angles)
    front_half = values[..., :half_dim]
    back_half = values[..., half_dim:]
    return jnp.concatenate(
        [
            front_half * cosines - back_half * sine_part,
            back_half * cosines + front_half * sine_part,
        ],
        axis=-1,
    )


def shift_exchange(chunks, axis, count, spread=False):
    me = lax.axis_index(axis)
    pieces = [chunks if spread else lax.dynamic_index_in_dim(chunks, me, 0, keepdims=False)]
    for shift in range(1, count):
        send = chunks if spread else lax.dynamic_index_in_dim(
            chunks, (me + shift) % count, 0, keepdims=False
        )
        pairs = [(source, (source + shift) % count) for source in range(count)]
        pieces.append(lax.ppermute(send, axis, pairs))
    return pieces


def by_source(pieces, axis, count):
    me = lax.axis_index(axis)
    stacked = jnp.stack(pieces)
    order = (me - jnp.arange(count, dtype=jnp.int32)) % count
    return jnp.take(stacked, order, axis=0)


def bcast_a2a(values, axis, count):
    spread = jnp.broadcast_to(values[None], (count,) + values.shape)
    return lax.all_to_all(spread, axis, 0, 0, tiled=True).reshape(
        (count * values.shape[0],) + values.shape[1:]
    )


def per_device(
    tokens_in,
    attn_norm,
    qkv_weight,
    qkv_bias,
    out_weight,
    cache_keys,
    cache_values,
    page_table,
    cache_lengths,
    mlp_norm,
    routes,
    route_gates,
    expert_w_gate,
    expert_w_up,
    expert_w_down,
    shared_w_gate,
    shared_w_up,
    shared_w_down,
    shared_switch,
):
    req_rows, step_count, model_width = tokens_in.shape
    head_width = qkv_weight.shape[2]
    local_heads = head_width // HD
    req_count = lax.axis_size("req")
    tp_count = lax.axis_size("tp")
    req_index = lax.axis_index("req")
    tp_index = lax.axis_index("tp")
    all_requests = page_table.shape[0]
    pool_here = cache_keys.shape[0]
    page_len = cache_keys.shape[1]
    score_scale = 1.0 / math.sqrt(HD)
    col_share = model_width // tp_count
    row_count = req_rows * step_count
    normed = rms_norm(tokens_in, attn_norm)
    own_lengths = lax.dynamic_slice_in_dim(cache_lengths, req_index * req_rows, req_rows)
    positions = own_lengths[:, None] + jnp.arange(step_count, dtype=jnp.int32)[None, :]
    head_shape = (req_rows, step_count, local_heads, HD)

    def project(part, rows):
        return jnp.einsum(
            "rsd,df->rsf", rows, qkv_weight[:, part], preferred_element_type=jnp.float32
        ) + qkv_bias[part].astype(jnp.float32)

    query_new = rotate(project(0, normed).reshape(head_shape), positions).astype(jnp.bfloat16)
    query_spread = jnp.broadcast_to(query_new[None], (req_count,) + query_new.shape)
    normed_late, query_spread = lax.optimization_barrier((normed, query_spread))
    query_all = lax.all_to_all(query_spread, "req", 0, 0, tiled=True).reshape(
        (req_count * req_rows,) + query_new.shape[1:]
    )
    key_value = jnp.einsum(
        "rsd,dcf->rscf", normed_late, qkv_weight[:, 1:], preferred_element_type=jnp.float32
    ) + qkv_bias[1:].astype(jnp.float32)
    key_new = rotate(key_value[:, :, 0].reshape(head_shape), positions).astype(jnp.bfloat16)
    value_new = key_value[:, :, 1].reshape(head_shape).astype(jnp.bfloat16)
    slot_ids = req_index * pool_here + jnp.arange(pool_here, dtype=jnp.int32)
    matches = (page_table[:, :, None] == slot_ids[None, None, :]).astype(jnp.int32)
    request_ids = jnp.arange(all_requests, dtype=jnp.int32)
    page_ids = jnp.arange(page_table.shape[1], dtype=jnp.int32)
    owner = jnp.sum(matches * request_ids[:, None, None], axis=(0, 1))
    logical = jnp.sum(matches * page_ids[None, :, None], axis=(0, 1))
    present = jnp.sum(matches, axis=(0, 1)) > 0
    token_pos = logical[:, None] * page_len + jnp.arange(page_len, dtype=jnp.int32)[None, :]
    live = present[:, None] & (token_pos < cache_lengths[owner][:, None])
    page_queries = query_all[owner]
    page_values = cache_values.reshape(pool_here, page_len, local_heads, HD)
    head_eye = jnp.arange(local_heads)[:, None] == jnp.arange(local_heads)[None, :]
    block_queries = jnp.where(
        head_eye[None, None, :, :, None], page_queries[:, :, :, None, :], jnp.zeros((), jnp.bfloat16)
    ).reshape(pool_here, step_count * local_heads, head_width)
    scores = (
        jnp.einsum("pxd,pkd->pxk", block_queries, cache_keys, preferred_element_type=jnp.float32)
        * score_scale
    ).reshape(pool_here, step_count, local_heads, page_len)
    page_mask = live[:, None, None, :]
    masked = jnp.where(page_mask, scores, NEG)
    page_max = jnp.max(masked, axis=-1)
    weights = jnp.where(page_mask, jnp.exp(masked - page_max[..., None]), 0.0)
    page_sum = jnp.sum(weights, axis=-1)
    page_out = jnp.einsum(
        "pshk,pkhd->pshd",
        weights.astype(jnp.bfloat16),
        page_values,
        preferred_element_type=jnp.float32,
    )
    belongs = (owner[None, :] == request_ids[:, None]) & present[None, :]
    owned = belongs[:, :, None, None]
    local_max = jnp.max(jnp.where(owned, page_max[None], NEG), axis=1)
    factors = jnp.where(owned, jnp.exp(page_max[None] - local_max[:, None]), 0.0)
    local_out = jnp.einsum("rpsh,pshd->rshd", factors, page_out, precision=HIGHEST)
    local_sum = jnp.einsum("rpsh,psh->rsh", factors, page_sum, precision=HIGHEST)
    stat_width = step_count * local_heads
    stat_row = jnp.concatenate(
        [
            local_max.reshape(all_requests, stat_width),
            local_sum.reshape(all_requests, stat_width),
            jnp.zeros((all_requests, HD - 2 * stat_width), jnp.float32),
        ],
        axis=1,
    )
    packed = jnp.concatenate(
        [local_out.reshape(all_requests, stat_width, HD), stat_row[:, None, :]], axis=1
    )
    gathered = lax.all_to_all(packed, "req", 0, 0, tiled=True).reshape(
        req_count, req_rows, stat_width + 1, HD
    )
    part_out = gathered[:, :, :stat_width, :]
    part_max = gathered[:, :, stat_width, :stat_width]
    part_sum = gathered[:, :, stat_width, stat_width : 2 * stat_width]
    cache_max = jnp.max(part_max, axis=0)
    rescale = jnp.exp(part_max - cache_max[None])
    cache_out = jnp.sum(part_out * rescale[..., None], axis=0).reshape(
        req_rows, step_count, local_heads, HD
    )
    cache_sum = jnp.sum(part_sum * rescale, axis=0).reshape(req_rows, step_count, local_heads)
    cache_max = cache_max.reshape(req_rows, step_count, local_heads)
    new_scores = (
        jnp.einsum("rshd,rthd->rsht", query_new, key_new, preferred_element_type=jnp.float32)
        * score_scale
    )
    causal = jnp.arange(step_count)[:, None] >= jnp.arange(step_count)[None, :]
    new_mask = causal[None, :, None, :]
    new_masked = jnp.where(new_mask, new_scores, NEG)
    new_max = jnp.max(new_masked, axis=-1)
    new_weights = jnp.where(new_mask, jnp.exp(new_masked - new_max[..., None]), 0.0)
    new_sum = jnp.sum(new_weights, axis=-1)
    new_out = jnp.einsum(
        "rsht,rthd->rshd",
        new_weights.astype(jnp.bfloat16),
        value_new,
        preferred_element_type=jnp.float32,
    )
    top_max = jnp.maximum(cache_max, new_max)
    cache_factor = jnp.exp(cache_max - top_max)
    new_factor = jnp.exp(new_max - top_max)
    attended = (cache_out * cache_factor[..., None] + new_out * new_factor[..., None]) / (
        cache_sum * cache_factor + new_sum * new_factor
    )[..., None]
    attended = attended.astype(jnp.bfloat16).reshape(row_count, head_width)
    attn_part = jnp.dot(attended, out_weight, preferred_element_type=jnp.float32)
    attn_full = sum(shift_exchange(attn_part, "tp", tp_count, spread=True))
    resid = tokens_in.reshape(row_count, model_width).astype(jnp.float32) + attn_full
    mixed = rms_norm(resid, mlp_norm)
    expert_count = req_count * expert_w_gate.shape[0]
    capacity = max(2, (row_count * TOPK + expert_count - 1) // expert_count)
    picks = routes.reshape(row_count * TOPK)
    gates_flat = route_gates.reshape(row_count * TOPK)
    expert_hot = (picks[:, None] == jnp.arange(expert_count, dtype=jnp.int32)[None, :]).astype(
        jnp.int32
    )
    slot_index = jnp.sum((jnp.cumsum(expert_hot, axis=0) - 1) * expert_hot, axis=1)
    destination = picks * capacity + slot_index
    dest_hot = (
        destination[:, None] == jnp.arange(expert_count * capacity, dtype=jnp.int32)[None, :]
    ).astype(jnp.float32)
    token_hot = (
        (jnp.arange(row_count * TOPK, dtype=jnp.int32) // TOPK)[:, None]
        == jnp.arange(row_count, dtype=jnp.int32)[None, :]
    ).astype(jnp.float32)
    placement = jnp.einsum("cx,ct->xt", dest_hot, token_hot, precision=HIGHEST).astype(jnp.bfloat16)
    outgoing = jnp.dot(placement, mixed, preferred_element_type=jnp.float32).astype(jnp.bfloat16)
    combine_map = jnp.einsum(
        "ct,cx->tx", token_hot, dest_hot * gates_flat[:, None], precision=HIGHEST
    )
    w_gate_here = expert_w_gate[0]
    w_up_here = expert_w_up[0]
    w_down_here = expert_w_down[0]
    mixed_cols = lax.dynamic_slice_in_dim(mixed, tp_index * col_share, col_share, 1)
    shared_send = jnp.broadcast_to(mixed_cols[None], (req_count, row_count, col_share))
    moe_lines = capacity * model_width // LANES
    dispatch = jnp.concatenate(
        [
            outgoing.reshape(req_count, moe_lines, LANES),
            shared_send.reshape(req_count, row_count * col_share // LANES, LANES),
        ],
        axis=1,
    )
    received = lax.all_to_all(dispatch, "req", 0, 0, tiled=True)
    flat_rows = received[:, :moe_lines].reshape(req_count * capacity, model_width)
    piece = received[:, moe_lines:].reshape(req_count * row_count, col_share)
    expert_rows = req_count * capacity
    gate_part = jnp.dot(piece, shared_w_gate, preferred_element_type=jnp.float32)
    up_part = jnp.dot(piece, shared_w_up, preferred_element_type=jnp.float32)
    unit_count = shared_w_gate.shape[1]
    all_rows = req_count * row_count
    share_rows = all_rows // tp_count
    shared_pre = jnp.concatenate([gate_part, up_part], axis=1).reshape(
        tp_count, share_rows * 2 * unit_count
    )
    flat_rows, shared_pre = lax.optimization_barrier((flat_rows, shared_pre))
    gate_pre = jnp.dot(flat_rows, w_gate_here, preferred_element_type=jnp.float32)
    up_pre = jnp.dot(flat_rows, w_up_here, preferred_element_type=jnp.float32)
    hidden = (jax.nn.silu(gate_pre) * up_pre).astype(jnp.bfloat16)
    shared_sum = sum(shift_exchange(shared_pre, "tp", tp_count)).reshape(
        share_rows, 2 * unit_count
    )
    partial_out = jnp.dot(hidden, w_down_here, preferred_element_type=jnp.float32)
    partial_out, shared_sum = lax.optimization_barrier((partial_out, shared_sum))
    partial_split = partial_out.reshape(expert_rows, tp_count, col_share).transpose(1, 0, 2)
    expert_sum = sum(
        shift_exchange(partial_split.reshape(tp_count, expert_rows * col_share), "tp", tp_count)
    ).reshape(expert_rows, col_share)
    shared_hidden = (jax.nn.silu(shared_sum[:, :unit_count]) * shared_sum[:, unit_count:]).astype(
        jnp.bfloat16
    )
    hidden_all = by_source(
        shift_exchange(shared_hidden, "tp", tp_count, spread=True), "tp", tp_count
    ).reshape(all_rows, unit_count)
    shared_down = jnp.dot(hidden_all, shared_w_down, preferred_element_type=jnp.float32)
    ey = expert_sum.astype(jnp.bfloat16).astype(jnp.float32)
    ey_lines = capacity * col_share // LANES
    back_in = jnp.concatenate(
        [
            ey.reshape(req_count, ey_lines, LANES),
            shared_down.reshape(req_count, row_count * col_share // LANES, LANES),
        ],
        axis=1,
    )
    back = lax.all_to_all(back_in, "req", 0, 0, tiled=True)
    returned = back[:, :ey_lines].reshape(expert_count * capacity, col_share)
    shared_mine = jnp.sum(back[:, ey_lines:].reshape(req_count, row_count, col_share), axis=0)
    moe_out = jnp.dot(combine_map, returned, precision=HIGHEST)
    switch = jax.nn.sigmoid(jnp.dot(mixed, shared_switch, preferred_element_type=jnp.float32))
    resid_mine = lax.dynamic_slice_in_dim(resid, tp_index * col_share, col_share, 1)
    final = resid_mine + moe_out + switch[:, None] * shared_mine
    return final.astype(jnp.bfloat16).reshape(req_rows, step_count, col_share)


def solution(mesh):
    return jax.shard_map(
        per_device,
        mesh=mesh,
        in_specs=(
            P("req", None, None),
            P(),
            P(None, None, "tp"),
            P(None, "tp"),
            P("tp", None),
            P("req", None, "tp"),
            P("req", None, "tp"),
            P(),
            P(),
            P(),
            P("req", None, None),
            P("req", None, None),
            P("req", None, "tp"),
            P("req", None, "tp"),
            P("req", "tp", None),
            P("tp", "req"),
            P("tp", "req"),
            P("req", "tp"),
            P(),
        ),
        out_specs=P("req", None, "tp"),
        check_vma=False,
    )
```

```python
import math

import jax
import jax.numpy as jnp
from jax import lax
from jax.sharding import PartitionSpec as P

HD = 128
TOPK = 4
LANES = 128


NEG = -1e30
EPS = 1e-06
THETA = 1000000.0
HIGHEST = lax.Precision.HIGHEST


def rms_norm(inputs, gain_vector):
    values = inputs.astype(jnp.float32)
    scaled = values * lax.rsqrt(jnp.mean(values * values, axis=-1, keepdims=True) + EPS)
    return (scaled * gain_vector.astype(jnp.float32)).astype(jnp.bfloat16)


def rotate(values, positions):
    half_dim = values.shape[-1] // 2
    exponents = jnp.arange(half_dim, dtype=jnp.float32) * (2.0 / values.shape[-1])
    frequency = jnp.power(THETA, -exponents)
    angles = positions.astype(jnp.float32)[..., None, None] * frequency
    cosines = jnp.cos(angles)
    sine_part = jnp.sin(angles)
    front_half = values[..., :half_dim]
    back_half = values[..., half_dim:]
    return jnp.concatenate(
        [
            front_half * cosines - back_half * sine_part,
            back_half * cosines + front_half * sine_part,
        ],
        axis=-1,
    )


def shift_exchange(chunks, axis, count, spread=False):
    me = lax.axis_index(axis)
    pieces = [chunks if spread else lax.dynamic_index_in_dim(chunks, me, 0, keepdims=False)]
    for shift in range(1, count):
        send = chunks if spread else lax.dynamic_index_in_dim(
            chunks, (me + shift) % count, 0, keepdims=False
        )
        pairs = [(source, (source + shift) % count) for source in range(count)]
        pieces.append(lax.ppermute(send, axis, pairs))
    return pieces


def by_source(pieces, axis, count):
    me = lax.axis_index(axis)
    blocks = []
    for source in range(count):
        shift = (me - source) % count
        block = pieces[count - 1]
        for candidate in range(count - 2, -1, -1):
            block = jnp.where(shift == candidate, pieces[candidate], block)
        blocks.append(block)
    return jnp.stack(blocks)


def bcast_a2a(values, axis, count):
    spread = jnp.broadcast_to(values[None], (count,) + values.shape)
    return lax.all_to_all(spread, axis, 0, 0, tiled=True).reshape(
        (count * values.shape[0],) + values.shape[1:]
    )


def per_device(
    tokens_in,
    attn_norm,
    qkv_weight,
    qkv_bias,
    out_weight,
    cache_keys,
    cache_values,
    page_table,
    cache_lengths,
    mlp_norm,
    routes,
    route_gates,
    expert_w_gate,
    expert_w_up,
    expert_w_down,
    shared_w_gate,
    shared_w_up,
    shared_w_down,
    shared_switch,
):
    req_rows, step_count, model_width = tokens_in.shape
    head_width = qkv_weight.shape[2]
    local_heads = head_width // HD
    req_count = lax.axis_size("req")
    tp_count = lax.axis_size("tp")
    req_index = lax.axis_index("req")
    tp_index = lax.axis_index("tp")
    all_requests = page_table.shape[0]
    pool_here = cache_keys.shape[0]
    page_len = cache_keys.shape[1]
    score_scale = 1.0 / math.sqrt(HD)
    col_share = model_width // tp_count
    row_count = req_rows * step_count
    normed = rms_norm(tokens_in, attn_norm)
    own_lengths = lax.dynamic_slice_in_dim(cache_lengths, req_index * req_rows, req_rows)
    positions = own_lengths[:, None] + jnp.arange(step_count, dtype=jnp.int32)[None, :]
    head_shape = (req_rows, step_count, local_heads, HD)

    def project(part, rows):
        return jnp.einsum(
            "rsd,df->rsf", rows, qkv_weight[:, part], preferred_element_type=jnp.float32
        ) + qkv_bias[part].astype(jnp.float32)

    query_new = rotate(project(0, normed).reshape(head_shape), positions).astype(jnp.bfloat16)
    query_spread = jnp.broadcast_to(query_new[None], (req_count,) + query_new.shape)
    normed_late, query_spread = lax.optimization_barrier((normed, query_spread))
    query_all = lax.all_to_all(query_spread, "req", 0, 0, tiled=True).reshape(
        (req_count * req_rows,) + query_new.shape[1:]
    )
    key_value = jnp.einsum(
        "rsd,dcf->rscf", normed_late, qkv_weight[:, 1:], preferred_element_type=jnp.float32
    ) + qkv_bias[1:].astype(jnp.float32)
    key_new = rotate(key_value[:, :, 0].reshape(head_shape), positions).astype(jnp.bfloat16)
    value_new = key_value[:, :, 1].reshape(head_shape).astype(jnp.bfloat16)
    slot_ids = req_index * pool_here + jnp.arange(pool_here, dtype=jnp.int32)
    matches = (page_table[:, :, None] == slot_ids[None, None, :]).astype(jnp.int32)
    request_ids = jnp.arange(all_requests, dtype=jnp.int32)
    page_ids = jnp.arange(page_table.shape[1], dtype=jnp.int32)
    owner = jnp.sum(matches * request_ids[:, None, None], axis=(0, 1))
    logical = jnp.sum(matches * page_ids[None, :, None], axis=(0, 1))
    present = jnp.sum(matches, axis=(0, 1)) > 0
    token_pos = logical[:, None] * page_len + jnp.arange(page_len, dtype=jnp.int32)[None, :]
    live = present[:, None] & (token_pos < cache_lengths[owner][:, None])
    page_queries = query_all[owner]
    page_values = cache_values.reshape(pool_here, page_len, local_heads, HD)
    head_eye = jnp.arange(local_heads)[:, None] == jnp.arange(local_heads)[None, :]
    block_queries = jnp.where(
        head_eye[None, None, :, :, None], page_queries[:, :, :, None, :], jnp.zeros((), jnp.bfloat16)
    ).reshape(pool_here, step_count * local_heads, head_width)
    scores = (
        jnp.einsum("pxd,pkd->pxk", block_queries, cache_keys, preferred_element_type=jnp.float32)
        * score_scale
    ).reshape(pool_here, step_count, local_heads, page_len)
    page_mask = live[:, None, None, :]
    masked = jnp.where(page_mask, scores, NEG)
    page_max = jnp.max(masked, axis=-1)
    weights = jnp.where(page_mask, jnp.exp(masked - page_max[..., None]), 0.0)
    page_sum = jnp.sum(weights, axis=-1)
    page_out = jnp.einsum(
        "pshk,pkhd->pshd",
        weights.astype(jnp.bfloat16),
        page_values,
        preferred_element_type=jnp.float32,
    )
    belongs = (owner[None, :] == request_ids[:, None]) & present[None, :]
    owned = belongs[:, :, None, None]
    local_max = jnp.max(jnp.where(owned, page_max[None], NEG), axis=1)
    factors = jnp.where(owned, jnp.exp(page_max[None] - local_max[:, None]), 0.0)
    local_out = jnp.einsum("rpsh,pshd->rshd", factors, page_out, precision=HIGHEST)
    local_sum = jnp.einsum("rpsh,psh->rsh", factors, page_sum, precision=HIGHEST)
    stat_width = step_count * local_heads
    stat_row = jnp.concatenate(
        [
            local_max.reshape(all_requests, stat_width),
            local_sum.reshape(all_requests, stat_width),
            jnp.zeros((all_requests, HD - 2 * stat_width), jnp.float32),
        ],
        axis=1,
    )
    packed = jnp.concatenate(
        [local_out.reshape(all_requests, stat_width, HD), stat_row[:, None, :]], axis=1
    )
    gathered = lax.all_to_all(packed, "req", 0, 0, tiled=True).reshape(
        req_count, req_rows, stat_width + 1, HD
    )
    part_out = gathered[:, :, :stat_width, :]
    part_max = gathered[:, :, stat_width, :stat_width]
    part_sum = gathered[:, :, stat_width, stat_width : 2 * stat_width]
    cache_max = jnp.max(part_max, axis=0)
    rescale = jnp.exp(part_max - cache_max[None])
    cache_out = jnp.sum(part_out * rescale[..., None], axis=0).reshape(
        req_rows, step_count, local_heads, HD
    )
    cache_sum = jnp.sum(part_sum * rescale, axis=0).reshape(req_rows, step_count, local_heads)
    cache_max = cache_max.reshape(req_rows, step_count, local_heads)
    new_scores = (
        jnp.einsum("rshd,rthd->rsht", query_new, key_new, preferred_element_type=jnp.float32)
        * score_scale
    )
    causal = jnp.arange(step_count)[:, None] >= jnp.arange(step_count)[None, :]
    new_mask = causal[None, :, None, :]
    new_masked = jnp.where(new_mask, new_scores, NEG)
    new_max = jnp.max(new_masked, axis=-1)
    new_weights = jnp.where(new_mask, jnp.exp(new_masked - new_max[..., None]), 0.0)
    new_sum = jnp.sum(new_weights, axis=-1)
    new_out = jnp.einsum(
        "rsht,rthd->rshd",
        new_weights.astype(jnp.bfloat16),
        value_new,
        preferred_element_type=jnp.float32,
    )
    top_max = jnp.maximum(cache_max, new_max)
    cache_factor = jnp.exp(cache_max - top_max)
    new_factor = jnp.exp(new_max - top_max)
    attended = (cache_out * cache_factor[..., None] + new_out * new_factor[..., None]) / (
        cache_sum * cache_factor + new_sum * new_factor
    )[..., None]
    attended = attended.astype(jnp.bfloat16).reshape(row_count, head_width)
    attn_part = jnp.dot(attended, out_weight, preferred_element_type=jnp.float32)
    attn_full = sum(shift_exchange(attn_part, "tp", tp_count, spread=True))
    resid = tokens_in.reshape(row_count, model_width).astype(jnp.float32) + attn_full
    mixed = rms_norm(resid, mlp_norm)
    expert_count = req_count * expert_w_gate.shape[0]
    capacity = max(2, (row_count * TOPK + expert_count - 1) // expert_count)
    picks = routes.reshape(row_count * TOPK)
    gates_flat = route_gates.reshape(row_count * TOPK)
    expert_hot = (picks[:, None] == jnp.arange(expert_count, dtype=jnp.int32)[None, :]).astype(
        jnp.int32
    )
    slot_index = jnp.sum((jnp.cumsum(expert_hot, axis=0) - 1) * expert_hot, axis=1)
    destination = picks * capacity + slot_index
    dest_hot = (
        destination[:, None] == jnp.arange(expert_count * capacity, dtype=jnp.int32)[None, :]
    ).astype(jnp.float32)
    token_hot = (
        (jnp.arange(row_count * TOPK, dtype=jnp.int32) // TOPK)[:, None]
        == jnp.arange(row_count, dtype=jnp.int32)[None, :]
    ).astype(jnp.float32)
    placement = jnp.einsum("cx,ct->xt", dest_hot, token_hot, precision=HIGHEST).astype(jnp.bfloat16)
    outgoing = jnp.dot(placement, mixed, preferred_element_type=jnp.float32).astype(jnp.bfloat16)
    combine_map = jnp.einsum(
        "ct,cx->tx", token_hot, dest_hot * gates_flat[:, None], precision=HIGHEST
    )
    w_gate_here = expert_w_gate[0]
    w_up_here = expert_w_up[0]
    w_down_here = expert_w_down[0]
    mixed_cols = lax.dynamic_slice_in_dim(mixed, tp_index * col_share, col_share, 1)
    shared_send = jnp.broadcast_to(mixed_cols[None], (req_count, row_count, col_share))
    moe_lines = capacity * model_width // LANES
    dispatch = jnp.concatenate(
        [
            outgoing.reshape(req_count, moe_lines, LANES),
            shared_send.reshape(req_count, row_count * col_share // LANES, LANES),
        ],
        axis=1,
    )
    received = lax.all_to_all(dispatch, "req", 0, 0, tiled=True)
    flat_rows = received[:, :moe_lines].reshape(req_count * capacity, model_width)
    piece = received[:, moe_lines:].reshape(req_count * row_count, col_share)
    expert_rows = req_count * capacity
    gate_part = jnp.dot(piece, shared_w_gate, preferred_element_type=jnp.float32)
    up_part = jnp.dot(piece, shared_w_up, preferred_element_type=jnp.float32)
    unit_count = shared_w_gate.shape[1]
    all_rows = req_count * row_count
    share_rows = all_rows // tp_count
    shared_pre = jnp.concatenate([gate_part, up_part], axis=1).reshape(
        tp_count, share_rows * 2 * unit_count
    )
    flat_rows, shared_pre = lax.optimization_barrier((flat_rows, shared_pre))
    gate_pre = jnp.dot(flat_rows, w_gate_here, preferred_element_type=jnp.float32)
    up_pre = jnp.dot(flat_rows, w_up_here, preferred_element_type=jnp.float32)
    hidden = (jax.nn.silu(gate_pre) * up_pre).astype(jnp.bfloat16)
    shared_sum = sum(shift_exchange(shared_pre, "tp", tp_count)).reshape(
        share_rows, 2 * unit_count
    )
    partial_out = jnp.dot(hidden, w_down_here, preferred_element_type=jnp.float32)
    partial_out, shared_sum = lax.optimization_barrier((partial_out, shared_sum))
    partial_split = partial_out.reshape(expert_rows, tp_count, col_share).transpose(1, 0, 2)
    expert_sum = sum(
        shift_exchange(partial_split.reshape(tp_count, expert_rows * col_share), "tp", tp_count)
    ).reshape(expert_rows, col_share)
    shared_hidden = (jax.nn.silu(shared_sum[:, :unit_count]) * shared_sum[:, unit_count:]).astype(
        jnp.bfloat16
    )
    hidden_all = by_source(
        shift_exchange(shared_hidden, "tp", tp_count, spread=True), "tp", tp_count
    ).reshape(all_rows, unit_count)
    shared_down = jnp.dot(hidden_all, shared_w_down, preferred_element_type=jnp.float32)
    ey = expert_sum.astype(jnp.bfloat16).astype(jnp.float32)
    ey_lines = capacity * col_share // LANES
    back_in = jnp.concatenate(
        [
            ey.reshape(req_count, ey_lines, LANES),
            shared_down.reshape(req_count, row_count * col_share // LANES, LANES),
        ],
        axis=1,
    )
    back = lax.all_to_all(back_in, "req", 0, 0, tiled=True)
    returned = back[:, :ey_lines].reshape(expert_count * capacity, col_share)
    shared_mine = jnp.sum(back[:, ey_lines:].reshape(req_count, row_count, col_share), axis=0)
    moe_out = jnp.dot(combine_map, returned, precision=HIGHEST)
    switch = jax.nn.sigmoid(jnp.dot(mixed, shared_switch, preferred_element_type=jnp.float32))
    resid_mine = lax.dynamic_slice_in_dim(resid, tp_index * col_share, col_share, 1)
    final = resid_mine + moe_out + switch[:, None] * shared_mine
    return final.astype(jnp.bfloat16).reshape(req_rows, step_count, col_share)


def solution(mesh):
    return jax.shard_map(
        per_device,
        mesh=mesh,
        in_specs=(
            P("req", None, None),
            P(),
            P(None, None, "tp"),
            P(None, "tp"),
            P("tp", None),
            P("req", None, "tp"),
            P("req", None, "tp"),
            P(),
            P(),
            P(),
            P("req", None, None),
            P("req", None, None),
            P("req", None, "tp"),
            P("req", None, "tp"),
            P("req", "tp", None),
            P("tp", "req"),
            P("tp", "req"),
            P("req", "tp"),
            P(),
        ),
        out_specs=P("req", None, "tp"),
        check_vma=False,
    )
```

```python
import math

import jax
import jax.numpy as jnp
from jax import lax
from jax.sharding import PartitionSpec as P

HD = 128
TOPK = 4
LANES = 128


NEG = -1e30
EPS = 1e-06
THETA = 1000000.0
HIGHEST = lax.Precision.HIGHEST


def rms_norm(inputs, gain_vector):
    values = inputs.astype(jnp.float32)
    scaled = values * lax.rsqrt(jnp.mean(values * values, axis=-1, keepdims=True) + EPS)
    return (scaled * gain_vector.astype(jnp.float32)).astype(jnp.bfloat16)


def rotate(values, positions):
    half_dim = values.shape[-1] // 2
    exponents = jnp.arange(half_dim, dtype=jnp.float32) * (2.0 / values.shape[-1])
    frequency = jnp.power(THETA, -exponents)
    angles = positions.astype(jnp.float32)[..., None, None] * frequency
    cosines = jnp.cos(angles)
    sine_part = jnp.sin(angles)
    front_half = values[..., :half_dim]
    back_half = values[..., half_dim:]
    return jnp.concatenate(
        [
            front_half * cosines - back_half * sine_part,
            back_half * cosines + front_half * sine_part,
        ],
        axis=-1,
    )


def shift_exchange(chunks, axis, count, spread=False):
    me = lax.axis_index(axis)
    pieces = [chunks if spread else lax.dynamic_index_in_dim(chunks, me, 0, keepdims=False)]
    for shift in range(1, count):
        send = chunks if spread else lax.dynamic_index_in_dim(
            chunks, (me + shift) % count, 0, keepdims=False
        )
        pairs = [(source, (source + shift) % count) for source in range(count)]
        pieces.append(lax.ppermute(send, axis, pairs))
    return pieces


def by_source(pieces, axis, count):
    me = lax.axis_index(axis)
    stacked = jnp.stack(pieces)
    order = (me - jnp.arange(count, dtype=jnp.int32)) % count
    return jnp.take(stacked, order, axis=0)


def bcast_a2a(values, axis, count):
    spread = jnp.broadcast_to(values[None], (count,) + values.shape)
    return lax.all_to_all(spread, axis, 0, 0, tiled=True).reshape(
        (count * values.shape[0],) + values.shape[1:]
    )


def per_device(
    tokens_in,
    attn_norm,
    qkv_weight,
    qkv_bias,
    out_weight,
    cache_keys,
    cache_values,
    page_table,
    cache_lengths,
    mlp_norm,
    routes,
    route_gates,
    expert_w_gate,
    expert_w_up,
    expert_w_down,
    shared_w_gate,
    shared_w_up,
    shared_w_down,
    shared_switch,
):
    req_rows, step_count, model_width = tokens_in.shape
    head_width = qkv_weight.shape[2]
    local_heads = head_width // HD
    req_count = lax.axis_size("req")
    tp_count = lax.axis_size("tp")
    req_index = lax.axis_index("req")
    tp_index = lax.axis_index("tp")
    all_requests = page_table.shape[0]
    pool_here = cache_keys.shape[0]
    page_len = cache_keys.shape[1]
    score_scale = 1.0 / math.sqrt(HD)
    col_share = model_width // tp_count
    row_count = req_rows * step_count
    normed = rms_norm(tokens_in, attn_norm)
    own_lengths = lax.dynamic_slice_in_dim(cache_lengths, req_index * req_rows, req_rows)
    positions = own_lengths[:, None] + jnp.arange(step_count, dtype=jnp.int32)[None, :]
    head_shape = (req_rows, step_count, local_heads, HD)

    def project(part, rows):
        return jnp.einsum(
            "rsd,df->rsf", rows, qkv_weight[:, part], preferred_element_type=jnp.float32
        ) + qkv_bias[part].astype(jnp.float32)

    query_new = rotate(project(0, normed).reshape(head_shape), positions).astype(jnp.bfloat16)
    normed_late, query_new = lax.optimization_barrier((normed, query_new))
    query_all = by_source(
        shift_exchange(query_new, "req", req_count, spread=True), "req", req_count
    ).reshape((req_count * req_rows,) + query_new.shape[1:])
    key_value = jnp.einsum(
        "rsd,dcf->rscf", normed_late, qkv_weight[:, 1:], preferred_element_type=jnp.float32
    ) + qkv_bias[1:].astype(jnp.float32)
    key_new = rotate(key_value[:, :, 0].reshape(head_shape), positions).astype(jnp.bfloat16)
    value_new = key_value[:, :, 1].reshape(head_shape).astype(jnp.bfloat16)
    slot_ids = req_index * pool_here + jnp.arange(pool_here, dtype=jnp.int32)
    matches = (page_table[:, :, None] == slot_ids[None, None, :]).astype(jnp.int32)
    request_ids = jnp.arange(all_requests, dtype=jnp.int32)
    page_ids = jnp.arange(page_table.shape[1], dtype=jnp.int32)
    owner = jnp.sum(matches * request_ids[:, None, None], axis=(0, 1))
    logical = jnp.sum(matches * page_ids[None, :, None], axis=(0, 1))
    present = jnp.sum(matches, axis=(0, 1)) > 0
    token_pos = logical[:, None] * page_len + jnp.arange(page_len, dtype=jnp.int32)[None, :]
    live = present[:, None] & (token_pos < cache_lengths[owner][:, None])
    page_queries = query_all[owner]
    page_values = cache_values.reshape(pool_here, page_len, local_heads, HD)
    head_eye = jnp.arange(local_heads)[:, None] == jnp.arange(local_heads)[None, :]
    block_queries = jnp.where(
        head_eye[None, None, :, :, None], page_queries[:, :, :, None, :], jnp.zeros((), jnp.bfloat16)
    ).reshape(pool_here, step_count * local_heads, head_width)
    scores = (
        jnp.einsum("pxd,pkd->pxk", block_queries, cache_keys, preferred_element_type=jnp.float32)
        * score_scale
    ).reshape(pool_here, step_count, local_heads, page_len)
    page_mask = live[:, None, None, :]
    masked = jnp.where(page_mask, scores, NEG)
    page_max = jnp.max(masked, axis=-1)
    weights = jnp.where(page_mask, jnp.exp(masked - page_max[..., None]), 0.0)
    page_sum = jnp.sum(weights, axis=-1)
    page_out = jnp.einsum(
        "pshk,pkhd->pshd",
        weights.astype(jnp.bfloat16),
        page_values,
        preferred_element_type=jnp.float32,
    )
    belongs = (owner[None, :] == request_ids[:, None]) & present[None, :]
    owned = belongs[:, :, None, None]
    local_max = jnp.max(jnp.where(owned, page_max[None], NEG), axis=1)
    factors = jnp.where(owned, jnp.exp(page_max[None] - local_max[:, None]), 0.0)
    local_out = jnp.einsum("rpsh,pshd->rshd", factors, page_out, precision=HIGHEST)
    local_sum = jnp.einsum("rpsh,psh->rsh", factors, page_sum, precision=HIGHEST)
    stat_width = step_count * local_heads
    stat_row = jnp.concatenate(
        [
            local_max.reshape(all_requests, stat_width),
            local_sum.reshape(all_requests, stat_width),
            jnp.zeros((all_requests, HD - 2 * stat_width), jnp.float32),
        ],
        axis=1,
    )
    packed = jnp.concatenate(
        [local_out.reshape(all_requests, stat_width, HD), stat_row[:, None, :]], axis=1
    )
    gathered = lax.all_to_all(packed, "req", 0, 0, tiled=True).reshape(
        req_count, req_rows, stat_width + 1, HD
    )
    part_out = gathered[:, :, :stat_width, :]
    part_max = gathered[:, :, stat_width, :stat_width]
    part_sum = gathered[:, :, stat_width, stat_width : 2 * stat_width]
    cache_max = jnp.max(part_max, axis=0)
    rescale = jnp.exp(part_max - cache_max[None])
    cache_out = jnp.sum(part_out * rescale[..., None], axis=0).reshape(
        req_rows, step_count, local_heads, HD
    )
    cache_sum = jnp.sum(part_sum * rescale, axis=0).reshape(req_rows, step_count, local_heads)
    cache_max = cache_max.reshape(req_rows, step_count, local_heads)
    new_scores = (
        jnp.einsum("rshd,rthd->rsht", query_new, key_new, preferred_element_type=jnp.float32)
        * score_scale
    )
    causal = jnp.arange(step_count)[:, None] >= jnp.arange(step_count)[None, :]
    new_mask = causal[None, :, None, :]
    new_masked = jnp.where(new_mask, new_scores, NEG)
    new_max = jnp.max(new_masked, axis=-1)
    new_weights = jnp.where(new_mask, jnp.exp(new_masked - new_max[..., None]), 0.0)
    new_sum = jnp.sum(new_weights, axis=-1)
    new_out = jnp.einsum(
        "rsht,rthd->rshd",
        new_weights.astype(jnp.bfloat16),
        value_new,
        preferred_element_type=jnp.float32,
    )
    top_max = jnp.maximum(cache_max, new_max)
    cache_factor = jnp.exp(cache_max - top_max)
    new_factor = jnp.exp(new_max - top_max)
    attended = (cache_out * cache_factor[..., None] + new_out * new_factor[..., None]) / (
        cache_sum * cache_factor + new_sum * new_factor
    )[..., None]
    attended = attended.astype(jnp.bfloat16).reshape(row_count, head_width)
    attn_part = jnp.dot(attended, out_weight, preferred_element_type=jnp.float32)
    attn_full = sum(shift_exchange(attn_part, "tp", tp_count, spread=True))
    resid = tokens_in.reshape(row_count, model_width).astype(jnp.float32) + attn_full
    mixed = rms_norm(resid, mlp_norm)
    expert_count = req_count * expert_w_gate.shape[0]
    capacity = max(2, (row_count * TOPK + expert_count - 1) // expert_count)
    picks = routes.reshape(row_count * TOPK)
    gates_flat = route_gates.reshape(row_count * TOPK)
    expert_hot = (picks[:, None] == jnp.arange(expert_count, dtype=jnp.int32)[None, :]).astype(
        jnp.int32
    )
    slot_index = jnp.sum((jnp.cumsum(expert_hot, axis=0) - 1) * expert_hot, axis=1)
    destination = picks * capacity + slot_index
    dest_hot = (
        destination[:, None] == jnp.arange(expert_count * capacity, dtype=jnp.int32)[None, :]
    ).astype(jnp.float32)
    token_hot = (
        (jnp.arange(row_count * TOPK, dtype=jnp.int32) // TOPK)[:, None]
        == jnp.arange(row_count, dtype=jnp.int32)[None, :]
    ).astype(jnp.float32)
    placement = jnp.einsum("cx,ct->xt", dest_hot, token_hot, precision=HIGHEST).astype(jnp.bfloat16)
    outgoing = jnp.dot(placement, mixed, preferred_element_type=jnp.float32).astype(jnp.bfloat16)
    combine_map = jnp.einsum(
        "ct,cx->tx", token_hot, dest_hot * gates_flat[:, None], precision=HIGHEST
    )
    w_gate_here = expert_w_gate[0]
    w_up_here = expert_w_up[0]
    w_down_here = expert_w_down[0]
    mixed_cols = lax.dynamic_slice_in_dim(mixed, tp_index * col_share, col_share, 1)
    shared_send = jnp.broadcast_to(mixed_cols[None], (req_count, row_count, col_share))
    moe_lines = capacity * model_width // LANES
    dispatch = jnp.concatenate(
        [
            outgoing.reshape(req_count, moe_lines, LANES),
            shared_send.reshape(req_count, row_count * col_share // LANES, LANES),
        ],
        axis=1,
    )
    received = lax.all_to_all(dispatch, "req", 0, 0, tiled=True)
    flat_rows = received[:, :moe_lines].reshape(req_count * capacity, model_width)
    piece = received[:, moe_lines:].reshape(req_count * row_count, col_share)
    expert_rows = req_count * capacity
    gate_part = jnp.dot(piece, shared_w_gate, preferred_element_type=jnp.float32)
    up_part = jnp.dot(piece, shared_w_up, preferred_element_type=jnp.float32)
    unit_count = shared_w_gate.shape[1]
    all_rows = req_count * row_count
    share_rows = all_rows // tp_count
    shared_pre = jnp.concatenate([gate_part, up_part], axis=1).reshape(
        tp_count, share_rows * 2 * unit_count
    )
    flat_rows, shared_pre = lax.optimization_barrier((flat_rows, shared_pre))
    gate_pre = jnp.dot(flat_rows, w_gate_here, preferred_element_type=jnp.float32)
    up_pre = jnp.dot(flat_rows, w_up_here, preferred_element_type=jnp.float32)
    hidden = (jax.nn.silu(gate_pre) * up_pre).astype(jnp.bfloat16)
    shared_sum = sum(shift_exchange(shared_pre, "tp", tp_count)).reshape(
        share_rows, 2 * unit_count
    )
    partial_out = jnp.dot(hidden, w_down_here, preferred_element_type=jnp.float32)
    partial_out, shared_sum = lax.optimization_barrier((partial_out, shared_sum))
    partial_split = partial_out.reshape(expert_rows, tp_count, col_share).transpose(1, 0, 2)
    expert_sum = sum(
        shift_exchange(partial_split.reshape(tp_count, expert_rows * col_share), "tp", tp_count)
    ).reshape(expert_rows, col_share)
    shared_hidden = (jax.nn.silu(shared_sum[:, :unit_count]) * shared_sum[:, unit_count:]).astype(
        jnp.bfloat16
    )
    hidden_all = by_source(
        shift_exchange(shared_hidden, "tp", tp_count, spread=True), "tp", tp_count
    ).reshape(all_rows, unit_count)
    shared_down = jnp.dot(hidden_all, shared_w_down, preferred_element_type=jnp.float32)
    ey = expert_sum.astype(jnp.bfloat16).astype(jnp.float32)
    ey_lines = capacity * col_share // LANES
    back_in = jnp.concatenate(
        [
            ey.reshape(req_count, ey_lines, LANES),
            shared_down.reshape(req_count, row_count * col_share // LANES, LANES),
        ],
        axis=1,
    )
    back = lax.all_to_all(back_in, "req", 0, 0, tiled=True)
    returned = back[:, :ey_lines].reshape(expert_count * capacity, col_share)
    shared_mine = jnp.sum(back[:, ey_lines:].reshape(req_count, row_count, col_share), axis=0)
    moe_out = jnp.dot(combine_map, returned, precision=HIGHEST)
    switch = jax.nn.sigmoid(jnp.dot(mixed, shared_switch, preferred_element_type=jnp.float32))
    resid_mine = lax.dynamic_slice_in_dim(resid, tp_index * col_share, col_share, 1)
    final = resid_mine + moe_out + switch[:, None] * shared_mine
    return final.astype(jnp.bfloat16).reshape(req_rows, step_count, col_share)


def solution(mesh):
    return jax.shard_map(
        per_device,
        mesh=mesh,
        in_specs=(
            P("req", None, None),
            P(),
            P(None, None, "tp"),
            P(None, "tp"),
            P("tp", None),
            P("req", None, "tp"),
            P("req", None, "tp"),
            P(),
            P(),
            P(),
            P("req", None, None),
            P("req", None, None),
            P("req", None, "tp"),
            P("req", None, "tp"),
            P("req", "tp", None),
            P("tp", "req"),
            P("tp", "req"),
            P("req", "tp"),
            P(),
        ),
        out_specs=P("req", None, "tp"),
        check_vma=False,
    )
```
